32 devices in a mesh: space: 8 (over z, y), chan: 4 (over x, core).
Axes of the slice: x: 2, y: 2, z: 4, core: 2. Of those that a mesh axis runs over, the one named last changes fastest.
Arguments:
- positions: float32 [3, 2048], P(None, 'space'), may hold values from 0 to 2
- features: bfloat16 [128, 2048], P('chan', 'space'), may hold values from -6 to 6
- send_rows: int32 [24, 128], P('space'), may hold values from 0 to 255, as said below
- pair_tiles: int32 [64, 2], P('space'), may hold values from 0 to 4, as said below
- tile_live: int32 [64], P('space'), may hold values from 0 to 1, as said below
- radial_weight: float32 [128, 8], P('chan'), may hold values from -1 to 1
- mix_weight: bfloat16 [3, 128, 128], replicated, may hold values from -0.5 to 0.5
- out_grad: bfloat16 [128, 9, 2048], P('chan', None, 'space'), may hold values from -6 to 6
Outputs:
- output: bfloat16 [128, 9, 2048], P('chan', None, 'space')
- grad_features: bfloat16 [128, 2048], P('chan', 'space')
- forces: float32 [3, 2048], P(None, 'space')
- grad_radial: float32 [128, 8], P('chan')
The draws below stay inside these ranges and needn't reach their ends.
Inputs may be any that keep to these rules, and one draw needn't show every extreme that they name: `send_rows`: row s * 3 + b lists 128 distinct atoms of domain s, numbered within the domain, that domain s sends to domain s xor 2^b. `pair_tiles`: row s * 8 + t holds domain s's tile t: a target block below 2 among its own blocks, then a source block below 5 among its source blocks. `tile_live`: on each domain the live tiles come first; each domain has 2 or more live tiles, and some domain has all 8.
All inputs are finite; a program needn't handle non-finite values.
Results may differ from the reference program's by a relative error of at most 0.025.
Values may be sent and summed in bfloat16 or wider, within the bound.
No kernel may reach another device: no remote copies, remote signals or barrier semaphores. Data moves between devices by JAX's collectives and lax.ppermute only.
A program may use at most 64 MiB of HBM per device.

```python
import math
import jax
import jax.numpy as jnp
from jax import lax

CH = 128
RADIAL = 8
COMPONENTS = 9
BLOCK = 128
BLK_DEV = 2
TILES_DEV = 8
LEVELS = 3
SRC_BLK = 5
A_DEV = 256
NATOMS = 2048
N_SPACE = 8


def draw_send_rows(key, part):
    keys = jax.random.split(jax.random.fold_in(key, 11), N_SPACE * LEVELS)
    chosen = jax.vmap(lambda single: jax.random.permutation(single, A_DEV)[:BLOCK])(keys)
    return chosen.astype(jnp.int32)


def draw_pair_tiles(key, part):
    target = jax.random.randint(jax.random.fold_in(key, 21), (N_SPACE * TILES_DEV, 1), 0, BLK_DEV)
    source = jax.random.randint(jax.random.fold_in(key, 22), (N_SPACE * TILES_DEV, 1), 0, SRC_BLK)
    return jnp.concatenate([target, source], axis=1).astype(jnp.int32)


def draw_tile_live(key, part):
    shrink = jax.random.randint(jax.random.fold_in(key, 31), (N_SPACE,), 0, 3)
    counts = jnp.maximum(TILES_DEV // 4, jnp.right_shift(jnp.full((N_SPACE,), TILES_DEV, jnp.int32), shrink))
    busiest = jax.random.randint(jax.random.fold_in(key, 32), (), 0, N_SPACE)
    counts = jnp.where(jnp.arange(N_SPACE) == busiest, TILES_DEV, counts)
    live = (jnp.arange(TILES_DEV)[None, :] < counts[:, None]).astype(jnp.int32)
    return live.reshape(N_SPACE * TILES_DEV)


def block_levels(own_key, shape, shards, low, top_value):
    loudness = 1.0
    for position, parts in shards:
        steps = jax.random.uniform(jax.random.fold_in(jax.random.fold_in(own_key, 6), position), (parts,), jnp.float32, low / len(shards), top_value / len(shards))
        loudness = loudness * jnp.repeat(jnp.exp(steps), shape[position] // parts).reshape((-1,) + (1,) * (len(shape) - 1 - position))
    return loudness


def normal_values(stream_key, dims, deviation, reach, cuts=(), kind=jnp.bfloat16):
    values = deviation * jax.random.normal(stream_key, dims, jnp.float32)
    if cuts:
        values = values * block_levels(stream_key, dims, cuts, -0.22, 0.18)
    return jnp.clip(values, -reach, reach).astype(kind)


def setup_inputs(seed: int = 0) -> dict:
    key_list = jax.random.split(jax.random.key(seed), 9)
    return {
        "positions": jnp.clip(2.0 * jax.random.uniform(key_list[0], (3, NATOMS), jnp.float32) ** block_levels(key_list[0], (3, NATOMS), ((1, 8),), -0.2, 0.2), 0.0, 2.0),
        "features": normal_values(key_list[1], (CH, NATOMS), 1.0, 6.0, ((0, 4), (1, 8))),
        "send_rows": draw_send_rows(jax.random.fold_in(key_list[8], 71), 0),
        "pair_tiles": draw_pair_tiles(jax.random.fold_in(key_list[8], 71), 0),
        "tile_live": draw_tile_live(jax.random.fold_in(key_list[8], 71), 0),
        "radial_weight": normal_values(key_list[5], (CH, RADIAL), (4 * RADIAL) ** -0.5, 1.0, ((0, 4),), jnp.float32),
        "mix_weight": normal_values(key_list[6], (3, CH, CH), CH ** -0.5, 0.5),
        "out_grad": normal_values(key_list[7], (CH, COMPONENTS, NATOMS), 1.0, 6.0, ((0, 4), (2, 8))),
    }


SOFTENING = 0.25
CUTOFF = 2.5
CUTOFF_SQ = 6.25
SHARPNESS = 10.0
ROOT_THREE = math.sqrt(3.0)
ORDER_OF = (0, 1, 1, 1, 2, 2, 2, 2, 2)

def geometry(target_pos, source_pos, pair_keep, radial_count):
    offset = source_pos[:, None, :] - target_pos[:, :, None]
    dist_sq = lax.optimization_barrier(jnp.sum(offset * offset, axis=0)) + SOFTENING
    distance = jnp.sqrt(dist_sq)
    along_x = offset[0] / distance
    along_y = offset[1] / distance
    along_z = offset[2] / distance
    harmonics = jnp.stack([jnp.ones_like(along_x), along_x, along_y, along_z, ROOT_THREE * along_x * along_y, ROOT_THREE * along_y * along_z, ROOT_THREE * along_x * along_z, 0.5 * (3.0 * along_z * along_z - 1.0), 0.5 * ROOT_THREE * (along_x * along_x - along_y * along_y)])
    envelope = jnp.square(jnp.maximum(1.0 - dist_sq / CUTOFF_SQ, 0.0)) * pair_keep
    centers = (jnp.arange(radial_count, dtype=jnp.float32) + 0.5) * (CUTOFF / radial_count)
    radial = jnp.exp(-SHARPNESS * jnp.square(distance[None] - centers[:, None, None])) * envelope[None]
    return (harmonics, radial)

def take_block(array, blk_index, block_size):
    return lax.dynamic_slice_in_dim(array, blk_index * block_size, block_size, array.ndim - 1)

def add_block(array, blk_index, value, block_size):
    current = take_block(array, blk_index, block_size)
    return lax.dynamic_update_slice_in_dim(array, current + value, blk_index * block_size, array.ndim - 1)

def reference(positions, features, send_rows, pair_tiles, tile_live, radial_weight, mix_weight, out_grad):
    radial_count = radial_weight.shape[1]
    mixing = jnp.take(mix_weight, jnp.array(ORDER_OF, dtype=jnp.int32), axis=0).astype(jnp.float32)
    src_atoms = SRC_BLK * BLOCK

    def domain(dom_index):
        start = dom_index * A_DEV
        own_pos = lax.dynamic_slice_in_dim(positions, start, A_DEV, 1)
        own_feat = lax.dynamic_slice_in_dim(features, start, A_DEV, 1)
        own_upstream = lax.dynamic_slice_in_dim(out_grad, start, A_DEV, 2)
        pos_list = [own_pos]
        feat_list = [own_feat]
        for level_bit in range(LEVELS):
            partner = jnp.bitwise_xor(dom_index, 1 << level_bit)
            sent_rows = lax.dynamic_index_in_dim(send_rows, partner * LEVELS + level_bit, 0, keepdims=False)
            partner_pos = lax.dynamic_slice_in_dim(positions, partner * A_DEV, A_DEV, 1)
            partner_feat = lax.dynamic_slice_in_dim(features, partner * A_DEV, A_DEV, 1)
            pos_list.append(jnp.take(partner_pos, sent_rows, axis=1))
            feat_list.append(jnp.take(partner_feat, sent_rows, axis=1))
        src_pos = jnp.concatenate(pos_list, axis=1)
        src_feat = jnp.concatenate(feat_list, axis=1)
        tiles = lax.dynamic_slice_in_dim(pair_tiles, dom_index * TILES_DEV, TILES_DEV, 0)
        live = lax.dynamic_slice_in_dim(tile_live, dom_index * TILES_DEV, TILES_DEV, 0)

        def tile_parts(tile_pair):
            target_blk = tile_pair[0]
            source_blk = tile_pair[1]
            same = (target_blk == source_blk).astype(jnp.float32)
            pair_keep = 1.0 - same * jnp.eye(BLOCK, dtype=jnp.float32)
            target_pos = take_block(src_pos, target_blk, BLOCK)
            source_pos = take_block(src_pos, source_blk, BLOCK)

            def geo_fn(first_pos, second_pos):
                return geometry(first_pos, second_pos, pair_keep, radial_count)
            return (target_blk, source_blk, target_pos, source_pos, geo_fn)

        def forward_step(moments, tile_item):
            tile_pair, tile_flag = tile_item

            def work(running):
                target_blk, source_blk, target_pos, source_pos, geo_fn = tile_parts(tile_pair)
                harmonics, radial = geo_fn(target_pos, source_pos)
                pair_values = (harmonics[:, None] * radial[None]).astype(jnp.bfloat16)
                source_feat = take_block(src_feat, source_blk, BLOCK)
                message = jnp.einsum('lkij,cj->clki', pair_values.astype(jnp.float32), source_feat.astype(jnp.float32))
                contrib = jnp.einsum('clki,ck->cli', message, radial_weight)
                return add_block(running, target_blk, contrib, BLOCK)
            return (lax.cond(tile_flag > 0, work, lambda running: running, moments), None)
        moments, _ = lax.scan(forward_step, jnp.zeros((CH, COMPONENTS, A_DEV), jnp.float32), (tiles, live))
        packed = moments.astype(jnp.bfloat16)
        mixed_out = jnp.einsum('lxc,cli->xli', mixing, packed.astype(jnp.float32))
        scalar_part = mixed_out[:, 0, :]
        gate_value = jax.nn.sigmoid(scalar_part)
        result = jnp.concatenate([(scalar_part * gate_value)[:, None, :], mixed_out[:, 1:, :] * gate_value[:, None, :]], axis=1).astype(jnp.bfloat16)
        upstream = own_upstream.astype(jnp.float32)
        scalar_grad = upstream[:, 0, :] * (gate_value * (1.0 + scalar_part * (1.0 - gate_value))) + gate_value * (1.0 - gate_value) * lax.optimization_barrier(jnp.sum(upstream[:, 1:, :] * mixed_out[:, 1:, :], axis=1))
        rest_grad = upstream[:, 1:, :] * gate_value[:, None, :]
        dz_packed = jnp.concatenate([scalar_grad[:, None, :], rest_grad], axis=1).astype(jnp.bfloat16)
        moment_grad_all = jnp.einsum('lxc,xli->cli', mixing, dz_packed.astype(jnp.float32))

        def backward_step(carried, tile_item):
            tile_pair, tile_flag = tile_item

            def work(running):
                grad_src, dpos_src, grad_rad = running
                target_blk, source_blk, target_pos, source_pos, geo_fn = tile_parts(tile_pair)
                (harmonics, radial), pullback = jax.vjp(geo_fn, target_pos, source_pos)
                pair_values = (harmonics[:, None] * radial[None]).astype(jnp.bfloat16)
                values_wide = pair_values.astype(jnp.float32)
                source_feat = take_block(src_feat, source_blk, BLOCK).astype(jnp.float32)
                message = jnp.einsum('lkij,cj->clki', values_wide, source_feat)
                moment_grad = take_block(moment_grad_all, target_blk, BLOCK)
                grad_rad = grad_rad + jnp.einsum('clki,cli->ck', message, moment_grad)
                weighted = (radial_weight[:, None, :, None] * moment_grad[:, :, None, :]).astype(jnp.bfloat16).astype(jnp.float32)
                grad_source = jnp.einsum('clki,lkij->cj', weighted, values_wide)
                value_grad = jnp.einsum('clki,cj->lkij', weighted, source_feat)
                harm_grad = lax.optimization_barrier(jnp.sum(value_grad * radial[None], axis=1))
                rad_grad = lax.optimization_barrier(jnp.sum(value_grad * harmonics[:, None], axis=0))
                target_grad, source_grad_pos = pullback((harm_grad, rad_grad))
                grad_src = add_block(grad_src, source_blk, grad_source, BLOCK)
                dpos_src = add_block(dpos_src, target_blk, target_grad, BLOCK)
                dpos_src = add_block(dpos_src, source_blk, source_grad_pos, BLOCK)
                return (grad_src, dpos_src, grad_rad)
            return (lax.cond(tile_flag > 0, work, lambda running: running, carried), None)
        init = (jnp.zeros((CH, src_atoms), jnp.float32), jnp.zeros((3, src_atoms), jnp.float32), jnp.zeros((CH, radial_count), jnp.float32))
        (grad_src, dpos_src, grad_rad), _ = lax.scan(backward_step, init, (tiles, live))
        return (result, grad_src, dpos_src, grad_rad)
    outs_all = lax.map(domain, jnp.arange(N_SPACE, dtype=jnp.int32))
    result_all, grad_src_all, dpos_all, grad_rad_all = outs_all
    own_grad = grad_src_all[:, :, :A_DEV]
    own_dpos = dpos_all[:, :, :A_DEV]
    rows_all = send_rows.reshape(N_SPACE, LEVELS, BLOCK)
    domains = jnp.arange(N_SPACE, dtype=jnp.int32)
    for level_bit in range(LEVELS):
        partners = jnp.bitwise_xor(domains, 1 << level_bit)
        low = A_DEV + level_bit * BLOCK
        back_grad = jnp.take(grad_src_all[:, :, low:low + BLOCK], partners, axis=0)
        back_pos = jnp.take(dpos_all[:, :, low:low + BLOCK], partners, axis=0)
        sent_rows = rows_all[:, level_bit]
        own_grad = jax.vmap(lambda target, where, value: target.at[:, where].add(value))(own_grad, sent_rows, back_grad)
        own_dpos = jax.vmap(lambda target, where, value: target.at[:, where].add(value))(own_dpos, sent_rows, back_pos)
    output = result_all.transpose(1, 2, 0, 3).reshape(CH, COMPONENTS, NATOMS)
    grad_features = own_grad.transpose(1, 0, 2).reshape(CH, NATOMS).astype(jnp.bfloat16)
    forces = (-own_dpos).transpose(1, 0, 2).reshape(3, NATOMS)
    grad_radial = lax.optimization_barrier(jnp.sum(grad_rad_all, axis=0))
    return (output, grad_features, forces, grad_radial)
```

```python
import math

import jax
import jax.numpy as jnp
from jax import lax
from jax.sharding import PartitionSpec as P

SOFTENING = 0.25
CUTOFF = 2.5
CUTOFF_SQ = 6.25
SHARPNESS = 10.0
ROOT_THREE = math.sqrt(3.0)
ORDER_OF = (0, 1, 1, 1, 2, 2, 2, 2, 2)


def partner(value, axis, bit):
    mask = 2**bit
    pairs = [(source, source ^ mask) for source in range(lax.axis_size(axis))]
    return lax.ppermute(value, axis, pairs)


def geometry(target_pos, source_pos, pair_keep, radial_count):
    offset = source_pos[:, None, :] - target_pos[:, :, None]
    dist_sq = jnp.sum(offset * offset, axis=0) + SOFTENING
    distance = jnp.sqrt(dist_sq)
    along_x = offset[0] / distance
    along_y = offset[1] / distance
    along_z = offset[2] / distance
    harmonics = jnp.stack(
        [
            jnp.ones_like(along_x),
            along_x,
            along_y,
            along_z,
            ROOT_THREE * along_x * along_y,
            ROOT_THREE * along_y * along_z,
            ROOT_THREE * along_x * along_z,
            0.5 * (3.0 * along_z * along_z - 1.0),
            0.5 * ROOT_THREE * (along_x * along_x - along_y * along_y),
        ]
    )
    envelope = jnp.square(jnp.maximum(1.0 - dist_sq / CUTOFF_SQ, 0.0)) * pair_keep
    centers = (jnp.arange(radial_count, dtype=jnp.float32) + 0.5) * (CUTOFF / radial_count)
    radial = (
        jnp.exp(-SHARPNESS * jnp.square(distance[None] - centers[:, None, None])) * envelope[None]
    )
    return (harmonics, radial)


def take_block(array, blk_index, block_size):
    return lax.dynamic_slice_in_dim(array, blk_index * block_size, block_size, array.ndim - 1)


def add_block(array, blk_index, value, block_size):
    current = take_block(array, blk_index, block_size)
    return lax.dynamic_update_slice_in_dim(
        array, current + value, blk_index * block_size, array.ndim - 1
    )


def body(
    positions, features, send_rows, pair_tiles, tile_live, radial_weight, mix_weight, out_grad
):
    block_size = send_rows.shape[1]
    atoms_dev = positions.shape[1]
    chan_dev = features.shape[0]
    radial_count = radial_weight.shape[1]
    components = out_grad.shape[1]
    levels = lax.axis_size("space").bit_length() - 1
    pos_list = [positions]
    feat_list = [features]
    for level_bit in range(levels):
        sent_rows = send_rows[level_bit]
        got_feat, got_pos = (
            partner(
                jnp.take(features, sent_rows, axis=1).astype(jnp.float32), "space", level_bit
            ).astype(jnp.bfloat16),
            partner(jnp.take(positions, sent_rows, axis=1), "space", level_bit),
        )
        feat_list.append(got_feat)
        pos_list.append(got_pos)
    src_pos = jnp.concatenate(pos_list, axis=1)
    src_feat = jnp.concatenate(feat_list, axis=1)
    src_atoms = src_pos.shape[1]
    live_count = jnp.sum(tile_live)

    def tile_parts(tile_index):
        target_blk = pair_tiles[tile_index, 0]
        source_blk = pair_tiles[tile_index, 1]
        same = (target_blk == source_blk).astype(jnp.float32)
        pair_keep = 1.0 - same * jnp.eye(block_size, dtype=jnp.float32)
        target_pos = take_block(src_pos, target_blk, block_size)
        source_pos = take_block(src_pos, source_blk, block_size)

        def geo_fn(first_pos, second_pos):
            return geometry(first_pos, second_pos, pair_keep, radial_count)

        return (target_blk, source_blk, target_pos, source_pos, geo_fn)

    def forward_tile(tile_index, msg_acc):
        target_blk, source_blk, target_pos, source_pos, geo_fn = tile_parts(tile_index)
        harmonics, radial = geo_fn(target_pos, source_pos)
        source_feat = take_block(src_feat, source_blk, block_size)
        pair_values = (harmonics[:, None] * radial[None]).astype(jnp.bfloat16)
        message = jnp.einsum(
            "lkij,cj->clki", pair_values, source_feat, preferred_element_type=jnp.float32
        )
        return add_block(msg_acc, target_blk, message, block_size)

    msg_acc = lax.fori_loop(
        0,
        live_count,
        forward_tile,
        jnp.zeros((chan_dev, components, radial_count, atoms_dev), jnp.float32),
    )
    moments = jnp.einsum("clki,ck->cli", msg_acc, radial_weight)
    packed = moments.astype(jnp.bfloat16)
    mixing = jnp.take(mix_weight, jnp.array(ORDER_OF, dtype=jnp.int32), axis=0)
    offset = lax.axis_index("chan") * chan_dev
    gathered_piece = lax.all_gather(packed, "chan", axis=0, tiled=True)
    weight_part = lax.dynamic_slice(
        mixing, (0, offset, 0), (components, chan_dev, gathered_piece.shape[0])
    )
    mixed_out = jnp.einsum(
        "lxc,cli->xli", weight_part, gathered_piece, preferred_element_type=jnp.float32
    )
    scalar_part = mixed_out[:, 0, :]
    gate_value = jax.nn.sigmoid(scalar_part)
    result = jnp.concatenate(
        [(scalar_part * gate_value)[:, None, :], mixed_out[:, 1:, :] * gate_value[:, None, :]],
        axis=1,
    ).astype(jnp.bfloat16)
    upstream = out_grad.astype(jnp.float32)
    scalar_grad = upstream[:, 0, :] * (
        gate_value * (1.0 + scalar_part * (1.0 - gate_value))
    ) + gate_value * (1.0 - gate_value) * jnp.sum(upstream[:, 1:, :] * mixed_out[:, 1:, :], axis=1)
    rest_grad = upstream[:, 1:, :] * gate_value[:, None, :]
    dz_packed = jnp.concatenate([scalar_grad[:, None, :], rest_grad], axis=1).astype(jnp.bfloat16)
    gathered_piece = lax.all_gather(dz_packed, "chan", axis=0, tiled=True)
    weight_part = lax.dynamic_slice(
        mixing, (0, 0, offset), (components, gathered_piece.shape[0], chan_dev)
    )
    moment_grad_all = jnp.einsum(
        "lxc,xli->cli", weight_part, gathered_piece, preferred_element_type=jnp.float32
    )
    grad_rad = jnp.einsum("clki,cli->ck", msg_acc, moment_grad_all)
    weighted_all = (radial_weight[:, None, :, None] * moment_grad_all[:, :, None, :]).astype(
        jnp.bfloat16
    )

    def backward_tile(tile_index, running):
        grad_src, dpos_src = running
        target_blk, source_blk, target_pos, source_pos, geo_fn = tile_parts(tile_index)
        (harmonics, radial), pullback = jax.vjp(geo_fn, target_pos, source_pos)
        source_feat = take_block(src_feat, source_blk, block_size)
        weighted = take_block(weighted_all, target_blk, block_size)
        pair_values = (harmonics[:, None] * radial[None]).astype(jnp.bfloat16)
        grad_source = jnp.einsum(
            "clki,lkij->cj", weighted, pair_values, preferred_element_type=jnp.float32
        )
        value_grad = jnp.einsum(
            "clki,cj->lkij", weighted, source_feat, preferred_element_type=jnp.float32
        )
        harm_grad = jnp.sum(value_grad * radial[None], axis=1)
        rad_grad = jnp.sum(value_grad * harmonics[:, None], axis=0)
        target_grad, source_grad_pos = pullback((harm_grad, rad_grad))
        grad_src = add_block(grad_src, source_blk, grad_source, block_size)
        dpos_src = add_block(dpos_src, target_blk, target_grad, block_size)
        dpos_src = add_block(dpos_src, source_blk, source_grad_pos, block_size)
        return (grad_src, dpos_src)

    init = (
        jnp.zeros((chan_dev, src_atoms), jnp.float32),
        jnp.zeros((3, src_atoms), jnp.float32),
    )
    grad_src, dpos_src = lax.fori_loop(0, live_count, backward_tile, init)
    dpos_src = lax.psum(dpos_src, "chan")
    own_grad = grad_src[:, :atoms_dev]
    own_dpos = dpos_src[:, :atoms_dev]
    for level_bit in range(levels):
        low = atoms_dev + level_bit * block_size
        back_grad, back_pos = partner(
            (grad_src[:, low : low + block_size], dpos_src[:, low : low + block_size]),
            "space",
            level_bit,
        )
        sent_rows = send_rows[level_bit]
        own_grad = own_grad.at[:, sent_rows].add(back_grad)
        own_dpos = own_dpos.at[:, sent_rows].add(back_pos)
    grad_radial = lax.psum(grad_rad, "space")
    return (result, own_grad.astype(jnp.bfloat16), -own_dpos, grad_radial)


def solution(mesh):
    placed = (
        P(None, "space"),
        P("chan", "space"),
        P("space", None),
        P("space", None),
        P("space"),
        P("chan", None),
        P(),
        P("chan", None, "space"),
    )
    return jax.shard_map(
        body,
        mesh=mesh,
        in_specs=placed,
        out_specs=(P("chan", None, "space"), P("chan", "space"), P(None, "space"), P("chan", None)),
        check_vma=False,
    )
```

```python
import math

import jax
import jax.numpy as jnp
from jax import lax
from jax.sharding import PartitionSpec as P

SOFTENING = 0.25
CUTOFF = 2.5
CUTOFF_SQ = 6.25
SHARPNESS = 10.0
ROOT_THREE = math.sqrt(3.0)
ORDER_OF = (0, 1, 1, 1, 2, 2, 2, 2, 2)


def partner(value, axis, bit):
    mask = 2**bit
    pairs = [(source, source ^ mask) for source in range(lax.axis_size(axis))]
    return lax.ppermute(value, axis, pairs)


def geometry(target_pos, source_pos, pair_keep, radial_count):
    offset = source_pos[:, None, :] - target_pos[:, :, None]
    dist_sq = jnp.sum(offset * offset, axis=0) + SOFTENING
    distance = jnp.sqrt(dist_sq)
    along_x = offset[0] / distance
    along_y = offset[1] / distance
    along_z = offset[2] / distance
    harmonics = jnp.stack(
        [
            jnp.ones_like(along_x),
            along_x,
            along_y,
            along_z,
            ROOT_THREE * along_x * along_y,
            ROOT_THREE * along_y * along_z,
            ROOT_THREE * along_x * along_z,
            0.5 * (3.0 * along_z * along_z - 1.0),
            0.5 * ROOT_THREE * (along_x * along_x - along_y * along_y),
        ]
    )
    envelope = jnp.square(jnp.maximum(1.0 - dist_sq / CUTOFF_SQ, 0.0)) * pair_keep
    centers = (jnp.arange(radial_count, dtype=jnp.float32) + 0.5) * (CUTOFF / radial_count)
    radial = (
        jnp.exp(-SHARPNESS * jnp.square(distance[None] - centers[:, None, None])) * envelope[None]
    )
    return (harmonics, radial)


def take_block(array, blk_index, block_size):
    return lax.dynamic_slice_in_dim(array, blk_index * block_size, block_size, array.ndim - 1)


def add_block(array, blk_index, value, block_size):
    current = take_block(array, blk_index, block_size)
    return lax.dynamic_update_slice_in_dim(
        array, current + value, blk_index * block_size, array.ndim - 1
    )


def body(
    positions, features, send_rows, pair_tiles, tile_live, radial_weight, mix_weight, out_grad
):
    block_size = send_rows.shape[1]
    atoms_dev = positions.shape[1]
    chan_dev = features.shape[0]
    radial_count = radial_weight.shape[1]
    components = out_grad.shape[1]
    levels = lax.axis_size("space").bit_length() - 1
    pos_list = [positions]
    feat_list = [features]
    for level_bit in range(levels):
        sent_rows = send_rows[level_bit]
        got_feat, got_pos = (
            partner(
                jnp.take(features, sent_rows, axis=1).astype(jnp.float32), "space", level_bit
            ).astype(jnp.bfloat16),
            partner(jnp.take(positions, sent_rows, axis=1), "space", level_bit),
        )
        feat_list.append(got_feat)
        pos_list.append(got_pos)
    src_pos = jnp.concatenate(pos_list, axis=1)
    src_feat = jnp.concatenate(feat_list, axis=1)
    src_atoms = src_pos.shape[1]
    src_blocks = src_atoms // block_size
    own_blocks = atoms_dev // block_size
    tile_count = pair_tiles.shape[0]
    target_idx = pair_tiles[:, 0]
    source_idx = pair_tiles[:, 1]
    live = tile_live.astype(jnp.float32)
    block_ids = jnp.arange(src_blocks, dtype=jnp.int32)
    target_hot = (target_idx[:, None] == block_ids[None]).astype(jnp.float32) * live[:, None]
    source_hot = (source_idx[:, None] == block_ids[None]).astype(jnp.float32) * live[:, None]
    same = (target_idx == source_idx).astype(jnp.float32)
    eye = jnp.eye(block_size, dtype=jnp.float32)
    keep_all = live[:, None, None] * (1.0 - same[:, None, None] * eye[None])
    pos_blocks = jnp.moveaxis(src_pos.reshape(3, src_blocks, block_size), 1, 0)
    feat_blocks = jnp.moveaxis(src_feat.reshape(chan_dev, src_blocks, block_size), 1, 0)
    target_pos_all = jnp.take(pos_blocks, target_idx, axis=0)
    source_pos_all = jnp.take(pos_blocks, source_idx, axis=0)
    source_feat_all = jnp.take(feat_blocks, source_idx, axis=0)

    def pick(array, tile_index):
        return lax.dynamic_index_in_dim(array, tile_index, 0, keepdims=False)

    def tile_parts(tile_index):
        pair_keep = pick(keep_all, tile_index)
        target_pos = pick(target_pos_all, tile_index)
        source_pos = pick(source_pos_all, tile_index)

        def geo_fn(first_pos, second_pos):
            return geometry(first_pos, second_pos, pair_keep, radial_count)

        return (target_pos, source_pos, geo_fn)

    def forward_tile(tile_index, msg_acc):
        target_pos, source_pos, geo_fn = tile_parts(tile_index)
        harmonics, radial = geo_fn(target_pos, source_pos)
        source_feat = pick(source_feat_all, tile_index)
        pair_values = (harmonics[:, None] * radial[None]).astype(jnp.bfloat16)
        message = jnp.einsum(
            "lkij,cj->clki", pair_values, source_feat, preferred_element_type=jnp.float32
        )
        hot = pick(target_hot, tile_index)[:own_blocks]
        return msg_acc + hot[None, None, None, :, None] * message[:, :, :, None, :]

    msg_acc = lax.fori_loop(
        0,
        tile_count,
        forward_tile,
        jnp.zeros((chan_dev, components, radial_count, own_blocks, block_size), jnp.float32),
    ).reshape(chan_dev, components, radial_count, atoms_dev)
    moments = jnp.einsum("clki,ck->cli", msg_acc, radial_weight)
    packed = moments.astype(jnp.bfloat16)
    mixing = jnp.take(mix_weight, jnp.array(ORDER_OF, dtype=jnp.int32), axis=0)
    offset = lax.axis_index("chan") * chan_dev
    gathered_piece = lax.all_gather(packed, "chan", axis=0, tiled=True)
    weight_part = lax.dynamic_slice(
        mixing, (0, offset, 0), (components, chan_dev, gathered_piece.shape[0])
    )
    mixed_out = jnp.einsum(
        "lxc,cli->xli", weight_part, gathered_piece, preferred_element_type=jnp.float32
    )
    scalar_part = mixed_out[:, 0, :]
    gate_value = jax.nn.sigmoid(scalar_part)
    result = jnp.concatenate(
        [(scalar_part * gate_value)[:, None, :], mixed_out[:, 1:, :] * gate_value[:, None, :]],
        axis=1,
    ).astype(jnp.bfloat16)
    upstream = out_grad.astype(jnp.float32)
    scalar_grad = upstream[:, 0, :] * (
        gate_value * (1.0 + scalar_part * (1.0 - gate_value))
    ) + gate_value * (1.0 - gate_value) * jnp.sum(upstream[:, 1:, :] * mixed_out[:, 1:, :], axis=1)
    rest_grad = upstream[:, 1:, :] * gate_value[:, None, :]
    dz_packed = jnp.concatenate([scalar_grad[:, None, :], rest_grad], axis=1).astype(jnp.bfloat16)
    gathered_piece = lax.all_gather(dz_packed, "chan", axis=0, tiled=True)
    weight_part = lax.dynamic_slice(
        mixing, (0, 0, offset), (components, gathered_piece.shape[0], chan_dev)
    )
    moment_grad_all = jnp.einsum(
        "lxc,xli->cli", weight_part, gathered_piece, preferred_element_type=jnp.float32
    )
    grad_rad = jnp.einsum("clki,cli->ck", msg_acc, moment_grad_all)
    weighted_all = (radial_weight[:, None, :, None] * moment_grad_all[:, :, None, :]).astype(
        jnp.bfloat16
    )
    weighted_blocks = jnp.moveaxis(
        weighted_all.reshape(chan_dev, components, radial_count, own_blocks, block_size), 3, 0
    )
    weighted_tiles = jnp.take(weighted_blocks, jnp.minimum(target_idx, own_blocks - 1), axis=0)

    def backward_tile(tile_index, running):
        grad_tiles, target_grads, source_grads = running
        target_pos, source_pos, geo_fn = tile_parts(tile_index)
        (harmonics, radial), pullback = jax.vjp(geo_fn, target_pos, source_pos)
        source_feat = pick(source_feat_all, tile_index)
        weighted = pick(weighted_tiles, tile_index)
        pair_values = (harmonics[:, None] * radial[None]).astype(jnp.bfloat16)
        grad_source = jnp.einsum(
            "clki,lkij->cj", weighted, pair_values, preferred_element_type=jnp.float32
        )
        value_grad = jnp.einsum(
            "clki,cj->lkij", weighted, source_feat, preferred_element_type=jnp.float32
        )
        harm_grad = jnp.sum(value_grad * radial[None], axis=1)
        rad_grad = jnp.sum(value_grad * harmonics[:, None], axis=0)
        target_grad, source_grad_pos = pullback((harm_grad, rad_grad))
        grad_tiles = lax.dynamic_update_index_in_dim(grad_tiles, grad_source, tile_index, 0)
        target_grads = lax.dynamic_update_index_in_dim(target_grads, target_grad, tile_index, 0)
        source_grads = lax.dynamic_update_index_in_dim(
            source_grads, source_grad_pos, tile_index, 0
        )
        return (grad_tiles, target_grads, source_grads)

    init = (
        jnp.zeros((tile_count, chan_dev, block_size), jnp.float32),
        jnp.zeros((tile_count, 3, block_size), jnp.float32),
        jnp.zeros((tile_count, 3, block_size), jnp.float32),
    )
    grad_tiles, target_grads, source_grads = lax.fori_loop(0, tile_count, backward_tile, init)
    grad_src = jnp.sum(
        source_hot[:, None, :, None] * grad_tiles[:, :, None, :], axis=0
    ).reshape(chan_dev, src_atoms)
    dpos_src = jnp.sum(
        target_hot[:, None, :, None] * target_grads[:, :, None, :]
        + source_hot[:, None, :, None] * source_grads[:, :, None, :],
        axis=0,
    ).reshape(3, src_atoms)
    for chan_bit in range(lax.axis_size("chan").bit_length() - 1):
        dpos_src = dpos_src + partner(dpos_src, "chan", chan_bit)
    own_both = jnp.concatenate([grad_src[:, :atoms_dev], dpos_src[:, :atoms_dev]], axis=0)
    back_list = []
    for level_bit in range(levels):
        low = atoms_dev + level_bit * block_size
        ghost_both = jnp.concatenate(
            [grad_src[:, low : low + block_size], dpos_src[:, low : low + block_size]], axis=0
        )
        back_both, other_rad = partner((ghost_both, grad_rad), "space", level_bit)
        grad_rad = grad_rad + other_rad
        back_list.append(back_both)
    all_rows = send_rows[:levels].reshape(-1)
    own_both = own_both.at[:, all_rows].add(jnp.concatenate(back_list, axis=1))
    own_grad = own_both[:chan_dev]
    own_dpos = own_both[chan_dev:]
    return (result, own_grad.astype(jnp.bfloat16), -own_dpos, grad_rad)


def solution(mesh):
    placed = (
        P(None, "space"),
        P("chan", "space"),
        P("space", None),
        P("space", None),
        P("space"),
        P("chan", None),
        P(),
        P("chan", None, "space"),
    )
    return jax.shard_map(
        body,
        mesh=mesh,
        in_specs=placed,
        out_specs=(P("chan", None, "space"), P("chan", "space"), P(None, "space"), P("chan", None)),
        check_vma=False,
    )
```

```python
import math

import jax
import jax.numpy as jnp
from jax import lax
from jax.sharding import PartitionSpec as P

SOFTENING = 0.25
CUTOFF = 2.5
CUTOFF_SQ = 6.25
SHARPNESS = 10.0
ROOT_THREE = math.sqrt(3.0)
ORDER_OF = (0, 1, 1, 1, 2, 2, 2, 2, 2)


def partner(value, axis, bit):
    mask = 2**bit
    pairs = [(source, source ^ mask) for source in range(lax.axis_size(axis))]
    return lax.ppermute(value, axis, pairs)


def geometry(target_pos, source_pos, pair_keep, radial_count):
    offset = source_pos[:, None, :] - target_pos[:, :, None]
    dist_sq = jnp.sum(offset * offset, axis=0) + SOFTENING
    distance = jnp.sqrt(dist_sq)
    along_x = offset[0] / distance
    along_y = offset[1] / distance
    along_z = offset[2] / distance
    harmonics = jnp.stack(
        [
            jnp.ones_like(along_x),
            along_x,
            along_y,
            along_z,
            ROOT_THREE * along_x * along_y,
            ROOT_THREE * along_y * along_z,
            ROOT_THREE * along_x * along_z,
            0.5 * (3.0 * along_z * along_z - 1.0),
            0.5 * ROOT_THREE * (along_x * along_x - along_y * along_y),
        ]
    )
    envelope = jnp.square(jnp.maximum(1.0 - dist_sq / CUTOFF_SQ, 0.0)) * pair_keep
    centers = (jnp.arange(radial_count, dtype=jnp.float32) + 0.5) * (CUTOFF / radial_count)
    radial = (
        jnp.exp(-SHARPNESS * jnp.square(distance[None] - centers[:, None, None])) * envelope[None]
    )
    return (harmonics, radial)


def take_block(array, blk_index, block_size):
    return lax.dynamic_slice_in_dim(array, blk_index * block_size, block_size, array.ndim - 1)


def add_block(array, blk_index, value, block_size):
    current = take_block(array, blk_index, block_size)
    return lax.dynamic_update_slice_in_dim(
        array, current + value, blk_index * block_size, array.ndim - 1
    )


def body(
    positions, features, send_rows, pair_tiles, tile_live, radial_weight, mix_weight, out_grad
):
    block_size = send_rows.shape[1]
    atoms_dev = positions.shape[1]
    chan_dev = features.shape[0]
    radial_count = radial_weight.shape[1]
    components = out_grad.shape[1]
    levels = lax.axis_size("space").bit_length() - 1
    pos_list = [positions]
    feat_list = [features]
    for level_bit in range(levels):
        sent_rows = send_rows[level_bit]
        got_feat, got_pos = (
            partner(
                jnp.take(features, sent_rows, axis=1).astype(jnp.float32), "space", level_bit
            ).astype(jnp.bfloat16),
            partner(jnp.take(positions, sent_rows, axis=1), "space", level_bit),
        )
        feat_list.append(got_feat)
        pos_list.append(got_pos)
    src_pos = jnp.concatenate(pos_list, axis=1)
    src_feat = jnp.concatenate(feat_list, axis=1)
    src_atoms = src_pos.shape[1]
    src_blocks = src_atoms // block_size
    own_blocks = atoms_dev // block_size
    tile_count = pair_tiles.shape[0]
    target_idx = pair_tiles[:, 0]
    source_idx = pair_tiles[:, 1]
    live = tile_live.astype(jnp.float32)
    block_ids = jnp.arange(src_blocks, dtype=jnp.int32)
    target_hot = (target_idx[:, None] == block_ids[None]).astype(jnp.float32) * live[:, None]
    source_hot = (source_idx[:, None] == block_ids[None]).astype(jnp.float32) * live[:, None]
    same = (target_idx == source_idx).astype(jnp.float32)
    eye = jnp.eye(block_size, dtype=jnp.float32)
    keep_all = live[:, None, None] * (1.0 - same[:, None, None] * eye[None])
    pos_blocks = jnp.moveaxis(src_pos.reshape(3, src_blocks, block_size), 1, 0)
    feat_blocks = jnp.moveaxis(src_feat.reshape(chan_dev, src_blocks, block_size), 1, 0)
    target_pos_all = jnp.take(pos_blocks, target_idx, axis=0, mode="clip")
    source_pos_all = jnp.take(pos_blocks, source_idx, axis=0, mode="clip")
    source_feat_all = jnp.take(feat_blocks, source_idx, axis=0, mode="clip")

    def pick(array, tile_index):
        return lax.dynamic_index_in_dim(array, tile_index, 0, keepdims=False)

    def tile_parts(tile_index):
        pair_keep = pick(keep_all, tile_index)
        target_pos = pick(target_pos_all, tile_index)
        source_pos = pick(source_pos_all, tile_index)

        def geo_fn(first_pos, second_pos):
            return geometry(first_pos, second_pos, pair_keep, radial_count)

        return (target_pos, source_pos, geo_fn)

    def forward_tile(tile_index, msg_acc):
        target_pos, source_pos, geo_fn = tile_parts(tile_index)
        harmonics, radial = geo_fn(target_pos, source_pos)
        source_feat = pick(source_feat_all, tile_index)
        pair_values = (harmonics[:, None] * radial[None]).astype(jnp.bfloat16)
        message = jnp.einsum(
            "lkij,cj->clki", pair_values, source_feat, preferred_element_type=jnp.float32
        )
        hot = pick(target_hot, tile_index)[:own_blocks]
        return msg_acc + hot[:, None, None, None, None] * message[None]

    msg_acc = lax.fori_loop(
        0,
        tile_count,
        forward_tile,
        jnp.zeros((own_blocks, chan_dev, components, radial_count, block_size), jnp.float32),
    )
    moments = jnp.einsum("bclki,ck->clbi", msg_acc, radial_weight).reshape(
        chan_dev, components, atoms_dev
    )
    packed = moments.astype(jnp.bfloat16)
    mixing = jnp.take(mix_weight, jnp.array(ORDER_OF, dtype=jnp.int32), axis=0)
    offset = lax.axis_index("chan") * chan_dev
    gathered_piece = lax.all_gather(packed, "chan", axis=0, tiled=True)
    weight_part = lax.dynamic_slice(
        mixing, (0, offset, 0), (components, chan_dev, gathered_piece.shape[0])
    )
    mixed_out = jnp.einsum(
        "lxc,cli->xli", weight_part, gathered_piece, preferred_element_type=jnp.float32
    )
    scalar_part = mixed_out[:, 0, :]
    gate_value = jax.nn.sigmoid(scalar_part)
    result = jnp.concatenate(
        [(scalar_part * gate_value)[:, None, :], mixed_out[:, 1:, :] * gate_value[:, None, :]],
        axis=1,
    ).astype(jnp.bfloat16)
    upstream = out_grad.astype(jnp.float32)
    scalar_grad = upstream[:, 0, :] * (
        gate_value * (1.0 + scalar_part * (1.0 - gate_value))
    ) + gate_value * (1.0 - gate_value) * jnp.sum(upstream[:, 1:, :] * mixed_out[:, 1:, :], axis=1)
    rest_grad = upstream[:, 1:, :] * gate_value[:, None, :]
    dz_packed = jnp.concatenate([scalar_grad[:, None, :], rest_grad], axis=1).astype(jnp.bfloat16)
    gathered_piece = lax.all_gather(dz_packed, "chan", axis=0, tiled=True)
    weight_part = lax.dynamic_slice(
        mixing, (0, 0, offset), (components, gathered_piece.shape[0], chan_dev)
    )
    moment_grad_all = jnp.einsum(
        "lxc,xli->cli", weight_part, gathered_piece, preferred_element_type=jnp.float32
    )
    grad_blocks = jnp.moveaxis(
        moment_grad_all.reshape(chan_dev, components, own_blocks, block_size), 2, 0
    )
    grad_rad = jnp.einsum("bclki,bcli->ck", msg_acc, grad_blocks)
    grad_tiles_in = jnp.take(grad_blocks, target_idx, axis=0, mode="clip")

    def backward_tile(tile_index, running):
        grad_tiles, target_grads, source_grads = running
        target_pos, source_pos, geo_fn = tile_parts(tile_index)
        (harmonics, radial), pullback = jax.vjp(geo_fn, target_pos, source_pos)
        source_feat = pick(source_feat_all, tile_index)
        moment_grad = pick(grad_tiles_in, tile_index)
        weighted = (radial_weight[:, None, :, None] * moment_grad[:, :, None, :]).astype(
            jnp.bfloat16
        )
        pair_values = (harmonics[:, None] * radial[None]).astype(jnp.bfloat16)
        grad_source = jnp.einsum(
            "clki,lkij->cj", weighted, pair_values, preferred_element_type=jnp.float32
        )
        value_grad = jnp.einsum(
            "clki,cj->lkij", weighted, source_feat, preferred_element_type=jnp.float32
        )
        harm_grad = jnp.sum(value_grad * radial[None], axis=1)
        rad_grad = jnp.sum(value_grad * harmonics[:, None], axis=0)
        target_grad, source_grad_pos = pullback((harm_grad, rad_grad))
        grad_tiles = lax.dynamic_update_index_in_dim(grad_tiles, grad_source, tile_index, 0)
        target_grads = lax.dynamic_update_index_in_dim(target_grads, target_grad, tile_index, 0)
        source_grads = lax.dynamic_update_index_in_dim(
            source_grads, source_grad_pos, tile_index, 0
        )
        return (grad_tiles, target_grads, source_grads)

    init = (
        jnp.zeros((tile_count, chan_dev, block_size), jnp.float32),
        jnp.zeros((tile_count, 3, block_size), jnp.float32),
        jnp.zeros((tile_count, 3, block_size), jnp.float32),
    )
    grad_tiles, target_grads, source_grads = lax.fori_loop(0, tile_count, backward_tile, init)
    grad_src = jnp.sum(
        source_hot[:, None, :, None] * grad_tiles[:, :, None, :], axis=0
    ).reshape(chan_dev, src_atoms)
    dpos_src = jnp.sum(
        target_hot[:, None, :, None] * target_grads[:, :, None, :]
        + source_hot[:, None, :, None] * source_grads[:, :, None, :],
        axis=0,
    ).reshape(3, src_atoms)
    for chan_bit in range(lax.axis_size("chan").bit_length() - 1):
        dpos_src = dpos_src + partner(dpos_src, "chan", chan_bit)
    own_both = jnp.concatenate([grad_src[:, :atoms_dev], dpos_src[:, :atoms_dev]], axis=0)
    back_list = []
    for level_bit in range(levels):
        low = atoms_dev + level_bit * block_size
        ghost_both = jnp.concatenate(
            [grad_src[:, low : low + block_size], dpos_src[:, low : low + block_size]], axis=0
        )
        back_both, other_rad = partner((ghost_both, grad_rad), "space", level_bit)
        grad_rad = grad_rad + other_rad
        back_list.append(back_both)
    all_rows = send_rows[:levels].reshape(-1)
    own_both = own_both.at[:, all_rows].add(jnp.concatenate(back_list, axis=1))
    own_grad = own_both[:chan_dev]
    own_dpos = own_both[chan_dev:]
    return (result, own_grad.astype(jnp.bfloat16), -own_dpos, grad_rad)


def solution(mesh):
    placed = (
        P(None, "space"),
        P("chan", "space"),
        P("space", None),
        P("space", None),
        P("space"),
        P("chan", None),
        P(),
        P("chan", None, "space"),
    )
    return jax.shard_map(
        body,
        mesh=mesh,
        in_specs=placed,
        out_specs=(P("chan", None, "space"), P("chan", "space"), P(None, "space"), P("chan", None)),
        check_vma=False,
    )
```

```python
import math

import jax
import jax.numpy as jnp
from jax import lax
from jax.sharding import PartitionSpec as P

SOFTENING = 0.25
CUTOFF = 2.5
CUTOFF_SQ = 6.25
SHARPNESS = 10.0
ROOT_THREE = math.sqrt(3.0)
ORDER_OF = (0, 1, 1, 1, 2, 2, 2, 2, 2)


def partner(value, axis, bit):
    mask = 2**bit
    pairs = [(source, source ^ mask) for source in range(lax.axis_size(axis))]
    return lax.ppermute(value, axis, pairs)


def geometry(target_pos, source_pos, pair_keep, radial_count):
    offset = source_pos[:, :, None, :] - target_pos[:, :, :, None]
    dist_sq = jnp.sum(offset * offset, axis=1) + SOFTENING
    distance = jnp.sqrt(dist_sq)
    along_x = offset[:, 0] / distance
    along_y = offset[:, 1] / distance
    along_z = offset[:, 2] / distance
    harmonics = jnp.stack(
        [
            jnp.ones_like(along_x),
            along_x,
            along_y,
            along_z,
            ROOT_THREE * along_x * along_y,
            ROOT_THREE * along_y * along_z,
            ROOT_THREE * along_x * along_z,
            0.5 * (3.0 * along_z * along_z - 1.0),
            0.5 * ROOT_THREE * (along_x * along_x - along_y * along_y),
        ]
    )
    envelope = jnp.square(jnp.maximum(1.0 - dist_sq / CUTOFF_SQ, 0.0)) * pair_keep
    centers = (jnp.arange(radial_count, dtype=jnp.float32) + 0.5) * (CUTOFF / radial_count)
    radial = (
        jnp.exp(-SHARPNESS * jnp.square(distance[None] - centers[:, None, None, None]))
        * envelope[None]
    )
    return (harmonics, radial)


def take_block(array, blk_index, block_size):
    return lax.dynamic_slice_in_dim(array, blk_index * block_size, block_size, array.ndim - 1)


def add_block(array, blk_index, value, block_size):
    current = take_block(array, blk_index, block_size)
    return lax.dynamic_update_slice_in_dim(
        array, current + value, blk_index * block_size, array.ndim - 1
    )


def body(
    positions, features, send_rows, pair_tiles, tile_live, radial_weight, mix_weight, out_grad
):
    block_size = send_rows.shape[1]
    atoms_dev = positions.shape[1]
    chan_dev = features.shape[0]
    radial_count = radial_weight.shape[1]
    components = out_grad.shape[1]
    levels = lax.axis_size("space").bit_length() - 1
    chan_count = lax.axis_size("chan")
    chan_index = lax.axis_index("chan")
    pos_list = [positions]
    feat_list = [features]
    for level_bit in range(levels):
        sent_rows = send_rows[level_bit]
        got_feat, got_pos = partner(
            (jnp.take(features, sent_rows, axis=1), jnp.take(positions, sent_rows, axis=1)),
            "space",
            level_bit,
        )
        feat_list.append(got_feat)
        pos_list.append(got_pos)
    src_pos = jnp.concatenate(pos_list, axis=1)
    src_feat = jnp.concatenate(feat_list, axis=1)
    full_feat = lax.all_gather(src_feat, "chan", axis=0, tiled=True)
    full_weight = lax.all_gather(radial_weight, "chan", axis=0, tiled=True)
    all_chan = full_feat.shape[0]
    src_atoms = src_pos.shape[1]
    src_blocks = src_atoms // block_size
    own_blocks = atoms_dev // block_size
    tiles_here = pair_tiles.shape[0] // chan_count
    my_tiles = chan_index * tiles_here + jnp.arange(tiles_here, dtype=jnp.int32)
    my_pairs = jnp.take(pair_tiles, my_tiles, axis=0, mode="clip")
    target_idx = my_pairs[:, 0]
    source_idx = my_pairs[:, 1]
    live = jnp.take(tile_live, my_tiles, mode="clip").astype(jnp.float32)
    block_ids = jnp.arange(src_blocks, dtype=jnp.int32)
    target_hot = (target_idx[:, None] == block_ids[None]).astype(jnp.float32) * live[:, None]
    source_hot = (source_idx[:, None] == block_ids[None]).astype(jnp.float32) * live[:, None]
    same = (target_idx == source_idx).astype(jnp.float32)
    eye = jnp.eye(block_size, dtype=jnp.float32)
    pair_keep = live[:, None, None] * (1.0 - same[:, None, None] * eye[None])
    pos_blocks = jnp.moveaxis(src_pos.reshape(3, src_blocks, block_size), 1, 0)
    feat_blocks = jnp.moveaxis(full_feat.reshape(all_chan, src_blocks, block_size), 1, 0)
    target_pos = jnp.take(pos_blocks, target_idx, axis=0, mode="clip")
    source_pos = jnp.take(pos_blocks, source_idx, axis=0, mode="clip")
    source_feat = jnp.take(feat_blocks, source_idx, axis=0, mode="clip")

    def geo_fn(first_pos, second_pos):
        return geometry(first_pos, second_pos, pair_keep, radial_count)

    (harmonics, radial), pullback = jax.vjp(geo_fn, target_pos, source_pos)
    pair_values = (harmonics[:, None] * radial[None]).astype(jnp.bfloat16)
    routed_feat = (
        target_hot[:, :own_blocks, None, None] * source_feat[:, None].astype(jnp.float32)
    ).astype(jnp.bfloat16)
    msg_acc = jnp.einsum(
        "lktij,tbcj->bclki", pair_values, routed_feat, preferred_element_type=jnp.float32
    )
    moment_part = jnp.einsum("bclki,ck->clbi", msg_acc, full_weight).reshape(
        all_chan, components, atoms_dev
    )
    moments = lax.psum_scatter(moment_part, "chan", scatter_dimension=0, tiled=True)
    packed = moments.astype(jnp.bfloat16)
    mixing = jnp.take(mix_weight, jnp.array(ORDER_OF, dtype=jnp.int32), axis=0)
    offset = chan_index * chan_dev
    gathered_piece = lax.all_gather(packed, "chan", axis=0, tiled=True)
    weight_part = lax.dynamic_slice(
        mixing, (0, offset, 0), (components, chan_dev, gathered_piece.shape[0])
    )
    mixed_out = jnp.einsum(
        "lxc,cli->xli", weight_part, gathered_piece, preferred_element_type=jnp.float32
    )
    scalar_part = mixed_out[:, 0, :]
    gate_value = jax.nn.sigmoid(scalar_part)
    result = jnp.concatenate(
        [(scalar_part * gate_value)[:, None, :], mixed_out[:, 1:, :] * gate_value[:, None, :]],
        axis=1,
    ).astype(jnp.bfloat16)
    upstream = out_grad.astype(jnp.float32)
    scalar_grad = upstream[:, 0, :] * (
        gate_value * (1.0 + scalar_part * (1.0 - gate_value))
    ) + gate_value * (1.0 - gate_value) * jnp.sum(upstream[:, 1:, :] * mixed_out[:, 1:, :], axis=1)
    rest_grad = upstream[:, 1:, :] * gate_value[:, None, :]
    dz_packed = jnp.concatenate([scalar_grad[:, None, :], rest_grad], axis=1).astype(jnp.bfloat16)
    gathered_piece = lax.all_gather(dz_packed, "chan", axis=0, tiled=True)
    moment_grad_all = jnp.einsum(
        "lxc,xli->cli", mixing, gathered_piece, preferred_element_type=jnp.float32
    )
    grad_blocks = jnp.moveaxis(
        moment_grad_all.reshape(all_chan, components, own_blocks, block_size), 2, 0
    )
    grad_rad = jnp.einsum("bclki,bcli->ck", msg_acc, grad_blocks)
    tile_grad = jnp.take(grad_blocks, target_idx, axis=0, mode="clip")
    weighted = (
        live[:, None, None, None, None]
        * full_weight[None, :, None, :, None]
        * tile_grad[:, :, :, None, :]
    ).astype(jnp.bfloat16)
    grad_source = jnp.einsum(
        "tclki,lktij->tcj", weighted, pair_values, preferred_element_type=jnp.float32
    )
    value_grad = jnp.einsum(
        "tclki,tcj->lktij", weighted, source_feat, preferred_element_type=jnp.float32
    )
    harm_grad = jnp.sum(value_grad * radial[None], axis=1)
    rad_grad = jnp.sum(value_grad * harmonics[:, None], axis=0)
    target_grad, source_grad_pos = pullback((harm_grad, rad_grad))
    grad_part = jnp.sum(
        source_hot[:, None, :, None] * grad_source[:, :, None, :], axis=0
    ).reshape(all_chan, src_atoms)
    dpos_src = jnp.sum(
        target_hot[:, None, :, None] * target_grad[:, :, None, :]
        + source_hot[:, None, :, None] * source_grad_pos[:, :, None, :],
        axis=0,
    ).reshape(3, src_atoms)
    grad_src = lax.psum_scatter(grad_part, "chan", scatter_dimension=0, tiled=True)
    for chan_bit in range(chan_count.bit_length() - 1):
        other_pos, other_rad = partner((dpos_src, grad_rad), "chan", chan_bit)
        dpos_src = dpos_src + other_pos
        grad_rad = grad_rad + other_rad
    grad_rad = lax.dynamic_slice_in_dim(grad_rad, offset, chan_dev, 0)
    own_both = jnp.concatenate([grad_src[:, :atoms_dev], dpos_src[:, :atoms_dev]], axis=0)
    back_list = []
    for level_bit in range(levels):
        low = atoms_dev + level_bit * block_size
        ghost_both = jnp.concatenate(
            [grad_src[:, low : low + block_size], dpos_src[:, low : low + block_size]], axis=0
        )
        back_both, other_rad = partner((ghost_both, grad_rad), "space", level_bit)
        grad_rad = grad_rad + other_rad
        back_list.append(back_both)
    all_rows = send_rows[:levels].reshape(-1)
    own_both = own_both.at[:, all_rows].add(jnp.concatenate(back_list, axis=1))
    own_grad = own_both[:chan_dev]
    own_dpos = own_both[chan_dev:]
    return (result, own_grad.astype(jnp.bfloat16), -own_dpos, grad_rad)


def solution(mesh):
    placed = (
        P(None, "space"),
        P("chan", "space"),
        P("space", None),
        P("space", None),
        P("space"),
        P("chan", None),
        P(),
        P("chan", None, "space"),
    )
    return jax.shard_map(
        body,
        mesh=mesh,
        in_specs=placed,
        out_specs=(P("chan", None, "space"), P("chan", "space"), P(None, "space"), P("chan", None)),
        check_vma=False,
    )
```

```python
import math

import jax
import jax.numpy as jnp
from jax import lax
from jax.sharding import PartitionSpec as P

SOFTENING = 0.25
CUTOFF = 2.5
CUTOFF_SQ = 6.25
SHARPNESS = 10.0
ROOT_THREE = math.sqrt(3.0)
ORDER_OF = (0, 1, 1, 1, 2, 2, 2, 2, 2)


def partner(value, axis, bit):
    mask = 2**bit
    pairs = [(source, source ^ mask) for source in range(lax.axis_size(axis))]
    return lax.ppermute(value, axis, pairs)


def halving_sum(value, axis):
    index = lax.axis_index(axis)
    for bit in reversed(range(lax.axis_size(axis).bit_length() - 1)):
        half = value.shape[0] // 2
        mine = (index >> bit) & 1
        keep = lax.dynamic_slice_in_dim(value, mine * half, half, 0)
        give = lax.dynamic_slice_in_dim(value, (1 - mine) * half, half, 0)
        value = keep + partner(give, axis, bit)
    return value


def geometry(target_pos, source_pos, pair_keep, radial_count):
    offset = source_pos[:, :, None, :] - target_pos[:, :, :, None]
    dist_sq = jnp.sum(offset * offset, axis=1) + SOFTENING
    distance = jnp.sqrt(dist_sq)
    along_x = offset[:, 0] / distance
    along_y = offset[:, 1] / distance
    along_z = offset[:, 2] / distance
    harmonics = jnp.stack(
        [
            jnp.ones_like(along_x),
            along_x,
            along_y,
            along_z,
            ROOT_THREE * along_x * along_y,
            ROOT_THREE * along_y * along_z,
            ROOT_THREE * along_x * along_z,
            0.5 * (3.0 * along_z * along_z - 1.0),
            0.5 * ROOT_THREE * (along_x * along_x - along_y * along_y),
        ]
    )
    envelope = jnp.square(jnp.maximum(1.0 - dist_sq / CUTOFF_SQ, 0.0)) * pair_keep
    centers = (jnp.arange(radial_count, dtype=jnp.float32) + 0.5) * (CUTOFF / radial_count)
    radial = (
        jnp.exp(-SHARPNESS * jnp.square(distance[None] - centers[:, None, None, None]))
        * envelope[None]
    )
    return (harmonics, radial)


def take_block(array, blk_index, block_size):
    return lax.dynamic_slice_in_dim(array, blk_index * block_size, block_size, array.ndim - 1)


def add_block(array, blk_index, value, block_size):
    current = take_block(array, blk_index, block_size)
    return lax.dynamic_update_slice_in_dim(
        array, current + value, blk_index * block_size, array.ndim - 1
    )


def body(
    positions, features, send_rows, pair_tiles, tile_live, radial_weight, mix_weight, out_grad
):
    block_size = send_rows.shape[1]
    atoms_dev = positions.shape[1]
    chan_dev = features.shape[0]
    radial_count = radial_weight.shape[1]
    components = out_grad.shape[1]
    levels = lax.axis_size("space").bit_length() - 1
    chan_count = lax.axis_size("chan")
    chan_index = lax.axis_index("chan")
    pos_list = [positions]
    feat_list = [features]
    for level_bit in range(levels):
        sent_rows = send_rows[level_bit]
        got_feat, got_pos = partner(
            (jnp.take(features, sent_rows, axis=1), jnp.take(positions, sent_rows, axis=1)),
            "space",
            level_bit,
        )
        feat_list.append(got_feat)
        pos_list.append(got_pos)
    src_pos = jnp.concatenate(pos_list, axis=1)
    src_feat = jnp.concatenate(feat_list, axis=1)
    full_feat = lax.all_gather(src_feat, "chan", axis=0, tiled=True)
    full_weight = lax.all_gather(radial_weight, "chan", axis=0, tiled=True)
    all_chan = full_feat.shape[0]
    src_atoms = src_pos.shape[1]
    src_blocks = src_atoms // block_size
    own_blocks = atoms_dev // block_size
    tiles_here = pair_tiles.shape[0] // chan_count
    my_tiles = chan_index * tiles_here + jnp.arange(tiles_here, dtype=jnp.int32)
    my_pairs = jnp.take(pair_tiles, my_tiles, axis=0, mode="clip")
    target_idx = my_pairs[:, 0]
    source_idx = my_pairs[:, 1]
    live = jnp.take(tile_live, my_tiles, mode="clip").astype(jnp.float32)
    block_ids = jnp.arange(src_blocks, dtype=jnp.int32)
    target_hot = (target_idx[:, None] == block_ids[None]).astype(jnp.float32) * live[:, None]
    source_hot = (source_idx[:, None] == block_ids[None]).astype(jnp.float32) * live[:, None]
    same = (target_idx == source_idx).astype(jnp.float32)
    eye = jnp.eye(block_size, dtype=jnp.float32)
    pair_keep = live[:, None, None] * (1.0 - same[:, None, None] * eye[None])
    pos_blocks = jnp.moveaxis(src_pos.reshape(3, src_blocks, block_size), 1, 0)
    feat_blocks = jnp.moveaxis(full_feat.reshape(all_chan, src_blocks, block_size), 1, 0)
    target_pos = jnp.take(pos_blocks, target_idx, axis=0, mode="clip")
    source_pos = jnp.take(pos_blocks, source_idx, axis=0, mode="clip")
    source_feat = jnp.take(feat_blocks, source_idx, axis=0, mode="clip")

    def geo_fn(first_pos, second_pos):
        return geometry(first_pos, second_pos, pair_keep, radial_count)

    (harmonics, radial), pullback = jax.vjp(geo_fn, target_pos, source_pos)
    pair_values = (harmonics[:, None] * radial[None]).astype(jnp.bfloat16)
    routed_feat = (
        target_hot[:, :own_blocks, None, None] * source_feat[:, None].astype(jnp.float32)
    ).astype(jnp.bfloat16)
    msg_acc = jnp.einsum(
        "lktij,tbcj->bclki", pair_values, routed_feat, preferred_element_type=jnp.float32
    )
    moment_part = jnp.einsum("bclki,ck->clbi", msg_acc, full_weight).reshape(
        all_chan, components, atoms_dev
    )
    moments = halving_sum(moment_part, "chan")
    packed = moments.astype(jnp.bfloat16)
    mixing = jnp.take(mix_weight, jnp.array(ORDER_OF, dtype=jnp.int32), axis=0)
    offset = chan_index * chan_dev
    gathered_piece = lax.all_gather(packed, "chan", axis=0, tiled=True)
    weight_part = lax.dynamic_slice(
        mixing, (0, offset, 0), (components, chan_dev, gathered_piece.shape[0])
    )
    mixed_out = jnp.einsum(
        "lxc,cli->xli", weight_part, gathered_piece, preferred_element_type=jnp.float32
    )
    scalar_part = mixed_out[:, 0, :]
    gate_value = jax.nn.sigmoid(scalar_part)
    result = jnp.concatenate(
        [(scalar_part * gate_value)[:, None, :], mixed_out[:, 1:, :] * gate_value[:, None, :]],
        axis=1,
    ).astype(jnp.bfloat16)
    upstream = out_grad.astype(jnp.float32)
    scalar_grad = upstream[:, 0, :] * (
        gate_value * (1.0 + scalar_part * (1.0 - gate_value))
    ) + gate_value * (1.0 - gate_value) * jnp.sum(upstream[:, 1:, :] * mixed_out[:, 1:, :], axis=1)
    rest_grad = upstream[:, 1:, :] * gate_value[:, None, :]
    dz_packed = jnp.concatenate([scalar_grad[:, None, :], rest_grad], axis=1).astype(jnp.bfloat16)
    gathered_piece = lax.all_gather(dz_packed, "chan", axis=0, tiled=True)
    moment_grad_all = jnp.einsum(
        "lxc,xli->cli", mixing, gathered_piece, preferred_element_type=jnp.float32
    )
    grad_blocks = jnp.moveaxis(
        moment_grad_all.reshape(all_chan, components, own_blocks, block_size), 2, 0
    )
    grad_rad = jnp.einsum("bclki,bcli->ck", msg_acc, grad_blocks)
    tile_grad = jnp.take(grad_blocks, target_idx, axis=0, mode="clip")
    weighted = (
        live[:, None, None, None, None]
        * full_weight[None, :, None, :, None]
        * tile_grad[:, :, :, None, :]
    ).astype(jnp.bfloat16)
    grad_source = jnp.einsum(
        "tclki,lktij->tcj", weighted, pair_values, preferred_element_type=jnp.float32
    )
    value_grad = jnp.einsum(
        "tclki,tcj->lktij", weighted, source_feat, preferred_element_type=jnp.float32
    )
    harm_grad = jnp.sum(value_grad * radial[None], axis=1)
    rad_grad = jnp.sum(value_grad * harmonics[:, None], axis=0)
    target_grad, source_grad_pos = pullback((harm_grad, rad_grad))
    grad_part = jnp.sum(
        source_hot[:, None, :, None] * grad_source[:, :, None, :], axis=0
    ).reshape(all_chan, src_atoms)
    dpos_src = jnp.sum(
        target_hot[:, None, :, None] * target_grad[:, :, None, :]
        + source_hot[:, None, :, None] * source_grad_pos[:, :, None, :],
        axis=0,
    ).reshape(3, src_atoms)
    grad_src = lax.psum_scatter(grad_part, "chan", scatter_dimension=0, tiled=True)
    for chan_bit in range(chan_count.bit_length() - 1):
        other_pos, other_rad = partner((dpos_src, grad_rad), "chan", chan_bit)
        dpos_src = dpos_src + other_pos
        grad_rad = grad_rad + other_rad
    grad_rad = lax.dynamic_slice_in_dim(grad_rad, offset, chan_dev, 0)
    own_both = jnp.concatenate([grad_src[:, :atoms_dev], dpos_src[:, :atoms_dev]], axis=0)
    back_list = []
    for level_bit in range(levels):
        low = atoms_dev + level_bit * block_size
        ghost_both = jnp.concatenate(
            [grad_src[:, low : low + block_size], dpos_src[:, low : low + block_size]], axis=0
        )
        back_both, other_rad = partner((ghost_both, grad_rad), "space", level_bit)
        grad_rad = grad_rad + other_rad
        back_list.append(back_both)
    all_rows = send_rows[:levels].reshape(-1)
    own_both = own_both.at[:, all_rows].add(jnp.concatenate(back_list, axis=1))
    own_grad = own_both[:chan_dev]
    own_dpos = own_both[chan_dev:]
    return (result, own_grad.astype(jnp.bfloat16), -own_dpos, grad_rad)


def solution(mesh):
    placed = (
        P(None, "space"),
        P("chan", "space"),
        P("space", None),
        P("space", None),
        P("space"),
        P("chan", None),
        P(),
        P("chan", None, "space"),
    )
    return jax.shard_map(
        body,
        mesh=mesh,
        in_specs=placed,
        out_specs=(P("chan", None, "space"), P("chan", "space"), P(None, "space"), P("chan", None)),
        check_vma=False,
    )
```

```python
import math

import jax
import jax.numpy as jnp
from jax import lax
from jax.sharding import PartitionSpec as P

SOFTENING = 0.25
CUTOFF = 2.5
CUTOFF_SQ = 6.25
SHARPNESS = 10.0
ROOT_THREE = math.sqrt(3.0)
ORDER_OF = (0, 1, 1, 1, 2, 2, 2, 2, 2)


def partner(value, axis, bit):
    mask = 2**bit
    pairs = [(source, source ^ mask) for source in range(lax.axis_size(axis))]
    return lax.ppermute(value, axis, pairs)


def halving_sum(value, axis):
    index = lax.axis_index(axis)
    for bit in reversed(range(lax.axis_size(axis).bit_length() - 1)):
        half = value.shape[0] // 2
        mine = (index >> bit) & 1
        keep = lax.dynamic_slice_in_dim(value, mine * half, half, 0)
        give = lax.dynamic_slice_in_dim(value, (1 - mine) * half, half, 0)
        value = keep + partner(give, axis, bit)
    return value


def geometry(target_pos, source_pos, pair_keep, radial_count):
    offset = source_pos[:, :, None, :] - target_pos[:, :, :, None]
    dist_sq = jnp.sum(offset * offset, axis=1) + SOFTENING
    distance = jnp.sqrt(dist_sq)
    along_x = offset[:, 0] / distance
    along_y = offset[:, 1] / distance
    along_z = offset[:, 2] / distance
    harmonics = jnp.stack(
        [
            jnp.ones_like(along_x),
            along_x,
            along_y,
            along_z,
            ROOT_THREE * along_x * along_y,
            ROOT_THREE * along_y * along_z,
            ROOT_THREE * along_x * along_z,
            0.5 * (3.0 * along_z * along_z - 1.0),
            0.5 * ROOT_THREE * (along_x * along_x - along_y * along_y),
        ]
    )
    envelope = jnp.square(jnp.maximum(1.0 - dist_sq / CUTOFF_SQ, 0.0)) * pair_keep
    centers = (jnp.arange(radial_count, dtype=jnp.float32) + 0.5) * (CUTOFF / radial_count)
    radial = (
        jnp.exp(-SHARPNESS * jnp.square(distance[None] - centers[:, None, None, None]))
        * envelope[None]
    )
    return (harmonics, radial)


def take_block(array, blk_index, block_size):
    return lax.dynamic_slice_in_dim(array, blk_index * block_size, block_size, array.ndim - 1)


def add_block(array, blk_index, value, block_size):
    current = take_block(array, blk_index, block_size)
    return lax.dynamic_update_slice_in_dim(
        array, current + value, blk_index * block_size, array.ndim - 1
    )


def body(
    positions, features, send_rows, pair_tiles, tile_live, radial_weight, mix_weight, out_grad
):
    block_size = send_rows.shape[1]
    atoms_dev = positions.shape[1]
    chan_dev = features.shape[0]
    radial_count = radial_weight.shape[1]
    components = out_grad.shape[1]
    levels = lax.axis_size("space").bit_length() - 1
    chan_count = lax.axis_size("chan")
    chan_index = lax.axis_index("chan")
    pos_list = [positions]
    feat_list = [features]
    for level_bit in range(levels):
        sent_rows = send_rows[level_bit]
        got_feat, got_pos = partner(
            (jnp.take(features, sent_rows, axis=1), jnp.take(positions, sent_rows, axis=1)),
            "space",
            level_bit,
        )
        feat_list.append(got_feat)
        pos_list.append(got_pos)
    src_pos = jnp.concatenate(pos_list, axis=1)
    src_feat = jnp.concatenate(feat_list, axis=1)
    full_feat = lax.all_gather(src_feat, "chan", axis=0, tiled=True)
    full_weight = lax.all_gather(radial_weight, "chan", axis=0, tiled=True)
    all_chan = full_feat.shape[0]
    src_atoms = src_pos.shape[1]
    src_blocks = src_atoms // block_size
    own_blocks = atoms_dev // block_size
    rows = block_size // chan_count
    row_low = chan_index * rows
    target_idx = pair_tiles[:, 0]
    source_idx = pair_tiles[:, 1]
    live = tile_live.astype(jnp.float32)
    block_ids = jnp.arange(src_blocks, dtype=jnp.int32)
    target_hot = (target_idx[:, None] == block_ids[None]).astype(jnp.float32) * live[:, None]
    source_hot = (source_idx[:, None] == block_ids[None]).astype(jnp.float32) * live[:, None]
    same = (target_idx == source_idx).astype(jnp.float32)
    eye = (
        (row_low + jnp.arange(rows, dtype=jnp.int32))[:, None]
        == jnp.arange(block_size, dtype=jnp.int32)[None]
    ).astype(jnp.float32)
    pair_keep = live[:, None, None] * (1.0 - same[:, None, None] * eye[None])
    pos_blocks = jnp.moveaxis(src_pos.reshape(3, src_blocks, block_size), 1, 0)
    pos_rows = lax.dynamic_slice_in_dim(pos_blocks, row_low, rows, 2)
    feat_blocks = jnp.moveaxis(full_feat.reshape(all_chan, src_blocks, block_size), 1, 0)
    target_pos = jnp.take(pos_rows, target_idx, axis=0, mode="clip")
    source_pos = jnp.take(pos_blocks, source_idx, axis=0, mode="clip")
    source_feat = jnp.take(feat_blocks, source_idx, axis=0, mode="clip")

    def geo_fn(first_pos, second_pos):
        return geometry(first_pos, second_pos, pair_keep, radial_count)

    (harmonics, radial), pullback = jax.vjp(geo_fn, target_pos, source_pos)
    pair_values = (harmonics[:, None] * radial[None]).astype(jnp.bfloat16)
    routed_feat = (
        target_hot[:, :own_blocks, None, None] * source_feat[:, None].astype(jnp.float32)
    ).astype(jnp.bfloat16)
    msg_acc = jnp.einsum(
        "lktij,tbcj->bclki", pair_values, routed_feat, preferred_element_type=jnp.float32
    )
    moments = jnp.einsum("bclki,ck->clbi", msg_acc, full_weight)
    packed = moments.astype(jnp.bfloat16)
    mixing = jnp.take(mix_weight, jnp.array(ORDER_OF, dtype=jnp.int32), axis=0)
    offset = chan_index * chan_dev
    mixed_out = jnp.einsum(
        "lxc,clbi->xlbi", mixing, packed, preferred_element_type=jnp.float32
    )
    scalar_part = mixed_out[:, 0]
    gate_value = jax.nn.sigmoid(scalar_part)
    result_rows = jnp.concatenate(
        [(scalar_part * gate_value)[:, None], mixed_out[:, 1:] * gate_value[:, None]],
        axis=1,
    ).astype(jnp.bfloat16)
    result = lax.all_to_all(
        result_rows.reshape(all_chan, components, own_blocks, 1, rows),
        "chan",
        0,
        3,
        tiled=True,
    ).reshape(chan_dev, components, atoms_dev)
    grad_rows = lax.all_to_all(
        out_grad.reshape(chan_dev, components, own_blocks, chan_count, rows),
        "chan",
        3,
        0,
        tiled=True,
    ).reshape(all_chan, components, own_blocks, rows)
    upstream = grad_rows.astype(jnp.float32)
    scalar_grad = upstream[:, 0] * (
        gate_value * (1.0 + scalar_part * (1.0 - gate_value))
    ) + gate_value * (1.0 - gate_value) * jnp.sum(upstream[:, 1:] * mixed_out[:, 1:], axis=1)
    rest_grad = upstream[:, 1:] * gate_value[:, None]
    dz_packed = jnp.concatenate([scalar_grad[:, None], rest_grad], axis=1).astype(jnp.bfloat16)
    moment_grad_all = jnp.einsum(
        "lxc,xlbi->clbi", mixing, dz_packed, preferred_element_type=jnp.float32
    )
    grad_rad = jnp.einsum("bclki,clbi->ck", msg_acc, moment_grad_all)
    grad_blocks = jnp.moveaxis(moment_grad_all, 2, 0)
    tile_grad = jnp.take(grad_blocks, target_idx, axis=0, mode="clip")
    weighted = (
        live[:, None, None, None, None]
        * full_weight[None, :, None, :, None]
        * tile_grad[:, :, :, None, :]
    ).astype(jnp.bfloat16)
    grad_source = jnp.einsum(
        "tclki,lktij->tcj", weighted, pair_values, preferred_element_type=jnp.float32
    )
    value_grad = jnp.einsum(
        "tclki,tcj->lktij", weighted, source_feat, preferred_element_type=jnp.float32
    )
    harm_grad = jnp.sum(value_grad * radial[None], axis=1)
    rad_grad = jnp.sum(value_grad * harmonics[:, None], axis=0)
    target_grad, source_grad_pos = pullback((harm_grad, rad_grad))
    grad_part = jnp.sum(
        source_hot[:, None, :, None] * grad_source[:, :, None, :], axis=0
    ).reshape(all_chan, src_atoms)
    row_hot = (jnp.arange(chan_count, dtype=jnp.int32) == chan_index).astype(jnp.float32)
    target_part = jnp.sum(target_hot[:, None, :, None] * target_grad[:, :, None, :], axis=0)
    dpos_src = (
        row_hot[None, None, :, None] * target_part[:, :, None, :]
        + jnp.sum(source_hot[:, None, :, None] * source_grad_pos[:, :, None, :], axis=0).reshape(
            3, src_blocks, chan_count, rows
        )
    ).reshape(3, src_atoms)
    grad_src = lax.psum_scatter(grad_part, "chan", scatter_dimension=0, tiled=True)
    for chan_bit in range(chan_count.bit_length() - 1):
        other_pos, other_rad = partner((dpos_src, grad_rad), "chan", chan_bit)
        dpos_src = dpos_src + other_pos
        grad_rad = grad_rad + other_rad
    grad_rad = lax.dynamic_slice_in_dim(grad_rad, offset, chan_dev, 0)
    own_both = jnp.concatenate([grad_src[:, :atoms_dev], dpos_src[:, :atoms_dev]], axis=0)
    back_list = []
    for level_bit in range(levels):
        low = atoms_dev + level_bit * block_size
        ghost_both = jnp.concatenate(
            [grad_src[:, low : low + block_size], dpos_src[:, low : low + block_size]], axis=0
        )
        back_both, other_rad = partner((ghost_both, grad_rad), "space", level_bit)
        grad_rad = grad_rad + other_rad
        back_list.append(back_both)
    all_rows = send_rows[:levels].reshape(-1)
    own_both = own_both.at[:, all_rows].add(jnp.concatenate(back_list, axis=1))
    own_grad = own_both[:chan_dev]
    own_dpos = own_both[chan_dev:]
    return (result, own_grad.astype(jnp.bfloat16), -own_dpos, grad_rad)


def solution(mesh):
    placed = (
        P(None, "space"),
        P("chan", "space"),
        P("space", None),
        P("space", None),
        P("space"),
        P("chan", None),
        P(),
        P("chan", None, "space"),
    )
    return jax.shard_map(
        body,
        mesh=mesh,
        in_specs=placed,
        out_specs=(P("chan", None, "space"), P("chan", "space"), P(None, "space"), P("chan", None)),
        check_vma=False,
    )
```

```python
import math

import jax
import jax.numpy as jnp
from jax import lax
from jax.sharding import PartitionSpec as P

SOFTENING = 0.25
CUTOFF = 2.5
CUTOFF_SQ = 6.25
SHARPNESS = 10.0
ROOT_THREE = math.sqrt(3.0)
ORDER_OF = (0, 1, 1, 1, 2, 2, 2, 2, 2)


def partner(value, axis, bit):
    mask = 2**bit
    pairs = [(source, source ^ mask) for source in range(lax.axis_size(axis))]
    return lax.ppermute(value, axis, pairs)


def halving_sum(value, axis):
    index = lax.axis_index(axis)
    for bit in reversed(range(lax.axis_size(axis).bit_length() - 1)):
        half = value.shape[0] // 2
        mine = (index >> bit) & 1
        keep = lax.dynamic_slice_in_dim(value, mine * half, half, 0)
        give = lax.dynamic_slice_in_dim(value, (1 - mine) * half, half, 0)
        value = keep + partner(give, axis, bit)
    return value


def geometry(target_pos, source_pos, pair_keep, radial_count):
    offset = source_pos[:, :, None, :] - target_pos[:, :, :, None]
    dist_sq = jnp.sum(offset * offset, axis=1) + SOFTENING
    distance = jnp.sqrt(dist_sq)
    along_x = offset[:, 0] / distance
    along_y = offset[:, 1] / distance
    along_z = offset[:, 2] / distance
    harmonics = jnp.stack(
        [
            jnp.ones_like(along_x),
            along_x,
            along_y,
            along_z,
            ROOT_THREE * along_x * along_y,
            ROOT_THREE * along_y * along_z,
            ROOT_THREE * along_x * along_z,
            0.5 * (3.0 * along_z * along_z - 1.0),
            0.5 * ROOT_THREE * (along_x * along_x - along_y * along_y),
        ]
    )
    envelope = jnp.square(jnp.maximum(1.0 - dist_sq / CUTOFF_SQ, 0.0)) * pair_keep
    centers = (jnp.arange(radial_count, dtype=jnp.float32) + 0.5) * (CUTOFF / radial_count)
    radial = (
        jnp.exp(-SHARPNESS * jnp.square(distance[None] - centers[:, None, None, None]))
        * envelope[None]
    )
    return (harmonics, radial)


def take_block(array, blk_index, block_size):
    return lax.dynamic_slice_in_dim(array, blk_index * block_size, block_size, array.ndim - 1)


def add_block(array, blk_index, value, block_size):
    current = take_block(array, blk_index, block_size)
    return lax.dynamic_update_slice_in_dim(
        array, current + value, blk_index * block_size, array.ndim - 1
    )


def body(
    positions, features, send_rows, pair_tiles, tile_live, radial_weight, mix_weight, out_grad
):
    block_size = send_rows.shape[1]
    atoms_dev = positions.shape[1]
    chan_dev = features.shape[0]
    radial_count = radial_weight.shape[1]
    components = out_grad.shape[1]
    levels = lax.axis_size("space").bit_length() - 1
    chan_count = lax.axis_size("chan")
    chan_index = lax.axis_index("chan")
    pos_list = [positions]
    feat_list = [features]
    for level_bit in range(levels):
        sent_rows = send_rows[level_bit]
        got_feat, got_pos = partner(
            (jnp.take(features, sent_rows, axis=1), jnp.take(positions, sent_rows, axis=1)),
            "space",
            level_bit,
        )
        feat_list.append(got_feat)
        pos_list.append(got_pos)
    src_pos = jnp.concatenate(pos_list, axis=1)
    src_feat = jnp.concatenate(feat_list, axis=1)
    src_atoms = src_pos.shape[1]
    weight_high = radial_weight.astype(jnp.bfloat16)
    weight_rest = radial_weight - weight_high.astype(jnp.float32)
    weight_mid = weight_rest.astype(jnp.bfloat16)
    weight_low = (weight_rest - weight_mid.astype(jnp.float32)).astype(jnp.bfloat16)
    full_both = lax.all_gather(
        jnp.concatenate([src_feat, weight_high, weight_mid, weight_low], axis=1),
        "chan",
        axis=0,
        tiled=True,
    )
    full_feat = full_both[:, :src_atoms]
    pieces = full_both[:, src_atoms:].astype(jnp.float32)
    full_weight = (
        pieces[:, :radial_count] + pieces[:, radial_count : 2 * radial_count]
    ) + pieces[:, 2 * radial_count :]
    all_chan = full_feat.shape[0]
    src_blocks = src_atoms // block_size
    own_blocks = atoms_dev // block_size
    rows = block_size // chan_count
    row_low = chan_index * rows
    target_idx = pair_tiles[:, 0]
    source_idx = pair_tiles[:, 1]
    live = tile_live.astype(jnp.float32)
    block_ids = jnp.arange(src_blocks, dtype=jnp.int32)
    target_hot = (target_idx[:, None] == block_ids[None]).astype(jnp.float32) * live[:, None]
    source_hot = (source_idx[:, None] == block_ids[None]).astype(jnp.float32) * live[:, None]
    same = (target_idx == source_idx).astype(jnp.float32)
    eye = (
        (row_low + jnp.arange(rows, dtype=jnp.int32))[:, None]
        == jnp.arange(block_size, dtype=jnp.int32)[None]
    ).astype(jnp.float32)
    pair_keep = live[:, None, None] * (1.0 - same[:, None, None] * eye[None])
    pos_blocks = jnp.moveaxis(src_pos.reshape(3, src_blocks, block_size), 1, 0)
    pos_rows = lax.dynamic_slice_in_dim(pos_blocks, row_low, rows, 2)
    feat_blocks = jnp.moveaxis(full_feat.reshape(all_chan, src_blocks, block_size), 1, 0)
    target_pos = jnp.take(pos_rows, target_idx, axis=0, mode="clip")
    source_pos = jnp.take(pos_blocks, source_idx, axis=0, mode="clip")
    source_feat = jnp.take(feat_blocks, source_idx, axis=0, mode="clip")

    def geo_fn(first_pos, second_pos):
        return geometry(first_pos, second_pos, pair_keep, radial_count)

    (harmonics, radial), pullback = jax.vjp(geo_fn, target_pos, source_pos)
    pair_values = (harmonics[:, None] * radial[None]).astype(jnp.bfloat16)
    routed_feat = (
        target_hot[:, :own_blocks, None, None] * source_feat[:, None].astype(jnp.float32)
    ).astype(jnp.bfloat16)
    msg_acc = jnp.einsum(
        "lktij,tbcj->bclki", pair_values, routed_feat, preferred_element_type=jnp.float32
    )
    moments = jnp.einsum("bclki,ck->clbi", msg_acc, full_weight)
    packed = moments.astype(jnp.bfloat16)
    mixing = jnp.take(mix_weight, jnp.array(ORDER_OF, dtype=jnp.int32), axis=0)
    offset = chan_index * chan_dev
    mixed_out = jnp.einsum(
        "lxc,clbi->xlbi", mixing, packed, preferred_element_type=jnp.float32
    )
    scalar_part = mixed_out[:, 0]
    gate_value = jax.nn.sigmoid(scalar_part)
    result_rows = jnp.concatenate(
        [(scalar_part * gate_value)[:, None], mixed_out[:, 1:] * gate_value[:, None]],
        axis=1,
    ).astype(jnp.bfloat16)
    result = lax.all_to_all(
        result_rows.reshape(all_chan, components, own_blocks, 1, rows),
        "chan",
        0,
        3,
        tiled=True,
    ).reshape(chan_dev, components, atoms_dev)
    grad_rows = lax.all_to_all(
        out_grad.reshape(chan_dev, components, own_blocks, chan_count, rows),
        "chan",
        3,
        0,
        tiled=True,
    ).reshape(all_chan, components, own_blocks, rows)
    upstream = grad_rows.astype(jnp.float32)
    scalar_grad = upstream[:, 0] * (
        gate_value * (1.0 + scalar_part * (1.0 - gate_value))
    ) + gate_value * (1.0 - gate_value) * jnp.sum(upstream[:, 1:] * mixed_out[:, 1:], axis=1)
    rest_grad = upstream[:, 1:] * gate_value[:, None]
    dz_packed = jnp.concatenate([scalar_grad[:, None], rest_grad], axis=1).astype(jnp.bfloat16)
    moment_grad_all = jnp.einsum(
        "lxc,xlbi->clbi", mixing, dz_packed, preferred_element_type=jnp.float32
    )
    grad_rad = jnp.einsum("bclki,clbi->ck", msg_acc, moment_grad_all)
    grad_blocks = jnp.moveaxis(moment_grad_all, 2, 0)
    tile_grad = jnp.take(grad_blocks, target_idx, axis=0, mode="clip")
    weighted = (
        live[:, None, None, None, None]
        * full_weight[None, :, None, :, None]
        * tile_grad[:, :, :, None, :]
    ).astype(jnp.bfloat16)
    grad_source = jnp.einsum(
        "tclki,lktij->tcj", weighted, pair_values, preferred_element_type=jnp.float32
    )
    value_grad = jnp.einsum(
        "tclki,tcj->lktij", weighted, source_feat, preferred_element_type=jnp.float32
    )
    harm_grad = jnp.sum(value_grad * radial[None], axis=1)
    rad_grad = jnp.sum(value_grad * harmonics[:, None], axis=0)
    target_grad, source_grad_pos = pullback((harm_grad, rad_grad))
    grad_part = jnp.sum(
        source_hot[:, None, :, None] * grad_source[:, :, None, :], axis=0
    ).reshape(all_chan, src_atoms)
    row_hot = (jnp.arange(chan_count, dtype=jnp.int32) == chan_index).astype(jnp.float32)
    target_part = jnp.sum(target_hot[:, None, :, None] * target_grad[:, :, None, :], axis=0)
    dpos_src = (
        row_hot[None, None, :, None] * target_part[:, :, None, :]
        + jnp.sum(source_hot[:, None, :, None] * source_grad_pos[:, :, None, :], axis=0).reshape(
            3, src_blocks, chan_count, rows
        )
    ).reshape(3, src_atoms)
    grad_src = lax.psum_scatter(grad_part, "chan", scatter_dimension=0, tiled=True)
    for chan_bit in range(chan_count.bit_length() - 1):
        other_pos, other_rad = partner((dpos_src, grad_rad), "chan", chan_bit)
        dpos_src = dpos_src + other_pos
        grad_rad = grad_rad + other_rad
    grad_rad = lax.dynamic_slice_in_dim(grad_rad, offset, chan_dev, 0)
    own_both = jnp.concatenate([grad_src[:, :atoms_dev], dpos_src[:, :atoms_dev]], axis=0)
    back_list = []
    for level_bit in range(levels):
        low = atoms_dev + level_bit * block_size
        ghost_both = jnp.concatenate(
            [grad_src[:, low : low + block_size], dpos_src[:, low : low + block_size]], axis=0
        )
        back_both, other_rad = partner((ghost_both, grad_rad), "space", level_bit)
        grad_rad = grad_rad + other_rad
        back_list.append(back_both)
    all_rows = send_rows[:levels].reshape(-1)
    own_both = own_both.at[:, all_rows].add(jnp.concatenate(back_list, axis=1))
    own_grad = own_both[:chan_dev]
    own_dpos = own_both[chan_dev:]
    return (result, own_grad.astype(jnp.bfloat16), -own_dpos, grad_rad)


def solution(mesh):
    placed = (
        P(None, "space"),
        P("chan", "space"),
        P("space", None),
        P("space", None),
        P("space"),
        P("chan", None),
        P(),
        P("chan", None, "space"),
    )
    return jax.shard_map(
        body,
        mesh=mesh,
        in_specs=placed,
        out_specs=(P("chan", None, "space"), P("chan", "space"), P(None, "space"), P("chan", None)),
        check_vma=False,
    )
```

```python
import math

import jax
import jax.numpy as jnp
from jax import lax
from jax.sharding import PartitionSpec as P

SOFTENING = 0.25
CUTOFF = 2.5
CUTOFF_SQ = 6.25
SHARPNESS = 10.0
ROOT_THREE = math.sqrt(3.0)
ORDER_OF = (0, 1, 1, 1, 2, 2, 2, 2, 2)


def partner(value, axis, bit):
    mask = 2**bit
    pairs = [(source, source ^ mask) for source in range(lax.axis_size(axis))]
    return lax.ppermute(value, axis, pairs)


def halving_sum(value, axis):
    index = lax.axis_index(axis)
    for bit in reversed(range(lax.axis_size(axis).bit_length() - 1)):
        half = value.shape[0] // 2
        mine = (index >> bit) & 1
        keep = lax.dynamic_slice_in_dim(value, mine * half, half, 0)
        give = lax.dynamic_slice_in_dim(value, (1 - mine) * half, half, 0)
        value = keep + partner(give, axis, bit)
    return value


def geometry(target_pos, source_pos, pair_keep, radial_count):
    offset = source_pos[:, :, None, :] - target_pos[:, :, :, None]
    dist_sq = jnp.sum(offset * offset, axis=1) + SOFTENING
    distance = jnp.sqrt(dist_sq)
    along_x = offset[:, 0] / distance
    along_y = offset[:, 1] / distance
    along_z = offset[:, 2] / distance
    harmonics = jnp.stack(
        [
            jnp.ones_like(along_x),
            along_x,
            along_y,
            along_z,
            ROOT_THREE * along_x * along_y,
            ROOT_THREE * along_y * along_z,
            ROOT_THREE * along_x * along_z,
            0.5 * (3.0 * along_z * along_z - 1.0),
            0.5 * ROOT_THREE * (along_x * along_x - along_y * along_y),
        ]
    )
    envelope = jnp.square(jnp.maximum(1.0 - dist_sq / CUTOFF_SQ, 0.0)) * pair_keep
    centers = (jnp.arange(radial_count, dtype=jnp.float32) + 0.5) * (CUTOFF / radial_count)
    radial = (
        jnp.exp(-SHARPNESS * jnp.square(distance[None] - centers[:, None, None, None]))
        * envelope[None]
    )
    return (harmonics, radial)


def take_block(array, blk_index, block_size):
    return lax.dynamic_slice_in_dim(array, blk_index * block_size, block_size, array.ndim - 1)


def add_block(array, blk_index, value, block_size):
    current = take_block(array, blk_index, block_size)
    return lax.dynamic_update_slice_in_dim(
        array, current + value, blk_index * block_size, array.ndim - 1
    )


def body(
    positions, features, send_rows, pair_tiles, tile_live, radial_weight, mix_weight, out_grad
):
    block_size = send_rows.shape[1]
    atoms_dev = positions.shape[1]
    chan_dev = features.shape[0]
    radial_count = radial_weight.shape[1]
    components = out_grad.shape[1]
    levels = lax.axis_size("space").bit_length() - 1
    chan_count = lax.axis_size("chan")
    chan_index = lax.axis_index("chan")
    pos_list = [positions]
    feat_list = [features]
    both_rows = jnp.take(
        jnp.concatenate([features.astype(jnp.float32), positions], axis=0),
        send_rows[:levels].reshape(-1),
        axis=1,
        mode="clip",
    )
    for level_bit in range(levels):
        got_both = partner(
            both_rows[:, level_bit * block_size : (level_bit + 1) * block_size],
            "space",
            level_bit,
        )
        feat_list.append(got_both[:chan_dev].astype(jnp.bfloat16))
        pos_list.append(got_both[chan_dev:])
    src_pos = jnp.concatenate(pos_list, axis=1)
    src_feat = jnp.concatenate(feat_list, axis=1)
    src_atoms = src_pos.shape[1]
    weight_high = radial_weight.astype(jnp.bfloat16)
    weight_rest = radial_weight - weight_high.astype(jnp.float32)
    weight_mid = weight_rest.astype(jnp.bfloat16)
    weight_low = (weight_rest - weight_mid.astype(jnp.float32)).astype(jnp.bfloat16)
    full_both = lax.all_gather(
        jnp.concatenate([src_feat, weight_high, weight_mid, weight_low], axis=1),
        "chan",
        axis=0,
        tiled=True,
    )
    full_feat = full_both[:, :src_atoms]
    pieces = full_both[:, src_atoms:].astype(jnp.float32)
    full_weight = (
        pieces[:, :radial_count] + pieces[:, radial_count : 2 * radial_count]
    ) + pieces[:, 2 * radial_count :]
    all_chan = full_feat.shape[0]
    src_blocks = src_atoms // block_size
    own_blocks = atoms_dev // block_size
    rows = block_size // chan_count
    row_low = chan_index * rows
    target_idx = pair_tiles[:, 0]
    source_idx = pair_tiles[:, 1]
    live = tile_live.astype(jnp.float32)
    block_ids = jnp.arange(src_blocks, dtype=jnp.int32)
    target_hot = (target_idx[:, None] == block_ids[None]).astype(jnp.float32) * live[:, None]
    source_hot = (source_idx[:, None] == block_ids[None]).astype(jnp.float32) * live[:, None]
    same = (target_idx == source_idx).astype(jnp.float32)
    eye = (
        (row_low + jnp.arange(rows, dtype=jnp.int32))[:, None]
        == jnp.arange(block_size, dtype=jnp.int32)[None]
    ).astype(jnp.float32)
    pair_keep = live[:, None, None] * (1.0 - same[:, None, None] * eye[None])
    pos_blocks = jnp.moveaxis(src_pos.reshape(3, src_blocks, block_size), 1, 0)
    pos_rows = lax.dynamic_slice_in_dim(pos_blocks, row_low, rows, 2)
    feat_blocks = jnp.moveaxis(full_feat.reshape(all_chan, src_blocks, block_size), 1, 0)
    target_pos = jnp.take(pos_rows, target_idx, axis=0, mode="clip")
    source_pos = jnp.take(pos_blocks, source_idx, axis=0, mode="clip")
    source_feat = jnp.take(feat_blocks, source_idx, axis=0, mode="clip")

    def geo_fn(first_pos, second_pos):
        return geometry(first_pos, second_pos, pair_keep, radial_count)

    (harmonics, radial), pullback = jax.vjp(geo_fn, target_pos, source_pos)
    pair_values = (harmonics[:, None] * radial[None]).astype(jnp.bfloat16)
    routed_feat = (
        target_hot[:, :own_blocks, None, None] * source_feat[:, None].astype(jnp.float32)
    ).astype(jnp.bfloat16)
    msg_acc = jnp.einsum(
        "lktij,tbcj->bclki", pair_values, routed_feat, preferred_element_type=jnp.float32
    )
    moments = jnp.einsum("bclki,ck->clbi", msg_acc, full_weight)
    packed = moments.astype(jnp.bfloat16)
    mixing = jnp.take(mix_weight, jnp.array(ORDER_OF, dtype=jnp.int32), axis=0)
    offset = chan_index * chan_dev
    mixed_out = jnp.einsum(
        "lxc,clbi->xlbi", mixing, packed, preferred_element_type=jnp.float32
    )
    scalar_part = mixed_out[:, 0]
    gate_value = jax.nn.sigmoid(scalar_part)
    result_rows = jnp.concatenate(
        [(scalar_part * gate_value)[:, None], mixed_out[:, 1:] * gate_value[:, None]],
        axis=1,
    ).astype(jnp.bfloat16)
    result = lax.all_to_all(
        result_rows.reshape(all_chan, components, own_blocks, 1, rows),
        "chan",
        0,
        3,
        tiled=True,
    ).reshape(chan_dev, components, atoms_dev)
    grad_rows = lax.all_to_all(
        out_grad.reshape(chan_dev, components, own_blocks, chan_count, rows),
        "chan",
        3,
        0,
        tiled=True,
    ).reshape(all_chan, components, own_blocks, rows)
    upstream = grad_rows.astype(jnp.float32)
    scalar_grad = upstream[:, 0] * (
        gate_value * (1.0 + scalar_part * (1.0 - gate_value))
    ) + gate_value * (1.0 - gate_value) * jnp.sum(upstream[:, 1:] * mixed_out[:, 1:], axis=1)
    rest_grad = upstream[:, 1:] * gate_value[:, None]
    dz_packed = jnp.concatenate([scalar_grad[:, None], rest_grad], axis=1).astype(jnp.bfloat16)
    moment_grad_all = jnp.einsum(
        "lxc,xlbi->clbi", mixing, dz_packed, preferred_element_type=jnp.float32
    )
    grad_rad = jnp.einsum("bclki,clbi->ck", msg_acc, moment_grad_all)
    grad_blocks = jnp.moveaxis(moment_grad_all, 2, 0)
    tile_grad = jnp.take(grad_blocks, target_idx, axis=0, mode="clip")
    weighted = (
        live[:, None, None, None, None]
        * full_weight[None, :, None, :, None]
        * tile_grad[:, :, :, None, :]
    ).astype(jnp.bfloat16)
    grad_source = jnp.einsum(
        "tclki,lktij->tcj", weighted, pair_values, preferred_element_type=jnp.float32
    )
    value_grad = jnp.einsum(
        "tclki,tcj->lktij", weighted, source_feat, preferred_element_type=jnp.float32
    )
    harm_grad = jnp.sum(value_grad * radial[None], axis=1)
    rad_grad = jnp.sum(value_grad * harmonics[:, None], axis=0)
    target_grad, source_grad_pos = pullback((harm_grad, rad_grad))
    grad_part = jnp.sum(
        source_hot[:, None, :, None] * grad_source[:, :, None, :], axis=0
    ).reshape(all_chan, src_atoms)
    row_hot = (jnp.arange(chan_count, dtype=jnp.int32) == chan_index).astype(jnp.float32)
    target_part = jnp.sum(target_hot[:, None, :, None] * target_grad[:, :, None, :], axis=0)
    dpos_src = (
        row_hot[None, None, :, None] * target_part[:, :, None, :]
        + jnp.sum(source_hot[:, None, :, None] * source_grad_pos[:, :, None, :], axis=0).reshape(
            3, src_blocks, chan_count, rows
        )
    ).reshape(3, src_atoms)
    grad_src = lax.psum_scatter(grad_part, "chan", scatter_dimension=0, tiled=True)
    for chan_bit in range(chan_count.bit_length() - 1):
        other_pos, other_rad = partner((dpos_src, grad_rad), "chan", chan_bit)
        dpos_src = dpos_src + other_pos
        grad_rad = grad_rad + other_rad
    grad_rad = lax.dynamic_slice_in_dim(grad_rad, offset, chan_dev, 0)
    own_both = jnp.concatenate([grad_src[:, :atoms_dev], dpos_src[:, :atoms_dev]], axis=0)
    back_list = []
    for level_bit in range(levels):
        low = atoms_dev + level_bit * block_size
        ghost_both = jnp.concatenate(
            [grad_src[:, low : low + block_size], dpos_src[:, low : low + block_size]], axis=0
        )
        back_both, other_rad = partner((ghost_both, grad_rad), "space", level_bit)
        grad_rad = grad_rad + other_rad
        back_list.append(back_both)
    all_rows = send_rows[:levels].reshape(-1)
    own_both = own_both.at[:, all_rows].add(jnp.concatenate(back_list, axis=1))
    own_grad = own_both[:chan_dev]
    own_dpos = own_both[chan_dev:]
    return (result, own_grad.astype(jnp.bfloat16), -own_dpos, grad_rad)


def solution(mesh):
    placed = (
        P(None, "space"),
        P("chan", "space"),
        P("space", None),
        P("space", None),
        P("space"),
        P("chan", None),
        P(),
        P("chan", None, "space"),
    )
    return jax.shard_map(
        body,
        mesh=mesh,
        in_specs=placed,
        out_specs=(P("chan", None, "space"), P("chan", "space"), P(None, "space"), P("chan", None)),
        check_vma=False,
    )
```

```python
import math

import jax
import jax.numpy as jnp
from jax import lax
from jax.sharding import PartitionSpec as P

SOFTENING = 0.25
CUTOFF = 2.5
CUTOFF_SQ = 6.25
SHARPNESS = 10.0
ROOT_THREE = math.sqrt(3.0)
ORDER_OF = (0, 1, 1, 1, 2, 2, 2, 2, 2)


def partner(value, axis, bit):
    mask = 2**bit
    pairs = [(source, source ^ mask) for source in range(lax.axis_size(axis))]
    return lax.ppermute(value, axis, pairs)


def halving_sum(value, axis):
    index = lax.axis_index(axis)
    for bit in reversed(range(lax.axis_size(axis).bit_length() - 1)):
        half = value.shape[0] // 2
        mine = (index >> bit) & 1
        keep = lax.dynamic_slice_in_dim(value, mine * half, half, 0)
        give = lax.dynamic_slice_in_dim(value, (1 - mine) * half, half, 0)
        value = keep + partner(give, axis, bit)
    return value


def as_rows(value, width):
    flat = value.reshape(-1)
    count = -(-flat.shape[0] // width)
    return jnp.pad(flat, (0, count * width - flat.shape[0])).reshape(count, width)


def halving_with(value, extras, axis):
    index = lax.axis_index(axis)
    width = value.shape[1]
    extra_rows = as_rows(jnp.concatenate([extra.reshape(-1) for extra in extras]), width)
    for bit in reversed(range(lax.axis_size(axis).bit_length() - 1)):
        half = value.shape[0] // 2
        mine = (index >> bit) & 1
        keep = lax.dynamic_slice_in_dim(value, mine * half, half, 0)
        give = lax.dynamic_slice_in_dim(value, (1 - mine) * half, half, 0)
        got = partner(jnp.concatenate([give, extra_rows], axis=0), axis, bit)
        value = keep + got[:half]
        extra_rows = extra_rows + got[half:]
    flat = extra_rows.reshape(-1)
    sums = []
    start = 0
    for extra in extras:
        sums.append(flat[start : start + extra.size].reshape(extra.shape))
        start += extra.size
    return value, sums


def geometry(target_pos, source_pos, pair_keep, radial_count):
    offset = source_pos[:, :, None, :] - target_pos[:, :, :, None]
    dist_sq = jnp.sum(offset * offset, axis=1) + SOFTENING
    distance = jnp.sqrt(dist_sq)
    along_x = offset[:, 0] / distance
    along_y = offset[:, 1] / distance
    along_z = offset[:, 2] / distance
    harmonics = jnp.stack(
        [
            jnp.ones_like(along_x),
            along_x,
            along_y,
            along_z,
            ROOT_THREE * along_x * along_y,
            ROOT_THREE * along_y * along_z,
            ROOT_THREE * along_x * along_z,
            0.5 * (3.0 * along_z * along_z - 1.0),
            0.5 * ROOT_THREE * (along_x * along_x - along_y * along_y),
        ]
    )
    envelope = jnp.square(jnp.maximum(1.0 - dist_sq / CUTOFF_SQ, 0.0)) * pair_keep
    centers = (jnp.arange(radial_count, dtype=jnp.float32) + 0.5) * (CUTOFF / radial_count)
    radial = (
        jnp.exp(-SHARPNESS * jnp.square(distance[None] - centers[:, None, None, None]))
        * envelope[None]
    )
    return (harmonics, radial)


def take_block(array, blk_index, block_size):
    return lax.dynamic_slice_in_dim(array, blk_index * block_size, block_size, array.ndim - 1)


def add_block(array, blk_index, value, block_size):
    current = take_block(array, blk_index, block_size)
    return lax.dynamic_update_slice_in_dim(
        array, current + value, blk_index * block_size, array.ndim - 1
    )


def body(
    positions, features, send_rows, pair_tiles, tile_live, radial_weight, mix_weight, out_grad
):
    block_size = send_rows.shape[1]
    atoms_dev = positions.shape[1]
    chan_dev = features.shape[0]
    radial_count = radial_weight.shape[1]
    components = out_grad.shape[1]
    levels = lax.axis_size("space").bit_length() - 1
    chan_count = lax.axis_size("chan")
    chan_index = lax.axis_index("chan")
    pos_list = [positions]
    feat_list = [features]
    both_rows = jnp.take(
        jnp.concatenate([features.astype(jnp.float32), positions], axis=0),
        send_rows[:levels].reshape(-1),
        axis=1,
        mode="clip",
    )
    for level_bit in range(levels):
        got_both = partner(
            both_rows[:, level_bit * block_size : (level_bit + 1) * block_size],
            "space",
            level_bit,
        )
        feat_list.append(got_both[:chan_dev].astype(jnp.bfloat16))
        pos_list.append(got_both[chan_dev:])
    src_pos = jnp.concatenate(pos_list, axis=1)
    src_feat = jnp.concatenate(feat_list, axis=1)
    src_atoms = src_pos.shape[1]
    weight_high = radial_weight.astype(jnp.bfloat16)
    weight_rest = radial_weight - weight_high.astype(jnp.float32)
    weight_mid = weight_rest.astype(jnp.bfloat16)
    weight_low = (weight_rest - weight_mid.astype(jnp.float32)).astype(jnp.bfloat16)
    full_both = lax.all_gather(
        jnp.concatenate([src_feat, weight_high, weight_mid, weight_low], axis=1),
        "chan",
        axis=0,
        tiled=True,
    )
    full_feat = full_both[:, :src_atoms]
    pieces = full_both[:, src_atoms:].astype(jnp.float32)
    full_weight = (
        pieces[:, :radial_count] + pieces[:, radial_count : 2 * radial_count]
    ) + pieces[:, 2 * radial_count :]
    all_chan = full_feat.shape[0]
    src_blocks = src_atoms // block_size
    own_blocks = atoms_dev // block_size
    rows = block_size // chan_count
    row_low = chan_index * rows
    target_idx = pair_tiles[:, 0]
    source_idx = pair_tiles[:, 1]
    live = tile_live.astype(jnp.float32)
    block_ids = jnp.arange(src_blocks, dtype=jnp.int32)
    target_hot = (target_idx[:, None] == block_ids[None]).astype(jnp.float32) * live[:, None]
    source_hot = (source_idx[:, None] == block_ids[None]).astype(jnp.float32) * live[:, None]
    same = (target_idx == source_idx).astype(jnp.float32)
    eye = (
        (row_low + jnp.arange(rows, dtype=jnp.int32))[:, None]
        == jnp.arange(block_size, dtype=jnp.int32)[None]
    ).astype(jnp.float32)
    pair_keep = live[:, None, None] * (1.0 - same[:, None, None] * eye[None])
    pos_blocks = jnp.moveaxis(src_pos.reshape(3, src_blocks, block_size), 1, 0)
    pos_rows = lax.dynamic_slice_in_dim(pos_blocks, row_low, rows, 2)
    feat_blocks = jnp.moveaxis(full_feat.reshape(all_chan, src_blocks, block_size), 1, 0)
    target_pos = jnp.take(pos_rows, target_idx, axis=0, mode="clip")
    source_pos = jnp.take(pos_blocks, source_idx, axis=0, mode="clip")
    source_feat = jnp.take(feat_blocks, source_idx, axis=0, mode="clip")

    def geo_fn(first_pos, second_pos):
        return geometry(first_pos, second_pos, pair_keep, radial_count)

    (harmonics, radial), pullback = jax.vjp(geo_fn, target_pos, source_pos)
    pair_values = (harmonics[:, None] * radial[None]).astype(jnp.bfloat16)
    routed_feat = (
        target_hot[:, :own_blocks, None, None] * source_feat[:, None].astype(jnp.float32)
    ).astype(jnp.bfloat16)
    msg_acc = jnp.einsum(
        "lktij,tbcj->bclki", pair_values, routed_feat, preferred_element_type=jnp.float32
    )
    moments = jnp.einsum("bclki,ck->clbi", msg_acc, full_weight)
    packed = moments.astype(jnp.bfloat16)
    mixing = jnp.take(mix_weight, jnp.array(ORDER_OF, dtype=jnp.int32), axis=0)
    offset = chan_index * chan_dev
    mixed_out = jnp.einsum(
        "lxc,clbi->xlbi", mixing, packed, preferred_element_type=jnp.float32
    )
    scalar_part = mixed_out[:, 0]
    gate_value = jax.nn.sigmoid(scalar_part)
    result_rows = jnp.concatenate(
        [(scalar_part * gate_value)[:, None], mixed_out[:, 1:] * gate_value[:, None]],
        axis=1,
    ).astype(jnp.bfloat16)
    result = lax.all_to_all(
        result_rows.reshape(all_chan, components, own_blocks, 1, rows),
        "chan",
        0,
        3,
        tiled=True,
    ).reshape(chan_dev, components, atoms_dev)
    grad_rows = lax.all_to_all(
        out_grad.reshape(chan_dev, components, own_blocks, chan_count, rows),
        "chan",
        3,
        0,
        tiled=True,
    ).reshape(all_chan, components, own_blocks, rows)
    upstream = grad_rows.astype(jnp.float32)
    scalar_grad = upstream[:, 0] * (
        gate_value * (1.0 + scalar_part * (1.0 - gate_value))
    ) + gate_value * (1.0 - gate_value) * jnp.sum(upstream[:, 1:] * mixed_out[:, 1:], axis=1)
    rest_grad = upstream[:, 1:] * gate_value[:, None]
    dz_packed = jnp.concatenate([scalar_grad[:, None], rest_grad], axis=1).astype(jnp.bfloat16)
    moment_grad_all = jnp.einsum(
        "lxc,xlbi->clbi", mixing, dz_packed, preferred_element_type=jnp.float32
    )
    grad_rad = jnp.einsum("bclki,clbi->ck", msg_acc, moment_grad_all)
    grad_blocks = jnp.moveaxis(moment_grad_all, 2, 0)
    tile_grad = jnp.take(grad_blocks, target_idx, axis=0, mode="clip")
    weighted = (
        live[:, None, None, None, None]
        * full_weight[None, :, None, :, None]
        * tile_grad[:, :, :, None, :]
    ).astype(jnp.bfloat16)
    grad_source = jnp.einsum(
        "tclki,lktij->tcj", weighted, pair_values, preferred_element_type=jnp.float32
    )
    value_grad = jnp.einsum(
        "tclki,tcj->lktij", weighted, source_feat, preferred_element_type=jnp.float32
    )
    harm_grad = jnp.sum(value_grad * radial[None], axis=1)
    rad_grad = jnp.sum(value_grad * harmonics[:, None], axis=0)
    target_grad, source_grad_pos = pullback((harm_grad, rad_grad))
    grad_part = jnp.sum(
        source_hot[:, None, :, None] * grad_source[:, :, None, :], axis=0
    ).reshape(all_chan, src_atoms)
    row_hot = (jnp.arange(chan_count, dtype=jnp.int32) == chan_index).astype(jnp.float32)
    target_part = jnp.sum(target_hot[:, None, :, None] * target_grad[:, :, None, :], axis=0)
    dpos_src = (
        row_hot[None, None, :, None] * target_part[:, :, None, :]
        + jnp.sum(source_hot[:, None, :, None] * source_grad_pos[:, :, None, :], axis=0).reshape(
            3, src_blocks, chan_count, rows
        )
    ).reshape(3, src_atoms)
    grad_src, (dpos_src, grad_rad) = halving_with(grad_part, (dpos_src, grad_rad), "chan")
    grad_rad = lax.dynamic_slice_in_dim(grad_rad, offset, chan_dev, 0)
    own_both = jnp.concatenate([grad_src[:, :atoms_dev], dpos_src[:, :atoms_dev]], axis=0)
    ghost_rows = chan_dev + 3
    back_list = []
    for level_bit in range(levels):
        low = atoms_dev + level_bit * block_size
        ghost_both = jnp.concatenate(
            [
                grad_src[:, low : low + block_size],
                dpos_src[:, low : low + block_size],
                as_rows(grad_rad, block_size),
            ],
            axis=0,
        )
        back_both = partner(ghost_both, "space", level_bit)
        grad_rad = grad_rad + back_both[ghost_rows:].reshape(-1)[: grad_rad.size].reshape(
            grad_rad.shape
        )
        back_list.append(back_both[:ghost_rows])
    all_rows = send_rows[:levels].reshape(-1)
    own_both = own_both.at[:, all_rows].add(jnp.concatenate(back_list, axis=1))
    own_grad = own_both[:chan_dev]
    own_dpos = own_both[chan_dev:]
    return (result, own_grad.astype(jnp.bfloat16), -own_dpos, grad_rad)


def solution(mesh):
    placed = (
        P(None, "space"),
        P("chan", "space"),
        P("space", None),
        P("space", None),
        P("space"),
        P("chan", None),
        P(),
        P("chan", None, "space"),
    )
    return jax.shard_map(
        body,
        mesh=mesh,
        in_specs=placed,
        out_specs=(P("chan", None, "space"), P("chan", "space"), P(None, "space"), P("chan", None)),
        check_vma=False,
    )
```

```python
import math

import jax
import jax.numpy as jnp
from jax import lax
from jax.sharding import PartitionSpec as P

SOFTENING = 0.25
CUTOFF = 2.5
CUTOFF_SQ = 6.25
SHARPNESS = 10.0
ROOT_THREE = math.sqrt(3.0)
ORDER_OF = (0, 1, 1, 1, 2, 2, 2, 2, 2)


def partner(value, axis, bit):
    mask = 2**bit
    pairs = [(source, source ^ mask) for source in range(lax.axis_size(axis))]
    return lax.ppermute(value, axis, pairs)


def halving_sum(value, axis):
    index = lax.axis_index(axis)
    for bit in reversed(range(lax.axis_size(axis).bit_length() - 1)):
        half = value.shape[0] // 2
        mine = (index >> bit) & 1
        keep = lax.dynamic_slice_in_dim(value, mine * half, half, 0)
        give = lax.dynamic_slice_in_dim(value, (1 - mine) * half, half, 0)
        value = keep + partner(give, axis, bit)
    return value


def as_rows(value, width):
    flat = value.reshape(-1)
    count = -(-flat.shape[0] // width)
    return jnp.pad(flat, (0, count * width - flat.shape[0])).reshape(count, width)


def halving_with(value, extras, axis):
    index = lax.axis_index(axis)
    width = value.shape[1]
    extra_rows = as_rows(jnp.concatenate([extra.reshape(-1) for extra in extras]), width)
    count = lax.axis_size(axis)
    chunk = value.shape[0] // count
    for bit in range(count.bit_length() - 1):
        groups = value.reshape(-1, 2, chunk, width)
        mine = (index >> bit) & 1
        keep = lax.dynamic_index_in_dim(groups, mine, 1, keepdims=False).reshape(-1, width)
        give = lax.dynamic_index_in_dim(groups, 1 - mine, 1, keepdims=False).reshape(-1, width)
        half = give.shape[0]
        got = partner(jnp.concatenate([give, extra_rows], axis=0), axis, bit)
        value = keep + got[:half]
        extra_rows = extra_rows + got[half:]
    flat = extra_rows.reshape(-1)
    sums = []
    start = 0
    for extra in extras:
        sums.append(flat[start : start + extra.size].reshape(extra.shape))
        start += extra.size
    return value, sums


def geometry(target_pos, source_pos, pair_keep, radial_count):
    offset = source_pos[:, :, None, :] - target_pos[:, :, :, None]
    dist_sq = jnp.sum(offset * offset, axis=1) + SOFTENING
    distance = jnp.sqrt(dist_sq)
    along_x = offset[:, 0] / distance
    along_y = offset[:, 1] / distance
    along_z = offset[:, 2] / distance
    harmonics = jnp.stack(
        [
            jnp.ones_like(along_x),
            along_x,
            along_y,
            along_z,
            ROOT_THREE * along_x * along_y,
            ROOT_THREE * along_y * along_z,
            ROOT_THREE * along_x * along_z,
            0.5 * (3.0 * along_z * along_z - 1.0),
            0.5 * ROOT_THREE * (along_x * along_x - along_y * along_y),
        ]
    )
    envelope = jnp.square(jnp.maximum(1.0 - dist_sq / CUTOFF_SQ, 0.0)) * pair_keep
    centers = (jnp.arange(radial_count, dtype=jnp.float32) + 0.5) * (CUTOFF / radial_count)
    radial = (
        jnp.exp(-SHARPNESS * jnp.square(distance[None] - centers[:, None, None, None]))
        * envelope[None]
    )
    return (harmonics, radial)


def take_block(array, blk_index, block_size):
    return lax.dynamic_slice_in_dim(array, blk_index * block_size, block_size, array.ndim - 1)


def add_block(array, blk_index, value, block_size):
    current = take_block(array, blk_index, block_size)
    return lax.dynamic_update_slice_in_dim(
        array, current + value, blk_index * block_size, array.ndim - 1
    )


def body(
    positions, features, send_rows, pair_tiles, tile_live, radial_weight, mix_weight, out_grad
):
    block_size = send_rows.shape[1]
    atoms_dev = positions.shape[1]
    chan_dev = features.shape[0]
    radial_count = radial_weight.shape[1]
    components = out_grad.shape[1]
    levels = lax.axis_size("space").bit_length() - 1
    chan_count = lax.axis_size("chan")
    chan_index = lax.axis_index("chan")
    pos_list = [positions]
    feat_list = [features]
    both_rows = jnp.take(
        jnp.concatenate([features.astype(jnp.float32), positions], axis=0),
        send_rows[:levels].reshape(-1),
        axis=1,
        mode="clip",
    )
    for level_bit in range(levels):
        got_both = partner(
            both_rows[:, level_bit * block_size : (level_bit + 1) * block_size],
            "space",
            level_bit,
        )
        feat_list.append(got_both[:chan_dev].astype(jnp.bfloat16))
        pos_list.append(got_both[chan_dev:])
    src_pos = jnp.concatenate(pos_list, axis=1)
    src_feat = jnp.concatenate(feat_list, axis=1)
    src_atoms = src_pos.shape[1]
    weight_high = radial_weight.astype(jnp.bfloat16)
    weight_rest = radial_weight - weight_high.astype(jnp.float32)
    weight_mid = weight_rest.astype(jnp.bfloat16)
    weight_low = (weight_rest - weight_mid.astype(jnp.float32)).astype(jnp.bfloat16)
    full_both = lax.all_gather(
        jnp.concatenate([src_feat, weight_high, weight_mid, weight_low], axis=1),
        "chan",
        axis=0,
        tiled=True,
    )
    full_feat = full_both[:, :src_atoms]
    pieces = full_both[:, src_atoms:].astype(jnp.float32)
    full_weight = (
        pieces[:, :radial_count] + pieces[:, radial_count : 2 * radial_count]
    ) + pieces[:, 2 * radial_count :]
    all_chan = full_feat.shape[0]
    src_blocks = src_atoms // block_size
    own_blocks = atoms_dev // block_size
    rows = block_size // chan_count
    row_low = chan_index * rows
    target_idx = pair_tiles[:, 0]
    source_idx = pair_tiles[:, 1]
    live = tile_live.astype(jnp.float32)
    block_ids = jnp.arange(src_blocks, dtype=jnp.int32)
    target_hot = (target_idx[:, None] == block_ids[None]).astype(jnp.float32) * live[:, None]
    source_hot = (source_idx[:, None] == block_ids[None]).astype(jnp.float32) * live[:, None]
    same = (target_idx == source_idx).astype(jnp.float32)
    eye = (
        (row_low + jnp.arange(rows, dtype=jnp.int32))[:, None]
        == jnp.arange(block_size, dtype=jnp.int32)[None]
    ).astype(jnp.float32)
    pair_keep = live[:, None, None] * (1.0 - same[:, None, None] * eye[None])
    pos_blocks = jnp.moveaxis(src_pos.reshape(3, src_blocks, block_size), 1, 0)
    pos_rows = lax.dynamic_slice_in_dim(pos_blocks, row_low, rows, 2)
    feat_blocks = jnp.moveaxis(full_feat.reshape(all_chan, src_blocks, block_size), 1, 0)
    target_pos = jnp.take(pos_rows, target_idx, axis=0, mode="clip")
    source_pos = jnp.take(pos_blocks, source_idx, axis=0, mode="clip")
    source_feat = jnp.take(feat_blocks, source_idx, axis=0, mode="clip")

    def geo_fn(first_pos, second_pos):
        return geometry(first_pos, second_pos, pair_keep, radial_count)

    (harmonics, radial), pullback = jax.vjp(geo_fn, target_pos, source_pos)
    pair_values = (harmonics[:, None] * radial[None]).astype(jnp.bfloat16)
    routed_feat = (
        target_hot[:, :own_blocks, None, None] * source_feat[:, None].astype(jnp.float32)
    ).astype(jnp.bfloat16)
    msg_acc = jnp.einsum(
        "lktij,tbcj->bclki", pair_values, routed_feat, preferred_element_type=jnp.float32
    )
    moments = jnp.einsum("bclki,ck->clbi", msg_acc, full_weight)
    packed = moments.astype(jnp.bfloat16)
    mixing = jnp.take(mix_weight, jnp.array(ORDER_OF, dtype=jnp.int32), axis=0)
    offset = chan_index * chan_dev
    mixed_out = jnp.einsum(
        "lxc,clbi->xlbi", mixing, packed, preferred_element_type=jnp.float32
    )
    scalar_part = mixed_out[:, 0]
    gate_value = jax.nn.sigmoid(scalar_part)
    result_rows = jnp.concatenate(
        [(scalar_part * gate_value)[:, None], mixed_out[:, 1:] * gate_value[:, None]],
        axis=1,
    ).astype(jnp.bfloat16)
    result = lax.all_to_all(
        result_rows.reshape(all_chan, components, own_blocks, 1, rows),
        "chan",
        0,
        3,
        tiled=True,
    ).reshape(chan_dev, components, atoms_dev)
    grad_rows = lax.all_to_all(
        out_grad.reshape(chan_dev, components, own_blocks, chan_count, rows),
        "chan",
        3,
        0,
        tiled=True,
    ).reshape(all_chan, components, own_blocks, rows)
    upstream = grad_rows.astype(jnp.float32)
    scalar_grad = upstream[:, 0] * (
        gate_value * (1.0 + scalar_part * (1.0 - gate_value))
    ) + gate_value * (1.0 - gate_value) * jnp.sum(upstream[:, 1:] * mixed_out[:, 1:], axis=1)
    rest_grad = upstream[:, 1:] * gate_value[:, None]
    dz_packed = jnp.concatenate([scalar_grad[:, None], rest_grad], axis=1).astype(jnp.bfloat16)
    moment_grad_all = jnp.einsum(
        "lxc,xlbi->clbi", mixing, dz_packed, preferred_element_type=jnp.float32
    )
    grad_rad = jnp.einsum("bclki,clbi->ck", msg_acc, moment_grad_all)
    grad_blocks = jnp.moveaxis(moment_grad_all, 2, 0)
    tile_grad = jnp.take(grad_blocks, target_idx, axis=0, mode="clip")
    weighted = (
        live[:, None, None, None, None]
        * full_weight[None, :, None, :, None]
        * tile_grad[:, :, :, None, :]
    ).astype(jnp.bfloat16)
    grad_source = jnp.einsum(
        "tclki,lktij->tcj", weighted, pair_values, preferred_element_type=jnp.float32
    )
    value_grad = jnp.einsum(
        "tclki,tcj->lktij", weighted, source_feat, preferred_element_type=jnp.float32
    )
    harm_grad = jnp.sum(value_grad * radial[None], axis=1)
    rad_grad = jnp.sum(value_grad * harmonics[:, None], axis=0)
    target_grad, source_grad_pos = pullback((harm_grad, rad_grad))
    grad_part = jnp.sum(
        source_hot[:, None, :, None] * grad_source[:, :, None, :], axis=0
    ).reshape(all_chan, src_atoms)
    row_hot = (jnp.arange(chan_count, dtype=jnp.int32) == chan_index).astype(jnp.float32)
    target_part = jnp.sum(target_hot[:, None, :, None] * target_grad[:, :, None, :], axis=0)
    dpos_src = (
        row_hot[None, None, :, None] * target_part[:, :, None, :]
        + jnp.sum(source_hot[:, None, :, None] * source_grad_pos[:, :, None, :], axis=0).reshape(
            3, src_blocks, chan_count, rows
        )
    ).reshape(3, src_atoms)
    grad_src, (dpos_src, grad_rad) = halving_with(grad_part, (dpos_src, grad_rad), "chan")
    grad_rad = lax.dynamic_slice_in_dim(grad_rad, offset, chan_dev, 0)
    own_both = jnp.concatenate([grad_src[:, :atoms_dev], dpos_src[:, :atoms_dev]], axis=0)
    ghost_rows = chan_dev + 3
    back_list = []
    for level_bit in range(levels):
        low = atoms_dev + level_bit * block_size
        ghost_both = jnp.concatenate(
            [
                grad_src[:, low : low + block_size],
                dpos_src[:, low : low + block_size],
                as_rows(grad_rad, block_size),
            ],
            axis=0,
        )
        back_both = partner(ghost_both, "space", level_bit)
        grad_rad = grad_rad + back_both[ghost_rows:].reshape(-1)[: grad_rad.size].reshape(
            grad_rad.shape
        )
        back_list.append(back_both[:ghost_rows])
    all_rows = send_rows[:levels].reshape(-1)
    own_both = own_both.at[:, all_rows].add(jnp.concatenate(back_list, axis=1))
    own_grad = own_both[:chan_dev]
    own_dpos = own_both[chan_dev:]
    return (result, own_grad.astype(jnp.bfloat16), -own_dpos, grad_rad)


def solution(mesh):
    placed = (
        P(None, "space"),
        P("chan", "space"),
        P("space", None),
        P("space", None),
        P("space"),
        P("chan", None),
        P(),
        P("chan", None, "space"),
    )
    return jax.shard_map(
        body,
        mesh=mesh,
        in_specs=placed,
        out_specs=(P("chan", None, "space"), P("chan", "space"), P(None, "space"), P("chan", None)),
        check_vma=False,
    )
```

```python
import math

import jax
import jax.numpy as jnp
from jax import lax
from jax.sharding import PartitionSpec as P

SOFTENING = 0.25
CUTOFF = 2.5
CUTOFF_SQ = 6.25
SHARPNESS = 10.0
ROOT_THREE = math.sqrt(3.0)
ORDER_OF = (0, 1, 1, 1, 2, 2, 2, 2, 2)


def partner(value, axis, bit):
    mask = 2**bit
    pairs = [(source, source ^ mask) for source in range(lax.axis_size(axis))]
    return lax.ppermute(value, axis, pairs)


def halving_sum(value, axis):
    index = lax.axis_index(axis)
    for bit in reversed(range(lax.axis_size(axis).bit_length() - 1)):
        half = value.shape[0] // 2
        mine = (index >> bit) & 1
        keep = lax.dynamic_slice_in_dim(value, mine * half, half, 0)
        give = lax.dynamic_slice_in_dim(value, (1 - mine) * half, half, 0)
        value = keep + partner(give, axis, bit)
    return value


def as_rows(value, width):
    flat = value.reshape(-1)
    count = -(-flat.shape[0] // width)
    return jnp.pad(flat, (0, count * width - flat.shape[0])).reshape(count, width)


def halving_with(value, extras, axis):
    index = lax.axis_index(axis)
    width = value.shape[1]
    extra_rows = as_rows(jnp.concatenate([extra.reshape(-1) for extra in extras]), width)
    count = lax.axis_size(axis)
    chunk = value.shape[0] // count
    for bit in range(count.bit_length() - 1):
        groups = value.reshape(-1, 2, chunk, width)
        mine = (index >> bit) & 1
        keep = lax.dynamic_index_in_dim(groups, mine, 1, keepdims=False).reshape(-1, width)
        give = lax.dynamic_index_in_dim(groups, 1 - mine, 1, keepdims=False).reshape(-1, width)
        half = give.shape[0]
        got = partner(jnp.concatenate([give, extra_rows], axis=0), axis, bit)
        value = keep + got[:half]
        extra_rows = extra_rows + got[half:]
    flat = extra_rows.reshape(-1)
    sums = []
    start = 0
    for extra in extras:
        sums.append(flat[start : start + extra.size].reshape(extra.shape))
        start += extra.size
    return value, sums


def geometry(target_pos, source_pos, pair_keep, radial_count):
    offset = source_pos[:, :, None, :] - target_pos[:, :, :, None]
    dist_sq = jnp.sum(offset * offset, axis=1) + SOFTENING
    distance = jnp.sqrt(dist_sq)
    along_x = offset[:, 0] / distance
    along_y = offset[:, 1] / distance
    along_z = offset[:, 2] / distance
    harmonics = jnp.stack(
        [
            jnp.ones_like(along_x),
            along_x,
            along_y,
            along_z,
            ROOT_THREE * along_x * along_y,
            ROOT_THREE * along_y * along_z,
            ROOT_THREE * along_x * along_z,
            0.5 * (3.0 * along_z * along_z - 1.0),
            0.5 * ROOT_THREE * (along_x * along_x - along_y * along_y),
        ]
    )
    envelope = jnp.square(jnp.maximum(1.0 - dist_sq / CUTOFF_SQ, 0.0)) * pair_keep
    centers = (jnp.arange(radial_count, dtype=jnp.float32) + 0.5) * (CUTOFF / radial_count)
    radial = (
        jnp.exp(-SHARPNESS * jnp.square(distance[None] - centers[:, None, None, None]))
        * envelope[None]
    )
    return (harmonics, radial)


def take_block(array, blk_index, block_size):
    return lax.dynamic_slice_in_dim(array, blk_index * block_size, block_size, array.ndim - 1)


def add_block(array, blk_index, value, block_size):
    current = take_block(array, blk_index, block_size)
    return lax.dynamic_update_slice_in_dim(
        array, current + value, blk_index * block_size, array.ndim - 1
    )


def body(
    positions, features, send_rows, pair_tiles, tile_live, radial_weight, mix_weight, out_grad
):
    block_size = send_rows.shape[1]
    atoms_dev = positions.shape[1]
    chan_dev = features.shape[0]
    radial_count = radial_weight.shape[1]
    components = out_grad.shape[1]
    levels = lax.axis_size("space").bit_length() - 1
    chan_count = lax.axis_size("chan")
    chan_index = lax.axis_index("chan")
    pos_list = [positions]
    feat_list = [features]
    both_rows = jnp.take(
        jnp.concatenate([features.astype(jnp.float32), positions], axis=0),
        send_rows[:levels].reshape(-1),
        axis=1,
        mode="clip",
    )
    for level_bit in range(levels):
        got_both = partner(
            both_rows[:, level_bit * block_size : (level_bit + 1) * block_size],
            "space",
            level_bit,
        )
        feat_list.append(got_both[:chan_dev].astype(jnp.bfloat16))
        pos_list.append(got_both[chan_dev:])
    src_pos = jnp.concatenate(pos_list, axis=1)
    src_feat = jnp.concatenate(feat_list, axis=1)
    src_atoms = src_pos.shape[1]
    weight_high = radial_weight.astype(jnp.bfloat16)
    weight_rest = radial_weight - weight_high.astype(jnp.float32)
    weight_mid = weight_rest.astype(jnp.bfloat16)
    weight_low = (weight_rest - weight_mid.astype(jnp.float32)).astype(jnp.bfloat16)
    full_both = lax.all_gather(
        jnp.concatenate([src_feat, weight_high, weight_mid, weight_low], axis=1),
        "chan",
        axis=0,
        tiled=True,
    )
    full_feat = full_both[:, :src_atoms]
    pieces = full_both[:, src_atoms:].astype(jnp.float32)
    full_weight = (
        pieces[:, :radial_count] + pieces[:, radial_count : 2 * radial_count]
    ) + pieces[:, 2 * radial_count :]
    all_chan = full_feat.shape[0]
    src_blocks = src_atoms // block_size
    own_blocks = atoms_dev // block_size
    rows = block_size // chan_count
    row_low = chan_index * rows
    target_idx = pair_tiles[:, 0]
    source_idx = pair_tiles[:, 1]
    live = tile_live.astype(jnp.float32)
    block_ids = jnp.arange(src_blocks, dtype=jnp.int32)
    target_hot = (target_idx[:, None] == block_ids[None]).astype(jnp.float32) * live[:, None]
    source_hot = (source_idx[:, None] == block_ids[None]).astype(jnp.float32) * live[:, None]
    same = (target_idx == source_idx).astype(jnp.float32)
    eye = (
        (row_low + jnp.arange(rows, dtype=jnp.int32))[:, None]
        == jnp.arange(block_size, dtype=jnp.int32)[None]
    ).astype(jnp.float32)
    pair_keep = live[:, None, None] * (1.0 - same[:, None, None] * eye[None])
    pos_blocks = jnp.moveaxis(src_pos.reshape(3, src_blocks, block_size), 1, 0)
    pos_rows = lax.dynamic_slice_in_dim(pos_blocks, row_low, rows, 2)
    feat_blocks = jnp.moveaxis(full_feat.reshape(all_chan, src_blocks, block_size), 1, 0)
    target_pos = jnp.take(pos_rows, target_idx, axis=0, mode="clip")
    source_pos = jnp.take(pos_blocks, source_idx, axis=0, mode="clip")
    source_feat = jnp.take(feat_blocks, source_idx, axis=0, mode="clip")

    def geo_fn(first_pos, second_pos):
        return geometry(first_pos, second_pos, pair_keep, radial_count)

    (harmonics, radial), pullback = jax.vjp(geo_fn, target_pos, source_pos)
    pair_values = (harmonics[:, None] * radial[None]).astype(jnp.bfloat16)
    routed_feat = (
        target_hot[:, :own_blocks, None, None] * source_feat[:, None].astype(jnp.float32)
    ).astype(jnp.bfloat16)
    msg_acc = jnp.einsum(
        "lktij,tbcj->bclki", pair_values, routed_feat, preferred_element_type=jnp.float32
    )
    moments = jnp.einsum("bclki,ck->clbi", msg_acc, full_weight)
    packed = moments.astype(jnp.bfloat16)
    mixing = jnp.take(mix_weight, jnp.array(ORDER_OF, dtype=jnp.int32), axis=0)
    offset = chan_index * chan_dev
    mixed_out = jnp.einsum(
        "lxc,clbi->xlbi", mixing, packed, preferred_element_type=jnp.float32
    )
    scalar_part = mixed_out[:, 0]
    gate_value = jax.nn.sigmoid(scalar_part)
    result_rows = jnp.concatenate(
        [(scalar_part * gate_value)[:, None], mixed_out[:, 1:] * gate_value[:, None]],
        axis=1,
    ).astype(jnp.bfloat16)
    result = lax.all_to_all(
        result_rows.reshape(all_chan, components, own_blocks, 1, rows),
        "chan",
        0,
        3,
        tiled=True,
    ).reshape(chan_dev, components, atoms_dev)
    grad_rows = lax.all_to_all(
        out_grad.reshape(chan_dev, components, own_blocks, chan_count, rows),
        "chan",
        3,
        0,
        tiled=True,
    ).reshape(all_chan, components, own_blocks, rows)
    upstream = grad_rows.astype(jnp.float32)
    scalar_grad = upstream[:, 0] * (
        gate_value * (1.0 + scalar_part * (1.0 - gate_value))
    ) + gate_value * (1.0 - gate_value) * jnp.sum(upstream[:, 1:] * mixed_out[:, 1:], axis=1)
    rest_grad = upstream[:, 1:] * gate_value[:, None]
    dz_packed = jnp.concatenate([scalar_grad[:, None], rest_grad], axis=1).astype(jnp.bfloat16)
    moment_grad_all = jnp.einsum(
        "lxc,xlbi->clbi", mixing, dz_packed, preferred_element_type=jnp.float32
    )
    grad_rad = jnp.einsum("bclki,clbi->ck", msg_acc, moment_grad_all)
    grad_blocks = jnp.moveaxis(moment_grad_all, 2, 0)
    tile_grad = jnp.take(grad_blocks, target_idx, axis=0, mode="clip")
    weighted = (
        live[:, None, None, None, None]
        * full_weight[None, :, None, :, None]
        * tile_grad[:, :, :, None, :]
    ).astype(jnp.bfloat16)
    grad_source = jnp.einsum(
        "tclki,lktij->tcj", weighted, pair_values, preferred_element_type=jnp.float32
    )
    value_grad = jnp.einsum(
        "tclki,tcj->lktij", weighted, source_feat, preferred_element_type=jnp.float32
    )
    harm_grad = jnp.sum(value_grad * radial[None], axis=1)
    rad_grad = jnp.sum(value_grad * harmonics[:, None], axis=0)
    target_grad, source_grad_pos = pullback((harm_grad, rad_grad))
    grad_part = jnp.sum(
        source_hot[:, None, :, None] * grad_source[:, :, None, :], axis=0
    ).reshape(all_chan, src_atoms)
    row_hot = (jnp.arange(chan_count, dtype=jnp.int32) == chan_index).astype(jnp.float32)
    target_part = jnp.sum(target_hot[:, None, :, None] * target_grad[:, :, None, :], axis=0)
    dpos_src = (
        row_hot[None, None, :, None] * target_part[:, :, None, :]
        + jnp.sum(source_hot[:, None, :, None] * source_grad_pos[:, :, None, :], axis=0).reshape(
            3, src_blocks, chan_count, rows
        )
    ).reshape(3, src_atoms)
    grad_src, (dpos_src, grad_rad) = halving_with(grad_part, (dpos_src, grad_rad), "chan")
    grad_rad = lax.dynamic_slice_in_dim(grad_rad, offset, chan_dev, 0)
    own_both = jnp.concatenate([grad_src[:, :atoms_dev], dpos_src[:, :atoms_dev]], axis=0)
    ghost_rows = chan_dev + 3
    back_list = []
    for level_bit in range(levels):
        low = atoms_dev + level_bit * block_size
        ghost_both = jnp.concatenate(
            [
                grad_src[:, low : low + block_size],
                dpos_src[:, low : low + block_size],
                as_rows(grad_rad, block_size),
            ],
            axis=0,
        )
        back_both = partner(ghost_both, "space", level_bit)
        grad_rad = grad_rad + back_both[ghost_rows:].reshape(-1)[: grad_rad.size].reshape(
            grad_rad.shape
        )
        back_list.append(back_both[:ghost_rows])
    all_rows = send_rows[:levels].reshape(-1)
    ghost_hot = (all_rows[:, None] == jnp.arange(atoms_dev, dtype=jnp.int32)[None]).astype(
        jnp.float32
    )
    own_both = own_both + jnp.dot(
        jnp.concatenate(back_list, axis=1), ghost_hot, precision=lax.Precision.HIGHEST
    )
    own_grad = own_both[:chan_dev]
    own_dpos = own_both[chan_dev:]
    return (result, own_grad.astype(jnp.bfloat16), -own_dpos, grad_rad)


def solution(mesh):
    placed = (
        P(None, "space"),
        P("chan", "space"),
        P("space", None),
        P("space", None),
        P("space"),
        P("chan", None),
        P(),
        P("chan", None, "space"),
    )
    return jax.shard_map(
        body,
        mesh=mesh,
        in_specs=placed,
        out_specs=(P("chan", None, "space"), P("chan", "space"), P(None, "space"), P("chan", None)),
        check_vma=False,
    )
```

```python
import math

import jax
import jax.numpy as jnp
from jax import lax
from jax.experimental import pallas as pl
from jax.sharding import PartitionSpec as P

SOFTENING = 0.25
CUTOFF = 2.5
CUTOFF_SQ = 6.25
SHARPNESS = 10.0
ROOT_THREE = math.sqrt(3.0)
ORDER_OF = (0, 1, 1, 1, 2, 2, 2, 2, 2)


def partner(value, axis, bit):
    mask = 2**bit
    pairs = [(source, source ^ mask) for source in range(lax.axis_size(axis))]
    return lax.ppermute(value, axis, pairs)


def halving_sum(value, axis):
    index = lax.axis_index(axis)
    for bit in reversed(range(lax.axis_size(axis).bit_length() - 1)):
        half = value.shape[0] // 2
        mine = (index >> bit) & 1
        keep = lax.dynamic_slice_in_dim(value, mine * half, half, 0)
        give = lax.dynamic_slice_in_dim(value, (1 - mine) * half, half, 0)
        value = keep + partner(give, axis, bit)
    return value


def as_rows(value, width):
    flat = value.reshape(-1)
    count = -(-flat.shape[0] // width)
    return jnp.pad(flat, (0, count * width - flat.shape[0])).reshape(count, width)


def halving_with(value, extras, axis):
    index = lax.axis_index(axis)
    width = value.shape[1]
    extra_rows = as_rows(jnp.concatenate([extra.reshape(-1) for extra in extras]), width)
    count = lax.axis_size(axis)
    chunk = value.shape[0] // count
    for bit in range(count.bit_length() - 1):
        groups = value.reshape(-1, 2, chunk, width)
        mine = (index >> bit) & 1
        keep = lax.dynamic_index_in_dim(groups, mine, 1, keepdims=False).reshape(-1, width)
        give = lax.dynamic_index_in_dim(groups, 1 - mine, 1, keepdims=False).reshape(-1, width)
        half = give.shape[0]
        got = partner(jnp.concatenate([give, extra_rows], axis=0), axis, bit)
        value = keep + got[:half]
        extra_rows = extra_rows + got[half:]
    flat = extra_rows.reshape(-1)
    sums = []
    start = 0
    for extra in extras:
        sums.append(flat[start : start + extra.size].reshape(extra.shape))
        start += extra.size
    return value, sums


def value_grad_kernel(weight_ref, feat_ref, radial_ref, harm_ref, harm_out, radial_out):
    value_grad = lax.dot_general(
        weight_ref[0],
        feat_ref[0],
        (((0,), (0,)), ((), ())),
        preferred_element_type=jnp.float32,
    )
    radial = radial_ref[:, 0]
    harmonics = harm_ref[:, 0]
    value_grad = value_grad.reshape(harmonics.shape[0], radial.shape[0], *radial.shape[1:])
    harm_out[:, 0] = jnp.sum(value_grad * radial[None], axis=1)
    radial_out[:, 0] = jnp.sum(value_grad * harmonics[:, None], axis=0)


def value_grad_sums(weighted, source_feat, radial, harmonics):
    tiles, chans = weighted.shape[:2]
    flat = weighted.reshape(tiles, chans, -1)
    lanes = source_feat.shape[2]
    radial_count, _, rows, _ = radial.shape
    components = harmonics.shape[0]
    return pl.pallas_call(
        value_grad_kernel,
        grid=(tiles,),
        in_specs=[
            pl.BlockSpec((1, chans, flat.shape[2]), lambda t: (t, 0, 0)),
            pl.BlockSpec((1, chans, lanes), lambda t: (t, 0, 0)),
            pl.BlockSpec((radial_count, 1, rows, lanes), lambda t: (0, t, 0, 0)),
            pl.BlockSpec((components, 1, rows, lanes), lambda t: (0, t, 0, 0)),
        ],
        out_specs=[
            pl.BlockSpec((components, 1, rows, lanes), lambda t: (0, t, 0, 0)),
            pl.BlockSpec((radial_count, 1, rows, lanes), lambda t: (0, t, 0, 0)),
        ],
        out_shape=[
            jax.ShapeDtypeStruct(harmonics.shape, jnp.float32),
            jax.ShapeDtypeStruct(radial.shape, jnp.float32),
        ],
    )(flat, source_feat, radial, harmonics)


def geometry(target_pos, source_pos, pair_keep, radial_count):
    offset = source_pos[:, :, None, :] - target_pos[:, :, :, None]
    dist_sq = jnp.sum(offset * offset, axis=1) + SOFTENING
    distance = jnp.sqrt(dist_sq)
    along_x = offset[:, 0] / distance
    along_y = offset[:, 1] / distance
    along_z = offset[:, 2] / distance
    harmonics = jnp.stack(
        [
            jnp.ones_like(along_x),
            along_x,
            along_y,
            along_z,
            ROOT_THREE * along_x * along_y,
            ROOT_THREE * along_y * along_z,
            ROOT_THREE * along_x * along_z,
            0.5 * (3.0 * along_z * along_z - 1.0),
            0.5 * ROOT_THREE * (along_x * along_x - along_y * along_y),
        ]
    )
    envelope = jnp.square(jnp.maximum(1.0 - dist_sq / CUTOFF_SQ, 0.0)) * pair_keep
    centers = (jnp.arange(radial_count, dtype=jnp.float32) + 0.5) * (CUTOFF / radial_count)
    radial = (
        jnp.exp(-SHARPNESS * jnp.square(distance[None] - centers[:, None, None, None]))
        * envelope[None]
    )
    return (harmonics, radial)


def take_block(array, blk_index, block_size):
    return lax.dynamic_slice_in_dim(array, blk_index * block_size, block_size, array.ndim - 1)


def add_block(array, blk_index, value, block_size):
    current = take_block(array, blk_index, block_size)
    return lax.dynamic_update_slice_in_dim(
        array, current + value, blk_index * block_size, array.ndim - 1
    )


def body(
    positions, features, send_rows, pair_tiles, tile_live, radial_weight, mix_weight, out_grad
):
    block_size = send_rows.shape[1]
    atoms_dev = positions.shape[1]
    chan_dev = features.shape[0]
    radial_count = radial_weight.shape[1]
    components = out_grad.shape[1]
    levels = lax.axis_size("space").bit_length() - 1
    chan_count = lax.axis_size("chan")
    chan_index = lax.axis_index("chan")
    pos_list = [positions]
    feat_list = [features]
    both_rows = jnp.take(
        jnp.concatenate([features.astype(jnp.float32), positions], axis=0),
        send_rows[:levels].reshape(-1),
        axis=1,
        mode="clip",
    )
    for level_bit in range(levels):
        got_both = partner(
            both_rows[:, level_bit * block_size : (level_bit + 1) * block_size],
            "space",
            level_bit,
        )
        feat_list.append(got_both[:chan_dev].astype(jnp.bfloat16))
        pos_list.append(got_both[chan_dev:])
    src_pos = jnp.concatenate(pos_list, axis=1)
    src_feat = jnp.concatenate(feat_list, axis=1)
    src_atoms = src_pos.shape[1]
    weight_high = radial_weight.astype(jnp.bfloat16)
    weight_rest = radial_weight - weight_high.astype(jnp.float32)
    weight_mid = weight_rest.astype(jnp.bfloat16)
    weight_low = (weight_rest - weight_mid.astype(jnp.float32)).astype(jnp.bfloat16)
    full_both = lax.all_gather(
        jnp.concatenate([src_feat, weight_high, weight_mid, weight_low], axis=1),
        "chan",
        axis=0,
        tiled=True,
    )
    full_feat = full_both[:, :src_atoms]
    pieces = full_both[:, src_atoms:].astype(jnp.float32)
    full_weight = (
        pieces[:, :radial_count] + pieces[:, radial_count : 2 * radial_count]
    ) + pieces[:, 2 * radial_count :]
    all_chan = full_feat.shape[0]
    src_blocks = src_atoms // block_size
    own_blocks = atoms_dev // block_size
    rows = block_size // chan_count
    row_low = chan_index * rows
    target_idx = pair_tiles[:, 0]
    source_idx = pair_tiles[:, 1]
    live = tile_live.astype(jnp.float32)
    block_ids = jnp.arange(src_blocks, dtype=jnp.int32)
    target_hot = (target_idx[:, None] == block_ids[None]).astype(jnp.float32) * live[:, None]
    source_hot = (source_idx[:, None] == block_ids[None]).astype(jnp.float32) * live[:, None]
    same = (target_idx == source_idx).astype(jnp.float32)
    eye = (
        (row_low + jnp.arange(rows, dtype=jnp.int32))[:, None]
        == jnp.arange(block_size, dtype=jnp.int32)[None]
    ).astype(jnp.float32)
    pair_keep = live[:, None, None] * (1.0 - same[:, None, None] * eye[None])
    pos_blocks = jnp.moveaxis(src_pos.reshape(3, src_blocks, block_size), 1, 0)
    pos_rows = lax.dynamic_slice_in_dim(pos_blocks, row_low, rows, 2)
    feat_blocks = jnp.moveaxis(full_feat.reshape(all_chan, src_blocks, block_size), 1, 0)
    target_pos = jnp.take(pos_rows, target_idx, axis=0, mode="clip")
    source_pos = jnp.take(pos_blocks, source_idx, axis=0, mode="clip")
    source_feat = jnp.take(feat_blocks, source_idx, axis=0, mode="clip")

    def geo_fn(first_pos, second_pos):
        return geometry(first_pos, second_pos, pair_keep, radial_count)

    (harmonics, radial), pullback = jax.vjp(geo_fn, target_pos, source_pos)
    pair_values = (harmonics[:, None] * radial[None]).astype(jnp.bfloat16)
    routed_feat = (
        target_hot[:, :own_blocks, None, None] * source_feat[:, None].astype(jnp.float32)
    ).astype(jnp.bfloat16)
    msg_acc = jnp.einsum(
        "lktij,tbcj->bclki", pair_values, routed_feat, preferred_element_type=jnp.float32
    )
    moments = jnp.einsum("bclki,ck->clbi", msg_acc, full_weight)
    packed = moments.astype(jnp.bfloat16)
    mixing = jnp.take(mix_weight, jnp.array(ORDER_OF, dtype=jnp.int32), axis=0)
    offset = chan_index * chan_dev
    mixed_out = jnp.einsum(
        "lxc,clbi->xlbi", mixing, packed, preferred_element_type=jnp.float32
    )
    scalar_part = mixed_out[:, 0]
    gate_value = jax.nn.sigmoid(scalar_part)
    result_rows = jnp.concatenate(
        [(scalar_part * gate_value)[:, None], mixed_out[:, 1:] * gate_value[:, None]],
        axis=1,
    ).astype(jnp.bfloat16)
    result = lax.all_to_all(
        result_rows.reshape(all_chan, components, own_blocks, 1, rows),
        "chan",
        0,
        3,
        tiled=True,
    ).reshape(chan_dev, components, atoms_dev)
    grad_rows = lax.all_to_all(
        out_grad.reshape(chan_dev, components, own_blocks, chan_count, rows),
        "chan",
        3,
        0,
        tiled=True,
    ).reshape(all_chan, components, own_blocks, rows)
    upstream = grad_rows.astype(jnp.float32)
    scalar_grad = upstream[:, 0] * (
        gate_value * (1.0 + scalar_part * (1.0 - gate_value))
    ) + gate_value * (1.0 - gate_value) * jnp.sum(upstream[:, 1:] * mixed_out[:, 1:], axis=1)
    rest_grad = upstream[:, 1:] * gate_value[:, None]
    dz_packed = jnp.concatenate([scalar_grad[:, None], rest_grad], axis=1).astype(jnp.bfloat16)
    moment_grad_all = jnp.einsum(
        "lxc,xlbi->clbi", mixing, dz_packed, preferred_element_type=jnp.float32
    )
    grad_rad = jnp.einsum("bclki,clbi->ck", msg_acc, moment_grad_all)
    grad_blocks = jnp.moveaxis(moment_grad_all, 2, 0)
    tile_grad = jnp.take(grad_blocks, target_idx, axis=0, mode="clip")
    weighted = (
        live[:, None, None, None, None]
        * full_weight[None, :, None, :, None]
        * tile_grad[:, :, :, None, :]
    ).astype(jnp.bfloat16)
    grad_source = jnp.einsum(
        "tclki,lktij->tcj", weighted, pair_values, preferred_element_type=jnp.float32
    )
    harm_grad, rad_grad = value_grad_sums(weighted, source_feat, radial, harmonics)
    target_grad, source_grad_pos = pullback((harm_grad, rad_grad))
    grad_part = jnp.sum(
        source_hot[:, None, :, None] * grad_source[:, :, None, :], axis=0
    ).reshape(all_chan, src_atoms)
    row_hot = (jnp.arange(chan_count, dtype=jnp.int32) == chan_index).astype(jnp.float32)
    target_part = jnp.sum(target_hot[:, None, :, None] * target_grad[:, :, None, :], axis=0)
    dpos_src = (
        row_hot[None, None, :, None] * target_part[:, :, None, :]
        + jnp.sum(source_hot[:, None, :, None] * source_grad_pos[:, :, None, :], axis=0).reshape(
            3, src_blocks, chan_count, rows
        )
    ).reshape(3, src_atoms)
    grad_src, (dpos_src, grad_rad) = halving_with(grad_part, (dpos_src, grad_rad), "chan")
    grad_rad = lax.dynamic_slice_in_dim(grad_rad, offset, chan_dev, 0)
    own_both = jnp.concatenate([grad_src[:, :atoms_dev], dpos_src[:, :atoms_dev]], axis=0)
    ghost_rows = chan_dev + 3
    back_list = []
    for level_bit in range(levels):
        low = atoms_dev + level_bit * block_size
        ghost_both = jnp.concatenate(
            [
                grad_src[:, low : low + block_size],
                dpos_src[:, low : low + block_size],
                as_rows(grad_rad, block_size),
            ],
            axis=0,
        )
        back_both = partner(ghost_both, "space", level_bit)
        grad_rad = grad_rad + back_both[ghost_rows:].reshape(-1)[: grad_rad.size].reshape(
            grad_rad.shape
        )
        back_list.append(back_both[:ghost_rows])
    all_rows = send_rows[:levels].reshape(-1)
    ghost_hot = (all_rows[:, None] == jnp.arange(atoms_dev, dtype=jnp.int32)[None]).astype(
        jnp.float32
    )
    own_both = own_both + jnp.dot(
        jnp.concatenate(back_list, axis=1), ghost_hot, precision=lax.Precision.HIGHEST
    )
    own_grad = own_both[:chan_dev]
    own_dpos = own_both[chan_dev:]
    return (result, own_grad.astype(jnp.bfloat16), -own_dpos, grad_rad)


def solution(mesh):
    placed = (
        P(None, "space"),
        P("chan", "space"),
        P("space", None),
        P("space", None),
        P("space"),
        P("chan", None),
        P(),
        P("chan", None, "space"),
    )
    return jax.shard_map(
        body,
        mesh=mesh,
        in_specs=placed,
        out_specs=(P("chan", None, "space"), P("chan", "space"), P(None, "space"), P("chan", None)),
        check_vma=False,
    )
```

```python
import math

import jax
import jax.numpy as jnp
from jax import lax
from jax.sharding import PartitionSpec as P

SOFTENING = 0.25
CUTOFF = 2.5
CUTOFF_SQ = 6.25
SHARPNESS = 10.0
ROOT_THREE = math.sqrt(3.0)
ORDER_OF = (0, 1, 1, 1, 2, 2, 2, 2, 2)


def partner(value, axis, bit):
    mask = 2**bit
    pairs = [(source, source ^ mask) for source in range(lax.axis_size(axis))]
    return lax.ppermute(value, axis, pairs)


def halving_sum(value, axis):
    index = lax.axis_index(axis)
    for bit in reversed(range(lax.axis_size(axis).bit_length() - 1)):
        half = value.shape[0] // 2
        mine = (index >> bit) & 1
        keep = lax.dynamic_slice_in_dim(value, mine * half, half, 0)
        give = lax.dynamic_slice_in_dim(value, (1 - mine) * half, half, 0)
        value = keep + partner(give, axis, bit)
    return value


def as_rows(value, width):
    flat = value.reshape(-1)
    count = -(-flat.shape[0] // width)
    return jnp.pad(flat, (0, count * width - flat.shape[0])).reshape(count, width)


def halving_with(value, extras, axis):
    index = lax.axis_index(axis)
    width = value.shape[1]
    extra_rows = as_rows(jnp.concatenate([extra.reshape(-1) for extra in extras]), width)
    count = lax.axis_size(axis)
    chunk = value.shape[0] // count
    for bit in range(count.bit_length() - 1):
        groups = value.reshape(-1, 2, chunk, width)
        mine = (index >> bit) & 1
        keep = lax.dynamic_index_in_dim(groups, mine, 1, keepdims=False).reshape(-1, width)
        give = lax.dynamic_index_in_dim(groups, 1 - mine, 1, keepdims=False).reshape(-1, width)
        half = give.shape[0]
        got = partner(jnp.concatenate([give, extra_rows], axis=0), axis, bit)
        value = keep + got[:half]
        extra_rows = extra_rows + got[half:]
    flat = extra_rows.reshape(-1)
    sums = []
    start = 0
    for extra in extras:
        sums.append(flat[start : start + extra.size].reshape(extra.shape))
        start += extra.size
    return value, sums


def geometry(target_pos, source_pos, pair_keep, radial_count):
    offset = source_pos[:, :, None, :] - target_pos[:, :, :, None]
    dist_sq = jnp.sum(offset * offset, axis=1) + SOFTENING
    distance = jnp.sqrt(dist_sq)
    along_x = offset[:, 0] / distance
    along_y = offset[:, 1] / distance
    along_z = offset[:, 2] / distance
    harmonics = jnp.stack(
        [
            jnp.ones_like(along_x),
            along_x,
            along_y,
            along_z,
            ROOT_THREE * along_x * along_y,
            ROOT_THREE * along_y * along_z,
            ROOT_THREE * along_x * along_z,
            0.5 * (3.0 * along_z * along_z - 1.0),
            0.5 * ROOT_THREE * (along_x * along_x - along_y * along_y),
        ]
    )
    envelope = jnp.square(jnp.maximum(1.0 - dist_sq / CUTOFF_SQ, 0.0)) * pair_keep
    centers = (jnp.arange(radial_count, dtype=jnp.float32) + 0.5) * (CUTOFF / radial_count)
    radial = (
        jnp.exp(-SHARPNESS * jnp.square(distance[None] - centers[:, None, None, None]))
        * envelope[None]
    )
    return (harmonics, radial)


def take_block(array, blk_index, block_size):
    return lax.dynamic_slice_in_dim(array, blk_index * block_size, block_size, array.ndim - 1)


def add_block(array, blk_index, value, block_size):
    current = take_block(array, blk_index, block_size)
    return lax.dynamic_update_slice_in_dim(
        array, current + value, blk_index * block_size, array.ndim - 1
    )


def body(
    positions, features, send_rows, pair_tiles, tile_live, radial_weight, mix_weight, out_grad
):
    block_size = send_rows.shape[1]
    atoms_dev = positions.shape[1]
    chan_dev = features.shape[0]
    radial_count = radial_weight.shape[1]
    components = out_grad.shape[1]
    levels = lax.axis_size("space").bit_length() - 1
    chan_count = lax.axis_size("chan")
    chan_index = lax.axis_index("chan")
    pos_list = [positions]
    feat_list = [features]
    send_hot = (
        jnp.arange(atoms_dev, dtype=jnp.int32)[:, None] == send_rows[:levels].reshape(1, -1)
    ).astype(jnp.float32)
    both_rows = jnp.dot(
        jnp.concatenate([features.astype(jnp.float32), positions], axis=0),
        send_hot,
        precision=lax.Precision.HIGHEST,
    )
    for level_bit in range(levels):
        got_both = partner(
            both_rows[:, level_bit * block_size : (level_bit + 1) * block_size],
            "space",
            level_bit,
        )
        feat_list.append(got_both[:chan_dev].astype(jnp.bfloat16))
        pos_list.append(got_both[chan_dev:])
    src_pos = jnp.concatenate(pos_list, axis=1)
    src_feat = jnp.concatenate(feat_list, axis=1)
    src_atoms = src_pos.shape[1]
    weight_high = radial_weight.astype(jnp.bfloat16)
    weight_rest = radial_weight - weight_high.astype(jnp.float32)
    weight_mid = weight_rest.astype(jnp.bfloat16)
    weight_low = (weight_rest - weight_mid.astype(jnp.float32)).astype(jnp.bfloat16)
    full_both = lax.all_gather(
        jnp.concatenate([src_feat, weight_high, weight_mid, weight_low], axis=1),
        "chan",
        axis=0,
        tiled=True,
    )
    full_feat = full_both[:, :src_atoms]
    pieces = full_both[:, src_atoms:].astype(jnp.float32)
    full_weight = (
        pieces[:, :radial_count] + pieces[:, radial_count : 2 * radial_count]
    ) + pieces[:, 2 * radial_count :]
    all_chan = full_feat.shape[0]
    src_blocks = src_atoms // block_size
    own_blocks = atoms_dev // block_size
    rows = block_size // chan_count
    row_low = chan_index * rows
    target_idx = pair_tiles[:, 0]
    source_idx = pair_tiles[:, 1]
    live = tile_live.astype(jnp.float32)
    block_ids = jnp.arange(src_blocks, dtype=jnp.int32)
    target_hot = (target_idx[:, None] == block_ids[None]).astype(jnp.float32) * live[:, None]
    source_hot = (source_idx[:, None] == block_ids[None]).astype(jnp.float32) * live[:, None]
    same = (target_idx == source_idx).astype(jnp.float32)
    eye = (
        (row_low + jnp.arange(rows, dtype=jnp.int32))[:, None]
        == jnp.arange(block_size, dtype=jnp.int32)[None]
    ).astype(jnp.float32)
    pair_keep = live[:, None, None] * (1.0 - same[:, None, None] * eye[None])
    pos_blocks = jnp.moveaxis(src_pos.reshape(3, src_blocks, block_size), 1, 0)
    pos_rows = lax.dynamic_slice_in_dim(pos_blocks, row_low, rows, 2)
    feat_blocks = jnp.moveaxis(full_feat.reshape(all_chan, src_blocks, block_size), 1, 0)
    target_pos = jnp.take(pos_rows, target_idx, axis=0, mode="clip")
    source_pos = jnp.take(pos_blocks, source_idx, axis=0, mode="clip")
    source_feat = jnp.take(feat_blocks, source_idx, axis=0, mode="clip")

    def geo_fn(first_pos, second_pos):
        return geometry(first_pos, second_pos, pair_keep, radial_count)

    (harmonics, radial), pullback = jax.vjp(geo_fn, target_pos, source_pos)
    pair_values = (harmonics[:, None] * radial[None]).astype(jnp.bfloat16)
    routed_feat = (
        target_hot[:, :own_blocks, None, None] * source_feat[:, None].astype(jnp.float32)
    ).astype(jnp.bfloat16)
    msg_acc = jnp.einsum(
        "lktij,tbcj->bclki", pair_values, routed_feat, preferred_element_type=jnp.float32
    )
    moments = jnp.einsum("bclki,ck->clbi", msg_acc, full_weight)
    packed = moments.astype(jnp.bfloat16)
    mixing = jnp.take(mix_weight, jnp.array(ORDER_OF, dtype=jnp.int32), axis=0)
    offset = chan_index * chan_dev
    mixed_out = jnp.einsum(
        "lxc,clbi->xlbi", mixing, packed, preferred_element_type=jnp.float32
    )
    scalar_part = mixed_out[:, 0]
    gate_value = jax.nn.sigmoid(scalar_part)
    result_rows = jnp.concatenate(
        [(scalar_part * gate_value)[:, None], mixed_out[:, 1:] * gate_value[:, None]],
        axis=1,
    ).astype(jnp.bfloat16)
    result = lax.all_to_all(
        result_rows.reshape(all_chan, components, own_blocks, 1, rows),
        "chan",
        0,
        3,
        tiled=True,
    ).reshape(chan_dev, components, atoms_dev)
    grad_rows = lax.all_to_all(
        out_grad.reshape(chan_dev, components, own_blocks, chan_count, rows),
        "chan",
        3,
        0,
        tiled=True,
    ).reshape(all_chan, components, own_blocks, rows)
    upstream = grad_rows.astype(jnp.float32)
    scalar_grad = upstream[:, 0] * (
        gate_value * (1.0 + scalar_part * (1.0 - gate_value))
    ) + gate_value * (1.0 - gate_value) * jnp.sum(upstream[:, 1:] * mixed_out[:, 1:], axis=1)
    rest_grad = upstream[:, 1:] * gate_value[:, None]
    dz_packed = jnp.concatenate([scalar_grad[:, None], rest_grad], axis=1).astype(jnp.bfloat16)
    moment_grad_all = jnp.einsum(
        "lxc,xlbi->clbi", mixing, dz_packed, preferred_element_type=jnp.float32
    )
    grad_rad = jnp.einsum("bclki,clbi->ck", msg_acc, moment_grad_all)
    grad_blocks = jnp.moveaxis(moment_grad_all, 2, 0)
    tile_grad = jnp.take(grad_blocks, target_idx, axis=0, mode="clip")
    weighted = (
        live[:, None, None, None, None]
        * full_weight[None, :, None, :, None]
        * tile_grad[:, :, :, None, :]
    ).astype(jnp.bfloat16)
    grad_source = jnp.einsum(
        "tclki,lktij->tcj", weighted, pair_values, preferred_element_type=jnp.float32
    )
    value_grad = jnp.einsum(
        "tclki,tcj->lktij", weighted, source_feat, preferred_element_type=jnp.float32
    )
    harm_grad = jnp.sum(value_grad * radial[None], axis=1)
    rad_grad = jnp.sum(value_grad * harmonics[:, None], axis=0)
    target_grad, source_grad_pos = pullback((harm_grad, rad_grad))
    grad_part = jnp.sum(
        source_hot[:, None, :, None] * grad_source[:, :, None, :], axis=0
    ).reshape(all_chan, src_atoms)
    row_hot = (jnp.arange(chan_count, dtype=jnp.int32) == chan_index).astype(jnp.float32)
    target_part = jnp.sum(target_hot[:, None, :, None] * target_grad[:, :, None, :], axis=0)
    dpos_src = (
        row_hot[None, None, :, None] * target_part[:, :, None, :]
        + jnp.sum(source_hot[:, None, :, None] * source_grad_pos[:, :, None, :], axis=0).reshape(
            3, src_blocks, chan_count, rows
        )
    ).reshape(3, src_atoms)
    grad_src, (dpos_src, grad_rad) = halving_with(grad_part, (dpos_src, grad_rad), "chan")
    grad_rad = lax.dynamic_slice_in_dim(grad_rad, offset, chan_dev, 0)
    own_both = jnp.concatenate([grad_src[:, :atoms_dev], dpos_src[:, :atoms_dev]], axis=0)
    ghost_rows = chan_dev + 3
    back_list = []
    for level_bit in range(levels):
        low = atoms_dev + level_bit * block_size
        ghost_both = jnp.concatenate(
            [
                grad_src[:, low : low + block_size],
                dpos_src[:, low : low + block_size],
                as_rows(grad_rad, block_size),
            ],
            axis=0,
        )
        back_both = partner(ghost_both, "space", level_bit)
        grad_rad = grad_rad + back_both[ghost_rows:].reshape(-1)[: grad_rad.size].reshape(
            grad_rad.shape
        )
        back_list.append(back_both[:ghost_rows])
    all_rows = send_rows[:levels].reshape(-1)
    ghost_hot = (all_rows[:, None] == jnp.arange(atoms_dev, dtype=jnp.int32)[None]).astype(
        jnp.float32
    )
    own_both = own_both + jnp.dot(
        jnp.concatenate(back_list, axis=1), ghost_hot, precision=lax.Precision.HIGHEST
    )
    own_grad = own_both[:chan_dev]
    own_dpos = own_both[chan_dev:]
    return (result, own_grad.astype(jnp.bfloat16), -own_dpos, grad_rad)


def solution(mesh):
    placed = (
        P(None, "space"),
        P("chan", "space"),
        P("space", None),
        P("space", None),
        P("space"),
        P("chan", None),
        P(),
        P("chan", None, "space"),
    )
    return jax.shard_map(
        body,
        mesh=mesh,
        in_specs=placed,
        out_specs=(P("chan", None, "space"), P("chan", "space"), P(None, "space"), P("chan", None)),
        check_vma=False,
    )
```

```python
import math

import jax
import jax.numpy as jnp
from jax import lax
from jax.sharding import PartitionSpec as P

SOFTENING = 0.25
CUTOFF = 2.5
CUTOFF_SQ = 6.25
SHARPNESS = 10.0
ROOT_THREE = math.sqrt(3.0)
ORDER_OF = (0, 1, 1, 1, 2, 2, 2, 2, 2)


def partner(value, axis, bit):
    mask = 2**bit
    pairs = [(source, source ^ mask) for source in range(lax.axis_size(axis))]
    return lax.ppermute(value, axis, pairs)


def halving_sum(value, axis):
    index = lax.axis_index(axis)
    for bit in reversed(range(lax.axis_size(axis).bit_length() - 1)):
        half = value.shape[0] // 2
        mine = (index >> bit) & 1
        keep = lax.dynamic_slice_in_dim(value, mine * half, half, 0)
        give = lax.dynamic_slice_in_dim(value, (1 - mine) * half, half, 0)
        value = keep + partner(give, axis, bit)
    return value


def as_rows(value, width):
    flat = value.reshape(-1)
    count = -(-flat.shape[0] // width)
    return jnp.pad(flat, (0, count * width - flat.shape[0])).reshape(count, width)


def halving_with(value, extras, axis):
    index = lax.axis_index(axis)
    width = value.shape[1]
    extra_rows = as_rows(jnp.concatenate([extra.reshape(-1) for extra in extras]), width)
    count = lax.axis_size(axis)
    chunk = value.shape[0] // count
    for bit in range(count.bit_length() - 1):
        groups = value.reshape(-1, 2, chunk, width)
        mine = (index >> bit) & 1
        keep = lax.dynamic_index_in_dim(groups, mine, 1, keepdims=False).reshape(-1, width)
        give = lax.dynamic_index_in_dim(groups, 1 - mine, 1, keepdims=False).reshape(-1, width)
        half = give.shape[0]
        got = partner(jnp.concatenate([give, extra_rows], axis=0), axis, bit)
        value = keep + got[:half]
        extra_rows = extra_rows + got[half:]
    flat = extra_rows.reshape(-1)
    sums = []
    start = 0
    for extra in extras:
        sums.append(flat[start : start + extra.size].reshape(extra.shape))
        start += extra.size
    return value, sums


def geometry(target_pos, source_pos, pair_keep, radial_count):
    offset = source_pos[:, :, None, :] - target_pos[:, :, :, None]
    dist_sq = jnp.sum(offset * offset, axis=1) + SOFTENING
    distance = jnp.sqrt(dist_sq)
    along_x = offset[:, 0] / distance
    along_y = offset[:, 1] / distance
    along_z = offset[:, 2] / distance
    harmonics = jnp.stack(
        [
            jnp.ones_like(along_x),
            along_x,
            along_y,
            along_z,
            ROOT_THREE * along_x * along_y,
            ROOT_THREE * along_y * along_z,
            ROOT_THREE * along_x * along_z,
            0.5 * (3.0 * along_z * along_z - 1.0),
            0.5 * ROOT_THREE * (along_x * along_x - along_y * along_y),
        ]
    )
    envelope = jnp.square(jnp.maximum(1.0 - dist_sq / CUTOFF_SQ, 0.0)) * pair_keep
    centers = (jnp.arange(radial_count, dtype=jnp.float32) + 0.5) * (CUTOFF / radial_count)
    radial = (
        jnp.exp(-SHARPNESS * jnp.square(distance[None] - centers[:, None, None, None]))
        * envelope[None]
    )
    return (harmonics, radial)


def take_block(array, blk_index, block_size):
    return lax.dynamic_slice_in_dim(array, blk_index * block_size, block_size, array.ndim - 1)


def add_block(array, blk_index, value, block_size):
    current = take_block(array, blk_index, block_size)
    return lax.dynamic_update_slice_in_dim(
        array, current + value, blk_index * block_size, array.ndim - 1
    )


def body(
    positions, features, send_rows, pair_tiles, tile_live, radial_weight, mix_weight, out_grad
):
    block_size = send_rows.shape[1]
    atoms_dev = positions.shape[1]
    chan_dev = features.shape[0]
    radial_count = radial_weight.shape[1]
    components = out_grad.shape[1]
    levels = lax.axis_size("space").bit_length() - 1
    chan_count = lax.axis_size("chan")
    chan_index = lax.axis_index("chan")
    pos_list = [positions]
    feat_list = [features]
    send_hot = (
        jnp.arange(atoms_dev, dtype=jnp.int32)[:, None] == send_rows[:levels].reshape(1, -1)
    ).astype(jnp.float32)
    both_rows = jnp.dot(
        jnp.concatenate([features.astype(jnp.float32), positions], axis=0),
        send_hot,
        precision=lax.Precision.HIGHEST,
    )
    for level_bit in range(levels):
        got_both = partner(
            both_rows[:, level_bit * block_size : (level_bit + 1) * block_size],
            "space",
            level_bit,
        )
        feat_list.append(got_both[:chan_dev].astype(jnp.bfloat16))
        pos_list.append(got_both[chan_dev:])
    src_pos = jnp.concatenate(pos_list, axis=1)
    src_feat = jnp.concatenate(feat_list, axis=1)
    src_atoms = src_pos.shape[1]
    weight_high = radial_weight.astype(jnp.bfloat16)
    weight_rest = radial_weight - weight_high.astype(jnp.float32)
    weight_mid = weight_rest.astype(jnp.bfloat16)
    weight_low = (weight_rest - weight_mid.astype(jnp.float32)).astype(jnp.bfloat16)
    full_both = lax.all_gather(
        jnp.concatenate([src_feat, weight_high, weight_mid, weight_low], axis=1),
        "chan",
        axis=0,
        tiled=True,
    )
    full_feat = full_both[:, :src_atoms]
    pieces = full_both[:, src_atoms:].astype(jnp.float32)
    full_weight = (
        pieces[:, :radial_count] + pieces[:, radial_count : 2 * radial_count]
    ) + pieces[:, 2 * radial_count :]
    all_chan = full_feat.shape[0]
    src_blocks = src_atoms // block_size
    own_blocks = atoms_dev // block_size
    rows = block_size // chan_count
    row_low = chan_index * rows
    target_idx = pair_tiles[:, 0]
    source_idx = pair_tiles[:, 1]
    live = tile_live.astype(jnp.float32)
    block_ids = jnp.arange(src_blocks, dtype=jnp.int32)
    target_hot = (target_idx[:, None] == block_ids[None]).astype(jnp.float32) * live[:, None]
    source_hot = (source_idx[:, None] == block_ids[None]).astype(jnp.float32) * live[:, None]
    same = (target_idx == source_idx).astype(jnp.float32)
    eye = (
        (row_low + jnp.arange(rows, dtype=jnp.int32))[:, None]
        == jnp.arange(block_size, dtype=jnp.int32)[None]
    ).astype(jnp.float32)
    pair_keep = live[:, None, None] * (1.0 - same[:, None, None] * eye[None])
    pos_blocks = jnp.moveaxis(src_pos.reshape(3, src_blocks, block_size), 1, 0)
    pos_rows = lax.dynamic_slice_in_dim(pos_blocks, row_low, rows, 2)
    feat_blocks = jnp.moveaxis(full_feat.reshape(all_chan, src_blocks, block_size), 1, 0)
    target_pick = (target_idx[:, None] == block_ids[None]).astype(jnp.float32)
    source_pick = (source_idx[:, None] == block_ids[None]).astype(jnp.float32)
    exact = lax.Precision.HIGHEST
    target_pos = jnp.einsum("ts,sdr->tdr", target_pick, pos_rows, precision=exact)
    source_pos = jnp.einsum("ts,sdb->tdb", source_pick, pos_blocks, precision=exact)
    source_feat = jnp.einsum(
        "ts,scb->tcb",
        source_pick.astype(jnp.bfloat16),
        feat_blocks,
        preferred_element_type=jnp.float32,
    ).astype(jnp.bfloat16)

    def geo_fn(first_pos, second_pos):
        return geometry(first_pos, second_pos, pair_keep, radial_count)

    (harmonics, radial), pullback = jax.vjp(geo_fn, target_pos, source_pos)
    pair_values = (harmonics[:, None] * radial[None]).astype(jnp.bfloat16)
    routed_feat = (
        target_hot[:, :own_blocks, None, None] * source_feat[:, None].astype(jnp.float32)
    ).astype(jnp.bfloat16)
    msg_acc = jnp.einsum(
        "lktij,tbcj->bclki", pair_values, routed_feat, preferred_element_type=jnp.float32
    )
    moments = jnp.einsum("bclki,ck->clbi", msg_acc, full_weight)
    packed = moments.astype(jnp.bfloat16)
    mixing = jnp.take(mix_weight, jnp.array(ORDER_OF, dtype=jnp.int32), axis=0)
    offset = chan_index * chan_dev
    mixed_out = jnp.einsum(
        "lxc,clbi->xlbi", mixing, packed, preferred_element_type=jnp.float32
    )
    scalar_part = mixed_out[:, 0]
    gate_value = jax.nn.sigmoid(scalar_part)
    result_rows = jnp.concatenate(
        [(scalar_part * gate_value)[:, None], mixed_out[:, 1:] * gate_value[:, None]],
        axis=1,
    ).astype(jnp.bfloat16)
    result = lax.all_to_all(
        result_rows.reshape(all_chan, components, own_blocks, 1, rows),
        "chan",
        0,
        3,
        tiled=True,
    ).reshape(chan_dev, components, atoms_dev)
    grad_rows = lax.all_to_all(
        out_grad.reshape(chan_dev, components, own_blocks, chan_count, rows),
        "chan",
        3,
        0,
        tiled=True,
    ).reshape(all_chan, components, own_blocks, rows)
    upstream = grad_rows.astype(jnp.float32)
    scalar_grad = upstream[:, 0] * (
        gate_value * (1.0 + scalar_part * (1.0 - gate_value))
    ) + gate_value * (1.0 - gate_value) * jnp.sum(upstream[:, 1:] * mixed_out[:, 1:], axis=1)
    rest_grad = upstream[:, 1:] * gate_value[:, None]
    dz_packed = jnp.concatenate([scalar_grad[:, None], rest_grad], axis=1).astype(jnp.bfloat16)
    moment_grad_all = jnp.einsum(
        "lxc,xlbi->clbi", mixing, dz_packed, preferred_element_type=jnp.float32
    )
    grad_rad = jnp.einsum("bclki,clbi->ck", msg_acc, moment_grad_all)
    grad_blocks = jnp.moveaxis(moment_grad_all, 2, 0)
    tile_grad = jnp.einsum(
        "tb,bcli->tcli", target_pick[:, :own_blocks], grad_blocks, precision=exact
    )
    weighted = (
        live[:, None, None, None, None]
        * full_weight[None, :, None, :, None]
        * tile_grad[:, :, :, None, :]
    ).astype(jnp.bfloat16)
    grad_source = jnp.einsum(
        "tclki,lktij->tcj", weighted, pair_values, preferred_element_type=jnp.float32
    )
    value_grad = jnp.einsum(
        "tclki,tcj->lktij", weighted, source_feat, preferred_element_type=jnp.float32
    )
    harm_grad = jnp.sum(value_grad * radial[None], axis=1)
    rad_grad = jnp.sum(value_grad * harmonics[:, None], axis=0)
    target_grad, source_grad_pos = pullback((harm_grad, rad_grad))
    grad_part = jnp.sum(
        source_hot[:, None, :, None] * grad_source[:, :, None, :], axis=0
    ).reshape(all_chan, src_atoms)
    row_hot = (jnp.arange(chan_count, dtype=jnp.int32) == chan_index).astype(jnp.float32)
    target_part = jnp.sum(target_hot[:, None, :, None] * target_grad[:, :, None, :], axis=0)
    dpos_src = (
        row_hot[None, None, :, None] * target_part[:, :, None, :]
        + jnp.sum(source_hot[:, None, :, None] * source_grad_pos[:, :, None, :], axis=0).reshape(
            3, src_blocks, chan_count, rows
        )
    ).reshape(3, src_atoms)
    grad_src, (dpos_src, grad_rad) = halving_with(grad_part, (dpos_src, grad_rad), "chan")
    grad_rad = lax.dynamic_slice_in_dim(grad_rad, offset, chan_dev, 0)
    own_both = jnp.concatenate([grad_src[:, :atoms_dev], dpos_src[:, :atoms_dev]], axis=0)
    ghost_rows = chan_dev + 3
    back_list = []
    for level_bit in range(levels):
        low = atoms_dev + level_bit * block_size
        ghost_both = jnp.concatenate(
            [
                grad_src[:, low : low + block_size],
                dpos_src[:, low : low + block_size],
                as_rows(grad_rad, block_size),
            ],
            axis=0,
        )
        back_both = partner(ghost_both, "space", level_bit)
        grad_rad = grad_rad + back_both[ghost_rows:].reshape(-1)[: grad_rad.size].reshape(
            grad_rad.shape
        )
        back_list.append(back_both[:ghost_rows])
    all_rows = send_rows[:levels].reshape(-1)
    ghost_hot = (all_rows[:, None] == jnp.arange(atoms_dev, dtype=jnp.int32)[None]).astype(
        jnp.float32
    )
    own_both = own_both + jnp.dot(
        jnp.concatenate(back_list, axis=1), ghost_hot, precision=lax.Precision.HIGHEST
    )
    own_grad = own_both[:chan_dev]
    own_dpos = own_both[chan_dev:]
    return (result, own_grad.astype(jnp.bfloat16), -own_dpos, grad_rad)


def solution(mesh):
    placed = (
        P(None, "space"),
        P("chan", "space"),
        P("space", None),
        P("space", None),
        P("space"),
        P("chan", None),
        P(),
        P("chan", None, "space"),
    )
    return jax.shard_map(
        body,
        mesh=mesh,
        in_specs=placed,
        out_specs=(P("chan", None, "space"), P("chan", "space"), P(None, "space"), P("chan", None)),
        check_vma=False,
    )
```

```python
import math

import jax
import jax.numpy as jnp
from jax import lax
from jax.sharding import PartitionSpec as P

SOFTENING = 0.25
CUTOFF = 2.5
CUTOFF_SQ = 6.25
SHARPNESS = 10.0
ROOT_THREE = math.sqrt(3.0)
ORDER_OF = (0, 1, 1, 1, 2, 2, 2, 2, 2)


def partner(value, axis, bit):
    mask = 2**bit
    pairs = [(source, source ^ mask) for source in range(lax.axis_size(axis))]
    return lax.ppermute(value, axis, pairs)


def halving_sum(value, axis):
    index = lax.axis_index(axis)
    for bit in reversed(range(lax.axis_size(axis).bit_length() - 1)):
        half = value.shape[0] // 2
        mine = (index >> bit) & 1
        keep = lax.dynamic_slice_in_dim(value, mine * half, half, 0)
        give = lax.dynamic_slice_in_dim(value, (1 - mine) * half, half, 0)
        value = keep + partner(give, axis, bit)
    return value


def as_rows(value, width):
    flat = value.reshape(-1)
    count = -(-flat.shape[0] // width)
    return jnp.pad(flat, (0, count * width - flat.shape[0])).reshape(count, width)


def halving_with(value, extras, axis):
    index = lax.axis_index(axis)
    width = value.shape[1]
    extra_rows = as_rows(jnp.concatenate([extra.reshape(-1) for extra in extras]), width)
    count = lax.axis_size(axis)
    chunk = value.shape[0] // count
    for bit in range(count.bit_length() - 1):
        groups = value.reshape(-1, 2, chunk, width)
        mine = (index >> bit) & 1
        keep = lax.dynamic_index_in_dim(groups, mine, 1, keepdims=False).reshape(-1, width)
        give = lax.dynamic_index_in_dim(groups, 1 - mine, 1, keepdims=False).reshape(-1, width)
        half = give.shape[0]
        got = partner(jnp.concatenate([give, extra_rows], axis=0), axis, bit)
        value = keep + got[:half]
        extra_rows = extra_rows + got[half:]
    flat = extra_rows.reshape(-1)
    sums = []
    start = 0
    for extra in extras:
        sums.append(flat[start : start + extra.size].reshape(extra.shape))
        start += extra.size
    return value, sums


def geometry(target_pos, source_pos, pair_keep, radial_count):
    offset = source_pos[:, :, None, :] - target_pos[:, :, :, None]
    dist_sq = jnp.sum(offset * offset, axis=1) + SOFTENING
    distance = jnp.sqrt(dist_sq)
    along_x = offset[:, 0] / distance
    along_y = offset[:, 1] / distance
    along_z = offset[:, 2] / distance
    harmonics = jnp.stack(
        [
            jnp.ones_like(along_x),
            along_x,
            along_y,
            along_z,
            ROOT_THREE * along_x * along_y,
            ROOT_THREE * along_y * along_z,
            ROOT_THREE * along_x * along_z,
            0.5 * (3.0 * along_z * along_z - 1.0),
            0.5 * ROOT_THREE * (along_x * along_x - along_y * along_y),
        ]
    )
    envelope = jnp.square(jnp.maximum(1.0 - dist_sq / CUTOFF_SQ, 0.0)) * pair_keep
    centers = (jnp.arange(radial_count, dtype=jnp.float32) + 0.5) * (CUTOFF / radial_count)
    radial = (
        jnp.exp(-SHARPNESS * jnp.square(distance[None] - centers[:, None, None, None]))
        * envelope[None]
    )
    return (harmonics, radial)


def take_block(array, blk_index, block_size):
    return lax.dynamic_slice_in_dim(array, blk_index * block_size, block_size, array.ndim - 1)


def add_block(array, blk_index, value, block_size):
    current = take_block(array, blk_index, block_size)
    return lax.dynamic_update_slice_in_dim(
        array, current + value, blk_index * block_size, array.ndim - 1
    )


def body(
    positions, features, send_rows, pair_tiles, tile_live, radial_weight, mix_weight, out_grad
):
    block_size = send_rows.shape[1]
    atoms_dev = positions.shape[1]
    chan_dev = features.shape[0]
    radial_count = radial_weight.shape[1]
    components = out_grad.shape[1]
    levels = lax.axis_size("space").bit_length() - 1
    chan_count = lax.axis_size("chan")
    chan_index = lax.axis_index("chan")
    pos_list = [positions]
    feat_list = [features]
    send_hot = (
        jnp.arange(atoms_dev, dtype=jnp.int32)[:, None] == send_rows[:levels].reshape(1, -1)
    ).astype(jnp.float32)
    both_rows = jnp.dot(
        jnp.concatenate([features.astype(jnp.float32), positions], axis=0),
        send_hot,
        precision=lax.Precision.HIGHEST,
    )
    for level_bit in range(levels):
        got_both = partner(
            both_rows[:, level_bit * block_size : (level_bit + 1) * block_size],
            "space",
            level_bit,
        )
        feat_list.append(got_both[:chan_dev].astype(jnp.bfloat16))
        pos_list.append(got_both[chan_dev:])
    src_pos = jnp.concatenate(pos_list, axis=1)
    src_feat = jnp.concatenate(feat_list, axis=1)
    src_atoms = src_pos.shape[1]
    weight_high = radial_weight.astype(jnp.bfloat16)
    weight_rest = radial_weight - weight_high.astype(jnp.float32)
    weight_mid = weight_rest.astype(jnp.bfloat16)
    weight_low = (weight_rest - weight_mid.astype(jnp.float32)).astype(jnp.bfloat16)
    full_both = lax.all_gather(
        jnp.concatenate([src_feat, weight_high, weight_mid, weight_low], axis=1),
        "chan",
        axis=0,
        tiled=True,
    )
    full_feat = full_both[:, :src_atoms]
    pieces = full_both[:, src_atoms:].astype(jnp.float32)
    full_weight = (
        pieces[:, :radial_count] + pieces[:, radial_count : 2 * radial_count]
    ) + pieces[:, 2 * radial_count :]
    all_chan = full_feat.shape[0]
    src_blocks = src_atoms // block_size
    own_blocks = atoms_dev // block_size
    rows = block_size // chan_count
    row_low = chan_index * rows
    target_idx = pair_tiles[:, 0]
    source_idx = pair_tiles[:, 1]
    live = tile_live.astype(jnp.float32)
    block_ids = jnp.arange(src_blocks, dtype=jnp.int32)
    target_hot = (target_idx[:, None] == block_ids[None]).astype(jnp.float32) * live[:, None]
    source_hot = (source_idx[:, None] == block_ids[None]).astype(jnp.float32) * live[:, None]
    same = (target_idx == source_idx).astype(jnp.float32)
    eye = (
        (row_low + jnp.arange(rows, dtype=jnp.int32))[:, None]
        == jnp.arange(block_size, dtype=jnp.int32)[None]
    ).astype(jnp.float32)
    pair_keep = live[:, None, None] * (1.0 - same[:, None, None] * eye[None])
    pos_blocks = jnp.moveaxis(src_pos.reshape(3, src_blocks, block_size), 1, 0)
    pos_rows = lax.dynamic_slice_in_dim(pos_blocks, row_low, rows, 2)
    feat_blocks = jnp.moveaxis(full_feat.reshape(all_chan, src_blocks, block_size), 1, 0)
    target_pos = jnp.take(pos_rows, target_idx, axis=0, mode="clip")
    source_pos = jnp.take(pos_blocks, source_idx, axis=0, mode="clip")
    source_feat = jnp.take(feat_blocks, source_idx, axis=0, mode="clip")

    def geo_fn(first_pos, second_pos):
        return geometry(first_pos, second_pos, pair_keep, radial_count)

    (harmonics, radial), pullback = jax.vjp(geo_fn, target_pos, source_pos)
    pair_values = (harmonics[:, None] * radial[None]).astype(jnp.bfloat16)
    routed_feat = (
        target_hot[:, :own_blocks, None, None] * source_feat[:, None].astype(jnp.float32)
    ).astype(jnp.bfloat16)
    msg_acc = jnp.einsum(
        "lktij,tbcj->bclki", pair_values, routed_feat, preferred_element_type=jnp.float32
    )
    moments = jnp.einsum("bclki,ck->clbi", msg_acc, full_weight)
    packed = moments.astype(jnp.bfloat16)
    mixing = jnp.take(mix_weight, jnp.array(ORDER_OF, dtype=jnp.int32), axis=0)
    offset = chan_index * chan_dev
    mixed_out = jnp.einsum(
        "lxc,clbi->xlbi", mixing, packed, preferred_element_type=jnp.float32
    )
    scalar_part = mixed_out[:, 0]
    gate_value = jax.nn.sigmoid(scalar_part)
    result_rows = jnp.concatenate(
        [(scalar_part * gate_value)[:, None], mixed_out[:, 1:] * gate_value[:, None]],
        axis=1,
    ).astype(jnp.bfloat16)
    result = lax.all_to_all(
        result_rows.reshape(all_chan, components, own_blocks, 1, rows),
        "chan",
        0,
        3,
        tiled=True,
    ).reshape(chan_dev, components, atoms_dev)
    grad_rows = lax.all_to_all(
        out_grad.reshape(chan_dev, components, own_blocks, chan_count, rows),
        "chan",
        3,
        0,
        tiled=True,
    ).reshape(all_chan, components, own_blocks, rows)
    upstream = grad_rows.astype(jnp.float32)
    scalar_grad = upstream[:, 0] * (
        gate_value * (1.0 + scalar_part * (1.0 - gate_value))
    ) + gate_value * (1.0 - gate_value) * jnp.sum(upstream[:, 1:] * mixed_out[:, 1:], axis=1)
    rest_grad = upstream[:, 1:] * gate_value[:, None]
    dz_packed = jnp.concatenate([scalar_grad[:, None], rest_grad], axis=1).astype(jnp.bfloat16)
    moment_grad_all = jnp.einsum(
        "lxc,xlbi->clbi", mixing, dz_packed, preferred_element_type=jnp.float32
    )
    grad_rad = jnp.einsum("bclki,clbi->ck", msg_acc, moment_grad_all)
    for level_bit in range(levels):
        grad_rad = grad_rad + partner(grad_rad, "space", level_bit)
    grad_blocks = jnp.moveaxis(moment_grad_all, 2, 0)
    tile_grad = jnp.take(grad_blocks, target_idx, axis=0, mode="clip")
    weighted = (
        live[:, None, None, None, None]
        * full_weight[None, :, None, :, None]
        * tile_grad[:, :, :, None, :]
    ).astype(jnp.bfloat16)
    grad_source = jnp.einsum(
        "tclki,lktij->tcj", weighted, pair_values, preferred_element_type=jnp.float32
    )
    value_grad = jnp.einsum(
        "tclki,tcj->lktij", weighted, source_feat, preferred_element_type=jnp.float32
    )
    harm_grad = jnp.sum(value_grad * radial[None], axis=1)
    rad_grad = jnp.sum(value_grad * harmonics[:, None], axis=0)
    target_grad, source_grad_pos = pullback((harm_grad, rad_grad))
    grad_part = jnp.sum(
        source_hot[:, None, :, None] * grad_source[:, :, None, :], axis=0
    ).reshape(all_chan, src_atoms)
    row_hot = (jnp.arange(chan_count, dtype=jnp.int32) == chan_index).astype(jnp.float32)
    target_part = jnp.sum(target_hot[:, None, :, None] * target_grad[:, :, None, :], axis=0)
    dpos_src = (
        row_hot[None, None, :, None] * target_part[:, :, None, :]
        + jnp.sum(source_hot[:, None, :, None] * source_grad_pos[:, :, None, :], axis=0).reshape(
            3, src_blocks, chan_count, rows
        )
    ).reshape(3, src_atoms)
    grad_src, (dpos_src, grad_rad) = halving_with(grad_part, (dpos_src, grad_rad), "chan")
    grad_rad = lax.dynamic_slice_in_dim(grad_rad, offset, chan_dev, 0)
    own_both = jnp.concatenate([grad_src[:, :atoms_dev], dpos_src[:, :atoms_dev]], axis=0)
    back_list = []
    for level_bit in range(levels):
        low = atoms_dev + level_bit * block_size
        ghost_both = jnp.concatenate(
            [grad_src[:, low : low + block_size], dpos_src[:, low : low + block_size]], axis=0
        )
        back_list.append(partner(ghost_both, "space", level_bit))
    all_rows = send_rows[:levels].reshape(-1)
    ghost_hot = (all_rows[:, None] == jnp.arange(atoms_dev, dtype=jnp.int32)[None]).astype(
        jnp.float32
    )
    own_both = own_both + jnp.dot(
        jnp.concatenate(back_list, axis=1), ghost_hot, precision=lax.Precision.HIGHEST
    )
    own_grad = own_both[:chan_dev]
    own_dpos = own_both[chan_dev:]
    return (result, own_grad.astype(jnp.bfloat16), -own_dpos, grad_rad)


def solution(mesh):
    placed = (
        P(None, "space"),
        P("chan", "space"),
        P("space", None),
        P("space", None),
        P("space"),
        P("chan", None),
        P(),
        P("chan", None, "space"),
    )
    return jax.shard_map(
        body,
        mesh=mesh,
        in_specs=placed,
        out_specs=(P("chan", None, "space"), P("chan", "space"), P(None, "space"), P("chan", None)),
        check_vma=False,
    )
```

```python
import math

import jax
import jax.numpy as jnp
from jax import lax
from jax.sharding import PartitionSpec as P

SOFTENING = 0.25
CUTOFF = 2.5
CUTOFF_SQ = 6.25
SHARPNESS = 10.0
ROOT_THREE = math.sqrt(3.0)
ORDER_OF = (0, 1, 1, 1, 2, 2, 2, 2, 2)


def partner(value, axis, bit):
    mask = 2**bit
    pairs = [(source, source ^ mask) for source in range(lax.axis_size(axis))]
    return lax.ppermute(value, axis, pairs)


def halving_sum(value, axis):
    index = lax.axis_index(axis)
    for bit in reversed(range(lax.axis_size(axis).bit_length() - 1)):
        half = value.shape[0] // 2
        mine = (index >> bit) & 1
        keep = lax.dynamic_slice_in_dim(value, mine * half, half, 0)
        give = lax.dynamic_slice_in_dim(value, (1 - mine) * half, half, 0)
        value = keep + partner(give, axis, bit)
    return value


def as_rows(value, width):
    flat = value.reshape(-1)
    count = -(-flat.shape[0] // width)
    return jnp.pad(flat, (0, count * width - flat.shape[0])).reshape(count, width)


def halving_with(value, extras, axis):
    index = lax.axis_index(axis)
    width = value.shape[1]
    extra_rows = as_rows(jnp.concatenate([extra.reshape(-1) for extra in extras]), width)
    count = lax.axis_size(axis)
    chunk = value.shape[0] // count
    for bit in range(count.bit_length() - 1):
        groups = value.reshape(-1, 2, chunk, width)
        mine = (index >> bit) & 1
        keep = lax.dynamic_index_in_dim(groups, mine, 1, keepdims=False).reshape(-1, width)
        give = lax.dynamic_index_in_dim(groups, 1 - mine, 1, keepdims=False).reshape(-1, width)
        half = give.shape[0]
        got = partner(jnp.concatenate([give, extra_rows], axis=0), axis, bit)
        value = keep + got[:half]
        extra_rows = extra_rows + got[half:]
    flat = extra_rows.reshape(-1)
    sums = []
    start = 0
    for extra in extras:
        sums.append(flat[start : start + extra.size].reshape(extra.shape))
        start += extra.size
    return value, sums


def geometry(target_pos, source_pos, pair_keep, radial_count):
    offset = source_pos[:, :, None, :] - target_pos[:, :, :, None]
    dist_sq = jnp.sum(offset * offset, axis=1) + SOFTENING
    distance = jnp.sqrt(dist_sq)
    along_x = offset[:, 0] / distance
    along_y = offset[:, 1] / distance
    along_z = offset[:, 2] / distance
    harmonics = jnp.stack(
        [
            jnp.ones_like(along_x),
            along_x,
            along_y,
            along_z,
            ROOT_THREE * along_x * along_y,
            ROOT_THREE * along_y * along_z,
            ROOT_THREE * along_x * along_z,
            0.5 * (3.0 * along_z * along_z - 1.0),
            0.5 * ROOT_THREE * (along_x * along_x - along_y * along_y),
        ]
    )
    envelope = jnp.square(jnp.maximum(1.0 - dist_sq / CUTOFF_SQ, 0.0)) * pair_keep
    centers = (jnp.arange(radial_count, dtype=jnp.float32) + 0.5) * (CUTOFF / radial_count)
    radial = (
        jnp.exp(-SHARPNESS * jnp.square(distance[None] - centers[:, None, None, None]))
        * envelope[None]
    )
    return (harmonics, radial)


def take_block(array, blk_index, block_size):
    return lax.dynamic_slice_in_dim(array, blk_index * block_size, block_size, array.ndim - 1)


def add_block(array, blk_index, value, block_size):
    current = take_block(array, blk_index, block_size)
    return lax.dynamic_update_slice_in_dim(
        array, current + value, blk_index * block_size, array.ndim - 1
    )


def body(
    positions, features, send_rows, pair_tiles, tile_live, radial_weight, mix_weight, out_grad
):
    block_size = send_rows.shape[1]
    atoms_dev = positions.shape[1]
    chan_dev = features.shape[0]
    radial_count = radial_weight.shape[1]
    components = out_grad.shape[1]
    levels = lax.axis_size("space").bit_length() - 1
    chan_count = lax.axis_size("chan")
    chan_index = lax.axis_index("chan")
    pos_list = [positions]
    feat_list = [features]
    send_hot = (
        jnp.arange(atoms_dev, dtype=jnp.int32)[:, None] == send_rows[:levels].reshape(1, -1)
    ).astype(jnp.float32)
    both_rows = jnp.dot(
        jnp.concatenate([features.astype(jnp.float32), positions], axis=0),
        send_hot,
        precision=lax.Precision.HIGHEST,
    )
    for level_bit in range(levels):
        got_both = partner(
            both_rows[:, level_bit * block_size : (level_bit + 1) * block_size],
            "space",
            level_bit,
        )
        feat_list.append(got_both[:chan_dev].astype(jnp.bfloat16))
        pos_list.append(got_both[chan_dev:])
    src_pos = jnp.concatenate(pos_list, axis=1)
    src_feat = jnp.concatenate(feat_list, axis=1)
    src_atoms = src_pos.shape[1]
    weight_high = radial_weight.astype(jnp.bfloat16)
    weight_rest = radial_weight - weight_high.astype(jnp.float32)
    weight_mid = weight_rest.astype(jnp.bfloat16)
    weight_low = (weight_rest - weight_mid.astype(jnp.float32)).astype(jnp.bfloat16)
    full_both = lax.all_gather(
        jnp.concatenate([src_feat, weight_high, weight_mid, weight_low], axis=1),
        "chan",
        axis=0,
        tiled=True,
    )
    full_feat = full_both[:, :src_atoms]
    pieces = full_both[:, src_atoms:].astype(jnp.float32)
    full_weight = (
        pieces[:, :radial_count] + pieces[:, radial_count : 2 * radial_count]
    ) + pieces[:, 2 * radial_count :]
    all_chan = full_feat.shape[0]
    src_blocks = src_atoms // block_size
    own_blocks = atoms_dev // block_size
    rows = block_size // chan_count
    row_low = chan_index * rows
    target_idx = pair_tiles[:, 0]
    source_idx = pair_tiles[:, 1]
    live = tile_live.astype(jnp.float32)
    block_ids = jnp.arange(src_blocks, dtype=jnp.int32)
    target_hot = (target_idx[:, None] == block_ids[None]).astype(jnp.float32) * live[:, None]
    source_hot = (source_idx[:, None] == block_ids[None]).astype(jnp.float32) * live[:, None]
    same = (target_idx == source_idx).astype(jnp.float32)
    eye = (
        (row_low + jnp.arange(rows, dtype=jnp.int32))[:, None]
        == jnp.arange(block_size, dtype=jnp.int32)[None]
    ).astype(jnp.float32)
    pair_keep = live[:, None, None] * (1.0 - same[:, None, None] * eye[None])
    pos_blocks = jnp.moveaxis(src_pos.reshape(3, src_blocks, block_size), 1, 0)
    pos_rows = lax.dynamic_slice_in_dim(pos_blocks, row_low, rows, 2)
    feat_blocks = jnp.moveaxis(full_feat.reshape(all_chan, src_blocks, block_size), 1, 0)
    target_pos = jnp.take(pos_rows, target_idx, axis=0, mode="clip")
    source_pos = jnp.take(pos_blocks, source_idx, axis=0, mode="clip")
    source_feat = jnp.take(feat_blocks, source_idx, axis=0, mode="clip")

    def geo_fn(first_pos, second_pos):
        return geometry(first_pos, second_pos, pair_keep, radial_count)

    (harmonics, radial), pullback = jax.vjp(geo_fn, target_pos, source_pos)
    pair_values = (harmonics[:, None] * radial[None]).astype(jnp.bfloat16)
    routed_feat = (
        target_hot[:, :own_blocks, None, None] * source_feat[:, None].astype(jnp.float32)
    ).astype(jnp.bfloat16)
    msg_acc = jnp.einsum(
        "lktij,tbcj->bclki", pair_values, routed_feat, preferred_element_type=jnp.float32
    )
    moments = jnp.einsum("bclki,ck->clbi", msg_acc, full_weight)
    packed = moments.astype(jnp.bfloat16)
    mixing = jnp.take(mix_weight, jnp.array(ORDER_OF, dtype=jnp.int32), axis=0)
    offset = chan_index * chan_dev
    mixed_out = jnp.einsum(
        "lxc,clbi->xlbi", mixing, packed, preferred_element_type=jnp.float32
    )
    scalar_part = mixed_out[:, 0]
    gate_value = jax.nn.sigmoid(scalar_part)
    result_rows = jnp.concatenate(
        [(scalar_part * gate_value)[:, None], mixed_out[:, 1:] * gate_value[:, None]],
        axis=1,
    ).astype(jnp.bfloat16)
    result = lax.all_to_all(
        result_rows.reshape(all_chan, components, own_blocks, 1, rows),
        "chan",
        0,
        3,
        tiled=True,
    ).reshape(chan_dev, components, atoms_dev)
    grad_rows = lax.all_to_all(
        out_grad.reshape(chan_dev, components, own_blocks, chan_count, rows),
        "chan",
        3,
        0,
        tiled=True,
    ).reshape(all_chan, components, own_blocks, rows)
    upstream = grad_rows.astype(jnp.float32)
    scalar_grad = upstream[:, 0] * (
        gate_value * (1.0 + scalar_part * (1.0 - gate_value))
    ) + gate_value * (1.0 - gate_value) * jnp.sum(upstream[:, 1:] * mixed_out[:, 1:], axis=1)
    rest_grad = upstream[:, 1:] * gate_value[:, None]
    dz_packed = jnp.concatenate([scalar_grad[:, None], rest_grad], axis=1).astype(jnp.bfloat16)
    moment_grad_all = jnp.einsum(
        "lxc,xlbi->clbi", mixing, dz_packed, preferred_element_type=jnp.float32
    )
    result, moment_grad_all = lax.optimization_barrier((result, moment_grad_all))
    grad_rad = jnp.einsum("bclki,clbi->ck", msg_acc, moment_grad_all)
    grad_blocks = jnp.moveaxis(moment_grad_all, 2, 0)
    tile_grad = jnp.take(grad_blocks, target_idx, axis=0, mode="clip")
    weighted = (
        live[:, None, None, None, None]
        * full_weight[None, :, None, :, None]
        * tile_grad[:, :, :, None, :]
    ).astype(jnp.bfloat16)
    grad_source = jnp.einsum(
        "tclki,lktij->tcj", weighted, pair_values, preferred_element_type=jnp.float32
    )
    value_grad = jnp.einsum(
        "tclki,tcj->lktij", weighted, source_feat, preferred_element_type=jnp.float32
    )
    harm_grad = jnp.sum(value_grad * radial[None], axis=1)
    rad_grad = jnp.sum(value_grad * harmonics[:, None], axis=0)
    target_grad, source_grad_pos = pullback((harm_grad, rad_grad))
    grad_part = jnp.sum(
        source_hot[:, None, :, None] * grad_source[:, :, None, :], axis=0
    ).reshape(all_chan, src_atoms)
    row_hot = (jnp.arange(chan_count, dtype=jnp.int32) == chan_index).astype(jnp.float32)
    target_part = jnp.sum(target_hot[:, None, :, None] * target_grad[:, :, None, :], axis=0)
    dpos_src = (
        row_hot[None, None, :, None] * target_part[:, :, None, :]
        + jnp.sum(source_hot[:, None, :, None] * source_grad_pos[:, :, None, :], axis=0).reshape(
            3, src_blocks, chan_count, rows
        )
    ).reshape(3, src_atoms)
    grad_src, (dpos_src, grad_rad) = halving_with(grad_part, (dpos_src, grad_rad), "chan")
    grad_rad = lax.dynamic_slice_in_dim(grad_rad, offset, chan_dev, 0)
    own_both = jnp.concatenate([grad_src[:, :atoms_dev], dpos_src[:, :atoms_dev]], axis=0)
    ghost_rows = chan_dev + 3
    back_list = []
    for level_bit in range(levels):
        low = atoms_dev + level_bit * block_size
        ghost_both = jnp.concatenate(
            [
                grad_src[:, low : low + block_size],
                dpos_src[:, low : low + block_size],
                as_rows(grad_rad, block_size),
            ],
            axis=0,
        )
        back_both = partner(ghost_both, "space", level_bit)
        grad_rad = grad_rad + back_both[ghost_rows:].reshape(-1)[: grad_rad.size].reshape(
            grad_rad.shape
        )
        back_list.append(back_both[:ghost_rows])
    all_rows = send_rows[:levels].reshape(-1)
    ghost_hot = (all_rows[:, None] == jnp.arange(atoms_dev, dtype=jnp.int32)[None]).astype(
        jnp.float32
    )
    own_both = own_both + jnp.dot(
        jnp.concatenate(back_list, axis=1), ghost_hot, precision=lax.Precision.HIGHEST
    )
    own_grad = own_both[:chan_dev]
    own_dpos = own_both[chan_dev:]
    return (result, own_grad.astype(jnp.bfloat16), -own_dpos, grad_rad)


def solution(mesh):
    placed = (
        P(None, "space"),
        P("chan", "space"),
        P("space", None),
        P("space", None),
        P("space"),
        P("chan", None),
        P(),
        P("chan", None, "space"),
    )
    return jax.shard_map(
        body,
        mesh=mesh,
        in_specs=placed,
        out_specs=(P("chan", None, "space"), P("chan", "space"), P(None, "space"), P("chan", None)),
        check_vma=False,
    )
```

```python
import math

import jax
import jax.numpy as jnp
from jax import lax
from jax.sharding import PartitionSpec as P

SOFTENING = 0.25
CUTOFF = 2.5
CUTOFF_SQ = 6.25
SHARPNESS = 10.0
ROOT_THREE = math.sqrt(3.0)
ORDER_OF = (0, 1, 1, 1, 2, 2, 2, 2, 2)


def partner(value, axis, bit):
    mask = 2**bit
    pairs = [(source, source ^ mask) for source in range(lax.axis_size(axis))]
    return lax.ppermute(value, axis, pairs)


def halving_sum(value, axis):
    index = lax.axis_index(axis)
    for bit in reversed(range(lax.axis_size(axis).bit_length() - 1)):
        half = value.shape[0] // 2
        mine = (index >> bit) & 1
        keep = lax.dynamic_slice_in_dim(value, mine * half, half, 0)
        give = lax.dynamic_slice_in_dim(value, (1 - mine) * half, half, 0)
        value = keep + partner(give, axis, bit)
    return value


def as_rows(value, width):
    flat = value.reshape(-1)
    count = -(-flat.shape[0] // width)
    return jnp.pad(flat, (0, count * width - flat.shape[0])).reshape(count, width)


def order_groups(count):
    groups = []
    for component, order in enumerate(ORDER_OF[:count]):
        if groups and groups[-1][0] == order:
            groups[-1] = (order, groups[-1][1], component + 1)
        else:
            groups.append((order, component, component + 1))
    return groups


def mix_orders(weights, values, spec):
    return jnp.concatenate(
        [
            jnp.einsum(
                spec,
                weights[order],
                values[:, low:high],
                preferred_element_type=jnp.float32,
            )
            for order, low, high in order_groups(values.shape[1])
        ],
        axis=1,
    )


def halving_with(value, extras, axis):
    index = lax.axis_index(axis)
    width = value.shape[1]
    extra_rows = as_rows(jnp.concatenate([extra.reshape(-1) for extra in extras]), width)
    count = lax.axis_size(axis)
    chunk = value.shape[0] // count
    for bit in range(count.bit_length() - 1):
        groups = value.reshape(-1, 2, chunk, width)
        mine = (index >> bit) & 1
        keep = lax.dynamic_index_in_dim(groups, mine, 1, keepdims=False).reshape(-1, width)
        give = lax.dynamic_index_in_dim(groups, 1 - mine, 1, keepdims=False).reshape(-1, width)
        half = give.shape[0]
        got = partner(jnp.concatenate([give, extra_rows], axis=0), axis, bit)
        value = keep + got[:half]
        extra_rows = extra_rows + got[half:]
    flat = extra_rows.reshape(-1)
    sums = []
    start = 0
    for extra in extras:
        sums.append(flat[start : start + extra.size].reshape(extra.shape))
        start += extra.size
    return value, sums


def geometry(target_pos, source_pos, pair_keep, radial_count):
    offset = source_pos[:, :, None, :] - target_pos[:, :, :, None]
    dist_sq = jnp.sum(offset * offset, axis=1) + SOFTENING
    distance = jnp.sqrt(dist_sq)
    along_x = offset[:, 0] / distance
    along_y = offset[:, 1] / distance
    along_z = offset[:, 2] / distance
    harmonics = jnp.stack(
        [
            jnp.ones_like(along_x),
            along_x,
            along_y,
            along_z,
            ROOT_THREE * along_x * along_y,
            ROOT_THREE * along_y * along_z,
            ROOT_THREE * along_x * along_z,
            0.5 * (3.0 * along_z * along_z - 1.0),
            0.5 * ROOT_THREE * (along_x * along_x - along_y * along_y),
        ]
    )
    envelope = jnp.square(jnp.maximum(1.0 - dist_sq / CUTOFF_SQ, 0.0)) * pair_keep
    centers = (jnp.arange(radial_count, dtype=jnp.float32) + 0.5) * (CUTOFF / radial_count)
    radial = (
        jnp.exp(-SHARPNESS * jnp.square(distance[None] - centers[:, None, None, None]))
        * envelope[None]
    )
    return (harmonics, radial)


def take_block(array, blk_index, block_size):
    return lax.dynamic_slice_in_dim(array, blk_index * block_size, block_size, array.ndim - 1)


def add_block(array, blk_index, value, block_size):
    current = take_block(array, blk_index, block_size)
    return lax.dynamic_update_slice_in_dim(
        array, current + value, blk_index * block_size, array.ndim - 1
    )


def body(
    positions, features, send_rows, pair_tiles, tile_live, radial_weight, mix_weight, out_grad
):
    block_size = send_rows.shape[1]
    atoms_dev = positions.shape[1]
    chan_dev = features.shape[0]
    radial_count = radial_weight.shape[1]
    components = out_grad.shape[1]
    levels = lax.axis_size("space").bit_length() - 1
    chan_count = lax.axis_size("chan")
    chan_index = lax.axis_index("chan")
    pos_list = [positions]
    feat_list = [features]
    send_hot = (
        jnp.arange(atoms_dev, dtype=jnp.int32)[:, None] == send_rows[:levels].reshape(1, -1)
    ).astype(jnp.float32)
    both_rows = jnp.dot(
        jnp.concatenate([features.astype(jnp.float32), positions], axis=0),
        send_hot,
        precision=lax.Precision.HIGHEST,
    )
    for level_bit in range(levels):
        got_both = partner(
            both_rows[:, level_bit * block_size : (level_bit + 1) * block_size],
            "space",
            level_bit,
        )
        feat_list.append(got_both[:chan_dev].astype(jnp.bfloat16))
        pos_list.append(got_both[chan_dev:])
    src_pos = jnp.concatenate(pos_list, axis=1)
    src_feat = jnp.concatenate(feat_list, axis=1)
    src_atoms = src_pos.shape[1]
    weight_high = radial_weight.astype(jnp.bfloat16)
    weight_rest = radial_weight - weight_high.astype(jnp.float32)
    weight_mid = weight_rest.astype(jnp.bfloat16)
    weight_low = (weight_rest - weight_mid.astype(jnp.float32)).astype(jnp.bfloat16)
    full_both = lax.all_gather(
        jnp.concatenate([src_feat, weight_high, weight_mid, weight_low], axis=1),
        "chan",
        axis=0,
        tiled=True,
    )
    full_feat = full_both[:, :src_atoms]
    pieces = full_both[:, src_atoms:].astype(jnp.float32)
    full_weight = (
        pieces[:, :radial_count] + pieces[:, radial_count : 2 * radial_count]
    ) + pieces[:, 2 * radial_count :]
    all_chan = full_feat.shape[0]
    src_blocks = src_atoms // block_size
    own_blocks = atoms_dev // block_size
    rows = block_size // chan_count
    row_low = chan_index * rows
    target_idx = pair_tiles[:, 0]
    source_idx = pair_tiles[:, 1]
    live = tile_live.astype(jnp.float32)
    block_ids = jnp.arange(src_blocks, dtype=jnp.int32)
    target_hot = (target_idx[:, None] == block_ids[None]).astype(jnp.float32) * live[:, None]
    source_hot = (source_idx[:, None] == block_ids[None]).astype(jnp.float32) * live[:, None]
    same = (target_idx == source_idx).astype(jnp.float32)
    eye = (
        (row_low + jnp.arange(rows, dtype=jnp.int32))[:, None]
        == jnp.arange(block_size, dtype=jnp.int32)[None]
    ).astype(jnp.float32)
    pair_keep = live[:, None, None] * (1.0 - same[:, None, None] * eye[None])
    pos_blocks = jnp.moveaxis(src_pos.reshape(3, src_blocks, block_size), 1, 0)
    pos_rows = lax.dynamic_slice_in_dim(pos_blocks, row_low, rows, 2)
    feat_blocks = jnp.moveaxis(full_feat.reshape(all_chan, src_blocks, block_size), 1, 0)
    target_pos = jnp.take(pos_rows, target_idx, axis=0, mode="clip")
    source_pos = jnp.take(pos_blocks, source_idx, axis=0, mode="clip")
    source_feat = jnp.take(feat_blocks, source_idx, axis=0, mode="clip")

    def geo_fn(first_pos, second_pos):
        return geometry(first_pos, second_pos, pair_keep, radial_count)

    (harmonics, radial), pullback = jax.vjp(geo_fn, target_pos, source_pos)
    pair_values = (harmonics[:, None] * radial[None]).astype(jnp.bfloat16)
    routed_feat = (
        target_hot[:, :own_blocks, None, None] * source_feat[:, None].astype(jnp.float32)
    ).astype(jnp.bfloat16)
    msg_acc = jnp.einsum(
        "lktij,tbcj->bclki", pair_values, routed_feat, preferred_element_type=jnp.float32
    )
    moments = jnp.einsum("bclki,ck->clbi", msg_acc, full_weight)
    packed = moments.astype(jnp.bfloat16)
    offset = chan_index * chan_dev
    mixed_out = mix_orders(mix_weight, packed, "xc,clbi->xlbi")
    scalar_part = mixed_out[:, 0]
    gate_value = jax.nn.sigmoid(scalar_part)
    result_rows = jnp.concatenate(
        [(scalar_part * gate_value)[:, None], mixed_out[:, 1:] * gate_value[:, None]],
        axis=1,
    ).astype(jnp.bfloat16)
    result = lax.all_to_all(
        result_rows.reshape(all_chan, components, own_blocks, 1, rows),
        "chan",
        0,
        3,
        tiled=True,
    ).reshape(chan_dev, components, atoms_dev)
    grad_rows = lax.all_to_all(
        out_grad.reshape(chan_dev, components, own_blocks, chan_count, rows),
        "chan",
        3,
        0,
        tiled=True,
    ).reshape(all_chan, components, own_blocks, rows)
    upstream = grad_rows.astype(jnp.float32)
    scalar_grad = upstream[:, 0] * (
        gate_value * (1.0 + scalar_part * (1.0 - gate_value))
    ) + gate_value * (1.0 - gate_value) * jnp.sum(upstream[:, 1:] * mixed_out[:, 1:], axis=1)
    rest_grad = upstream[:, 1:] * gate_value[:, None]
    dz_packed = jnp.concatenate([scalar_grad[:, None], rest_grad], axis=1).astype(jnp.bfloat16)
    moment_grad_all = mix_orders(mix_weight, dz_packed, "xc,xlbi->clbi")
    grad_rad = jnp.einsum("bclki,clbi->ck", msg_acc, moment_grad_all)
    grad_blocks = jnp.moveaxis(moment_grad_all, 2, 0)
    tile_grad = jnp.take(grad_blocks, target_idx, axis=0, mode="clip")
    weighted = (
        live[:, None, None, None, None]
        * full_weight[None, :, None, :, None]
        * tile_grad[:, :, :, None, :]
    ).astype(jnp.bfloat16)
    grad_source = jnp.einsum(
        "tclki,lktij->tcj", weighted, pair_values, preferred_element_type=jnp.float32
    )
    value_grad = jnp.einsum(
        "tclki,tcj->lktij", weighted, source_feat, preferred_element_type=jnp.float32
    )
    harm_grad = jnp.sum(value_grad * radial[None], axis=1)
    rad_grad = jnp.sum(value_grad * harmonics[:, None], axis=0)
    target_grad, source_grad_pos = pullback((harm_grad, rad_grad))
    grad_part = jnp.sum(
        source_hot[:, None, :, None] * grad_source[:, :, None, :], axis=0
    ).reshape(all_chan, src_atoms)
    row_hot = (jnp.arange(chan_count, dtype=jnp.int32) == chan_index).astype(jnp.float32)
    target_part = jnp.sum(target_hot[:, None, :, None] * target_grad[:, :, None, :], axis=0)
    dpos_src = (
        row_hot[None, None, :, None] * target_part[:, :, None, :]
        + jnp.sum(source_hot[:, None, :, None] * source_grad_pos[:, :, None, :], axis=0).reshape(
            3, src_blocks, chan_count, rows
        )
    ).reshape(3, src_atoms)
    grad_src, (dpos_src, grad_rad) = halving_with(grad_part, (dpos_src, grad_rad), "chan")
    grad_rad = lax.dynamic_slice_in_dim(grad_rad, offset, chan_dev, 0)
    own_both = jnp.concatenate([grad_src[:, :atoms_dev], dpos_src[:, :atoms_dev]], axis=0)
    ghost_rows = chan_dev + 3
    back_list = []
    for level_bit in range(levels):
        low = atoms_dev + level_bit * block_size
        ghost_both = jnp.concatenate(
            [
                grad_src[:, low : low + block_size],
                dpos_src[:, low : low + block_size],
                as_rows(grad_rad, block_size),
            ],
            axis=0,
        )
        back_both = partner(ghost_both, "space", level_bit)
        grad_rad = grad_rad + back_both[ghost_rows:].reshape(-1)[: grad_rad.size].reshape(
            grad_rad.shape
        )
        back_list.append(back_both[:ghost_rows])
    all_rows = send_rows[:levels].reshape(-1)
    ghost_hot = (all_rows[:, None] == jnp.arange(atoms_dev, dtype=jnp.int32)[None]).astype(
        jnp.float32
    )
    own_both = own_both + jnp.dot(
        jnp.concatenate(back_list, axis=1), ghost_hot, precision=lax.Precision.HIGHEST
    )
    own_grad = own_both[:chan_dev]
    own_dpos = own_both[chan_dev:]
    return (result, own_grad.astype(jnp.bfloat16), -own_dpos, grad_rad)


def solution(mesh):
    placed = (
        P(None, "space"),
        P("chan", "space"),
        P("space", None),
        P("space", None),
        P("space"),
        P("chan", None),
        P(),
        P("chan", None, "space"),
    )
    return jax.shard_map(
        body,
        mesh=mesh,
        in_specs=placed,
        out_specs=(P("chan", None, "space"), P("chan", "space"), P(None, "space"), P("chan", None)),
        check_vma=False,
    )
```

```python
import math

import jax
import jax.numpy as jnp
from jax import lax
from jax.sharding import PartitionSpec as P

SOFTENING = 0.25
CUTOFF = 2.5
CUTOFF_SQ = 6.25
SHARPNESS = 10.0
ROOT_THREE = math.sqrt(3.0)
ORDER_OF = (0, 1, 1, 1, 2, 2, 2, 2, 2)


def partner(value, axis, bit):
    mask = 2**bit
    pairs = [(source, source ^ mask) for source in range(lax.axis_size(axis))]
    return lax.ppermute(value, axis, pairs)


def halving_sum(value, axis):
    index = lax.axis_index(axis)
    for bit in reversed(range(lax.axis_size(axis).bit_length() - 1)):
        half = value.shape[0] // 2
        mine = (index >> bit) & 1
        keep = lax.dynamic_slice_in_dim(value, mine * half, half, 0)
        give = lax.dynamic_slice_in_dim(value, (1 - mine) * half, half, 0)
        value = keep + partner(give, axis, bit)
    return value


def as_rows(value, width):
    flat = value.reshape(-1)
    count = -(-flat.shape[0] // width)
    return jnp.pad(flat, (0, count * width - flat.shape[0])).reshape(count, width)


def order_groups(count):
    groups = []
    for component, order in enumerate(ORDER_OF[:count]):
        if groups and groups[-1][0] == order:
            groups[-1] = (order, groups[-1][1], component + 1)
        else:
            groups.append((order, component, component + 1))
    return groups


def mix_orders(weights, values, spec):
    return jnp.concatenate(
        [
            jnp.einsum(
                spec,
                weights[order],
                values[:, low:high],
                preferred_element_type=jnp.float32,
            )
            for order, low, high in order_groups(values.shape[1])
        ],
        axis=1,
    )


def halving_with(value, extras, axis):
    index = lax.axis_index(axis)
    width = value.shape[1]
    extra_rows = as_rows(jnp.concatenate([extra.reshape(-1) for extra in extras]), width)
    count = lax.axis_size(axis)
    chunk = value.shape[0] // count
    for bit in range(count.bit_length() - 1):
        groups = value.reshape(-1, 2, chunk, width)
        mine = (index >> bit) & 1
        keep = lax.dynamic_index_in_dim(groups, mine, 1, keepdims=False).reshape(-1, width)
        give = lax.dynamic_index_in_dim(groups, 1 - mine, 1, keepdims=False).reshape(-1, width)
        half = give.shape[0]
        got = partner(jnp.concatenate([give, extra_rows], axis=0), axis, bit)
        value = keep + got[:half]
        extra_rows = extra_rows + got[half:]
    flat = extra_rows.reshape(-1)
    sums = []
    start = 0
    for extra in extras:
        sums.append(flat[start : start + extra.size].reshape(extra.shape))
        start += extra.size
    return value, sums


def geometry(target_pos, source_pos, pair_keep, radial_count):
    offset = source_pos[:, :, None, :] - target_pos[:, :, :, None]
    dist_sq = jnp.sum(offset * offset, axis=1) + SOFTENING
    distance = jnp.sqrt(dist_sq)
    along_x = offset[:, 0] / distance
    along_y = offset[:, 1] / distance
    along_z = offset[:, 2] / distance
    harmonics = jnp.stack(
        [
            jnp.ones_like(along_x),
            along_x,
            along_y,
            along_z,
            ROOT_THREE * along_x * along_y,
            ROOT_THREE * along_y * along_z,
            ROOT_THREE * along_x * along_z,
            0.5 * (3.0 * along_z * along_z - 1.0),
            0.5 * ROOT_THREE * (along_x * along_x - along_y * along_y),
        ]
    )
    envelope = jnp.square(jnp.maximum(1.0 - dist_sq / CUTOFF_SQ, 0.0)) * pair_keep
    centers = (jnp.arange(radial_count, dtype=jnp.float32) + 0.5) * (CUTOFF / radial_count)
    radial = (
        jnp.exp(-SHARPNESS * jnp.square(distance[None] - centers[:, None, None, None]))
        * envelope[None]
    )
    return (harmonics, radial)


def take_block(array, blk_index, block_size):
    return lax.dynamic_slice_in_dim(array, blk_index * block_size, block_size, array.ndim - 1)


def add_block(array, blk_index, value, block_size):
    current = take_block(array, blk_index, block_size)
    return lax.dynamic_update_slice_in_dim(
        array, current + value, blk_index * block_size, array.ndim - 1
    )


def body(
    positions, features, send_rows, pair_tiles, tile_live, radial_weight, mix_weight, out_grad
):
    block_size = send_rows.shape[1]
    atoms_dev = positions.shape[1]
    chan_dev = features.shape[0]
    radial_count = radial_weight.shape[1]
    components = out_grad.shape[1]
    levels = lax.axis_size("space").bit_length() - 1
    chan_count = lax.axis_size("chan")
    chan_index = lax.axis_index("chan")
    pos_list = [positions]
    feat_list = [features]
    send_hot = (
        jnp.arange(atoms_dev, dtype=jnp.int32)[:, None] == send_rows[:levels].reshape(1, -1)
    ).astype(jnp.float32)
    both_rows = jnp.dot(
        jnp.concatenate([features.astype(jnp.float32), positions], axis=0),
        send_hot,
        precision=lax.Precision.HIGHEST,
    )
    for level_bit in range(levels):
        got_both = partner(
            both_rows[:, level_bit * block_size : (level_bit + 1) * block_size],
            "space",
            level_bit,
        )
        feat_list.append(got_both[:chan_dev].astype(jnp.bfloat16))
        pos_list.append(got_both[chan_dev:])
    src_pos = jnp.concatenate(pos_list, axis=1)
    src_feat = jnp.concatenate(feat_list, axis=1)
    src_atoms = src_pos.shape[1]
    weight_high = radial_weight.astype(jnp.bfloat16)
    weight_rest = radial_weight - weight_high.astype(jnp.float32)
    weight_mid = weight_rest.astype(jnp.bfloat16)
    weight_low = (weight_rest - weight_mid.astype(jnp.float32)).astype(jnp.bfloat16)
    full_both = lax.all_gather(
        jnp.concatenate([src_feat, weight_high, weight_mid, weight_low], axis=1),
        "chan",
        axis=0,
        tiled=True,
    )
    full_feat = full_both[:, :src_atoms]
    pieces = full_both[:, src_atoms:].astype(jnp.float32)
    full_weight = (
        pieces[:, :radial_count] + pieces[:, radial_count : 2 * radial_count]
    ) + pieces[:, 2 * radial_count :]
    all_chan = full_feat.shape[0]
    src_blocks = src_atoms // block_size
    own_blocks = atoms_dev // block_size
    rows = block_size // chan_count
    row_low = chan_index * rows
    target_idx = pair_tiles[:, 0]
    source_idx = pair_tiles[:, 1]
    live = tile_live.astype(jnp.float32)
    block_ids = jnp.arange(src_blocks, dtype=jnp.int32)
    target_hot = (target_idx[:, None] == block_ids[None]).astype(jnp.float32) * live[:, None]
    source_hot = (source_idx[:, None] == block_ids[None]).astype(jnp.float32) * live[:, None]
    same = (target_idx == source_idx).astype(jnp.float32)
    eye = (
        (row_low + jnp.arange(rows, dtype=jnp.int32))[:, None]
        == jnp.arange(block_size, dtype=jnp.int32)[None]
    ).astype(jnp.float32)
    pair_keep = live[:, None, None] * (1.0 - same[:, None, None] * eye[None])
    pos_blocks = jnp.moveaxis(src_pos.reshape(3, src_blocks, block_size), 1, 0)
    pos_rows = lax.dynamic_slice_in_dim(pos_blocks, row_low, rows, 2)
    feat_blocks = jnp.moveaxis(full_feat.reshape(all_chan, src_blocks, block_size), 1, 0)
    target_pos = jnp.take(pos_rows, target_idx, axis=0, mode="clip")
    source_pos = jnp.take(pos_blocks, source_idx, axis=0, mode="clip")
    source_feat = jnp.take(feat_blocks, source_idx, axis=0, mode="clip")

    def geo_fn(first_pos, second_pos):
        return geometry(first_pos, second_pos, pair_keep, radial_count)

    (harmonics, radial), pullback = jax.vjp(geo_fn, target_pos, source_pos)
    pair_values = (harmonics[:, None] * radial[None]).astype(jnp.bfloat16)
    routed_feat = (
        target_hot[:, :own_blocks, None, None] * source_feat[:, None].astype(jnp.float32)
    ).astype(jnp.bfloat16)
    msg_acc = jnp.einsum(
        "lktij,tbcj->bclki", pair_values, routed_feat, preferred_element_type=jnp.float32
    )
    moments = jnp.einsum("bclki,ck->clbi", msg_acc, full_weight)
    packed = moments.astype(jnp.bfloat16)
    offset = chan_index * chan_dev
    mixed_out = mix_orders(mix_weight, packed, "xc,clbi->xlbi")
    scalar_part = mixed_out[:, 0]
    gate_value = jax.nn.sigmoid(scalar_part)
    result_rows = jnp.concatenate(
        [(scalar_part * gate_value)[:, None], mixed_out[:, 1:] * gate_value[:, None]],
        axis=1,
    ).astype(jnp.bfloat16)
    result = lax.all_to_all(
        result_rows.reshape(all_chan, components, own_blocks, 1, rows),
        "chan",
        0,
        3,
        tiled=True,
    ).reshape(chan_dev, components, atoms_dev)
    grad_rows = lax.all_to_all(
        out_grad.reshape(chan_dev, components, own_blocks, chan_count, rows),
        "chan",
        3,
        0,
        tiled=True,
    ).reshape(all_chan, components, own_blocks, rows)
    upstream = grad_rows.astype(jnp.float32)
    scalar_grad = upstream[:, 0] * (
        gate_value * (1.0 + scalar_part * (1.0 - gate_value))
    ) + gate_value * (1.0 - gate_value) * jnp.sum(upstream[:, 1:] * mixed_out[:, 1:], axis=1)
    rest_grad = upstream[:, 1:] * gate_value[:, None]
    dz_packed = jnp.concatenate([scalar_grad[:, None], rest_grad], axis=1).astype(jnp.bfloat16)
    moment_grad_all = mix_orders(mix_weight, dz_packed, "xc,xlbi->clbi")
    grad_rad = jnp.einsum("bclki,clbi->ck", msg_acc, moment_grad_all)
    grad_blocks = jnp.moveaxis(moment_grad_all, 2, 0)
    tile_grad = jnp.take(grad_blocks, target_idx, axis=0, mode="clip")
    weighted = (
        live[:, None, None, None, None]
        * full_weight[None, :, None, :, None]
        * tile_grad[:, :, :, None, :]
    ).astype(jnp.bfloat16)
    grad_source = jnp.einsum(
        "tclki,lktij->tcj", weighted, pair_values, preferred_element_type=jnp.float32
    )
    value_grad = jnp.einsum(
        "tclki,tcj->lktij", weighted, source_feat, preferred_element_type=jnp.float32
    )
    harm_grad = jnp.sum(value_grad * radial[None], axis=1)
    rad_grad = jnp.sum(value_grad * harmonics[:, None], axis=0)
    target_grad, source_grad_pos = pullback((harm_grad, rad_grad))
    grad_part = jnp.sum(
        source_hot[:, None, :, None] * grad_source[:, :, None, :], axis=0
    ).reshape(all_chan, src_atoms)
    target_part = jnp.sum(target_hot[:, None, :, None] * target_grad[:, :, None, :], axis=0)
    source_part = jnp.sum(
        source_hot[:, None, :, None] * source_grad_pos[:, :, None, :], axis=0
    ).reshape(3, src_blocks, chan_count, rows)
    own_rows = lax.dynamic_index_in_dim(source_part, chan_index, 2, keepdims=False)
    dpos_src = lax.dynamic_update_index_in_dim(
        source_part, own_rows + target_part, chan_index, 2
    ).reshape(3, src_atoms)
    grad_src, (dpos_src, grad_rad) = halving_with(grad_part, (dpos_src, grad_rad), "chan")
    grad_rad = lax.dynamic_slice_in_dim(grad_rad, offset, chan_dev, 0)
    own_both = jnp.concatenate([grad_src[:, :atoms_dev], dpos_src[:, :atoms_dev]], axis=0)
    ghost_rows = chan_dev + 3
    back_list = []
    for level_bit in range(levels):
        low = atoms_dev + level_bit * block_size
        ghost_both = jnp.concatenate(
            [
                grad_src[:, low : low + block_size],
                dpos_src[:, low : low + block_size],
                as_rows(grad_rad, block_size),
            ],
            axis=0,
        )
        back_both = partner(ghost_both, "space", level_bit)
        grad_rad = grad_rad + back_both[ghost_rows:].reshape(-1)[: grad_rad.size].reshape(
            grad_rad.shape
        )
        back_list.append(back_both[:ghost_rows])
    all_rows = send_rows[:levels].reshape(-1)
    ghost_hot = (all_rows[:, None] == jnp.arange(atoms_dev, dtype=jnp.int32)[None]).astype(
        jnp.float32
    )
    own_both = own_both + jnp.dot(
        jnp.concatenate(back_list, axis=1), ghost_hot, precision=lax.Precision.HIGHEST
    )
    own_grad = own_both[:chan_dev]
    own_dpos = own_both[chan_dev:]
    return (result, own_grad.astype(jnp.bfloat16), -own_dpos, grad_rad)


def solution(mesh):
    placed = (
        P(None, "space"),
        P("chan", "space"),
        P("space", None),
        P("space", None),
        P("space"),
        P("chan", None),
        P(),
        P("chan", None, "space"),
    )
    return jax.shard_map(
        body,
        mesh=mesh,
        in_specs=placed,
        out_specs=(P("chan", None, "space"), P("chan", "space"), P(None, "space"), P("chan", None)),
        check_vma=False,
    )
```

```python
import math

import jax
import jax.numpy as jnp
from jax import lax
from jax.sharding import PartitionSpec as P

SOFTENING = 0.25
CUTOFF = 2.5
CUTOFF_SQ = 6.25
SHARPNESS = 10.0
ROOT_THREE = math.sqrt(3.0)
ORDER_OF = (0, 1, 1, 1, 2, 2, 2, 2, 2)


def partner(value, axis, bit):
    mask = 2**bit
    pairs = [(source, source ^ mask) for source in range(lax.axis_size(axis))]
    return lax.ppermute(value, axis, pairs)


def halving_sum(value, axis):
    index = lax.axis_index(axis)
    for bit in reversed(range(lax.axis_size(axis).bit_length() - 1)):
        half = value.shape[0] // 2
        mine = (index >> bit) & 1
        keep = lax.dynamic_slice_in_dim(value, mine * half, half, 0)
        give = lax.dynamic_slice_in_dim(value, (1 - mine) * half, half, 0)
        value = keep + partner(give, axis, bit)
    return value


def as_rows(value, width):
    flat = value.reshape(-1)
    count = -(-flat.shape[0] // width)
    return jnp.pad(flat, (0, count * width - flat.shape[0])).reshape(count, width)


def order_groups(count):
    groups = []
    for component, order in enumerate(ORDER_OF[:count]):
        if groups and groups[-1][0] == order:
            groups[-1] = (order, groups[-1][1], component + 1)
        else:
            groups.append((order, component, component + 1))
    return groups


def mix_orders(weights, values, spec):
    return jnp.concatenate(
        [
            jnp.einsum(
                spec,
                weights[order],
                values[:, low:high],
                preferred_element_type=jnp.float32,
            )
            for order, low, high in order_groups(values.shape[1])
        ],
        axis=1,
    )


def halving_with(value, extras, axis):
    index = lax.axis_index(axis)
    width = value.shape[1]
    pieces = [
        extra if extra.ndim == 2 and extra.shape[1] == width else as_rows(extra, width)
        for extra in extras
    ]
    extra_rows = jnp.concatenate(pieces, axis=0)
    count = lax.axis_size(axis)
    chunk = value.shape[0] // count
    for bit in range(count.bit_length() - 1):
        groups = value.reshape(-1, 2, chunk, width)
        mine = (index >> bit) & 1
        keep = lax.dynamic_index_in_dim(groups, mine, 1, keepdims=False).reshape(-1, width)
        give = lax.dynamic_index_in_dim(groups, 1 - mine, 1, keepdims=False).reshape(-1, width)
        half = give.shape[0]
        got = partner(jnp.concatenate([give, extra_rows], axis=0), axis, bit)
        value = keep + got[:half]
        extra_rows = extra_rows + got[half:]
    sums = []
    start = 0
    for extra, piece in zip(extras, pieces):
        rows = extra_rows[start : start + piece.shape[0]]
        sums.append(rows.reshape(-1)[: extra.size].reshape(extra.shape))
        start += piece.shape[0]
    return value, sums


def geometry(target_pos, source_pos, pair_keep, radial_count):
    offset = source_pos[:, :, None, :] - target_pos[:, :, :, None]
    dist_sq = jnp.sum(offset * offset, axis=1) + SOFTENING
    distance = jnp.sqrt(dist_sq)
    along_x = offset[:, 0] / distance
    along_y = offset[:, 1] / distance
    along_z = offset[:, 2] / distance
    harmonics = jnp.stack(
        [
            jnp.ones_like(along_x),
            along_x,
            along_y,
            along_z,
            ROOT_THREE * along_x * along_y,
            ROOT_THREE * along_y * along_z,
            ROOT_THREE * along_x * along_z,
            0.5 * (3.0 * along_z * along_z - 1.0),
            0.5 * ROOT_THREE * (along_x * along_x - along_y * along_y),
        ]
    )
    envelope = jnp.square(jnp.maximum(1.0 - dist_sq / CUTOFF_SQ, 0.0)) * pair_keep
    centers = (jnp.arange(radial_count, dtype=jnp.float32) + 0.5) * (CUTOFF / radial_count)
    radial = (
        jnp.exp(-SHARPNESS * jnp.square(distance[None] - centers[:, None, None, None]))
        * envelope[None]
    )
    return (harmonics, radial)


def take_block(array, blk_index, block_size):
    return lax.dynamic_slice_in_dim(array, blk_index * block_size, block_size, array.ndim - 1)


def add_block(array, blk_index, value, block_size):
    current = take_block(array, blk_index, block_size)
    return lax.dynamic_update_slice_in_dim(
        array, current + value, blk_index * block_size, array.ndim - 1
    )


def body(
    positions, features, send_rows, pair_tiles, tile_live, radial_weight, mix_weight, out_grad
):
    block_size = send_rows.shape[1]
    atoms_dev = positions.shape[1]
    chan_dev = features.shape[0]
    radial_count = radial_weight.shape[1]
    components = out_grad.shape[1]
    levels = lax.axis_size("space").bit_length() - 1
    chan_count = lax.axis_size("chan")
    chan_index = lax.axis_index("chan")
    pos_list = [positions]
    feat_list = [features]
    send_hot = (
        jnp.arange(atoms_dev, dtype=jnp.int32)[:, None] == send_rows[:levels].reshape(1, -1)
    ).astype(jnp.float32)
    both_rows = jnp.dot(
        jnp.concatenate([features.astype(jnp.float32), positions], axis=0),
        send_hot,
        precision=lax.Precision.HIGHEST,
    )
    for level_bit in range(levels):
        got_both = partner(
            both_rows[:, level_bit * block_size : (level_bit + 1) * block_size],
            "space",
            level_bit,
        )
        feat_list.append(got_both[:chan_dev].astype(jnp.bfloat16))
        pos_list.append(got_both[chan_dev:])
    src_pos = jnp.concatenate(pos_list, axis=1)
    src_feat = jnp.concatenate(feat_list, axis=1)
    src_atoms = src_pos.shape[1]
    weight_high = radial_weight.astype(jnp.bfloat16)
    weight_rest = radial_weight - weight_high.astype(jnp.float32)
    weight_mid = weight_rest.astype(jnp.bfloat16)
    weight_low = (weight_rest - weight_mid.astype(jnp.float32)).astype(jnp.bfloat16)
    full_both = lax.all_gather(
        jnp.concatenate([src_feat, weight_high, weight_mid, weight_low], axis=1),
        "chan",
        axis=0,
        tiled=True,
    )
    full_feat = full_both[:, :src_atoms]
    pieces = full_both[:, src_atoms:].astype(jnp.float32)
    full_weight = (
        pieces[:, :radial_count] + pieces[:, radial_count : 2 * radial_count]
    ) + pieces[:, 2 * radial_count :]
    all_chan = full_feat.shape[0]
    src_blocks = src_atoms // block_size
    own_blocks = atoms_dev // block_size
    rows = block_size // chan_count
    row_low = chan_index * rows
    target_idx = pair_tiles[:, 0]
    source_idx = pair_tiles[:, 1]
    live = tile_live.astype(jnp.float32)
    block_ids = jnp.arange(src_blocks, dtype=jnp.int32)
    target_hot = (target_idx[:, None] == block_ids[None]).astype(jnp.float32) * live[:, None]
    source_hot = (source_idx[:, None] == block_ids[None]).astype(jnp.float32) * live[:, None]
    same = (target_idx == source_idx).astype(jnp.float32)
    eye = (
        (row_low + jnp.arange(rows, dtype=jnp.int32))[:, None]
        == jnp.arange(block_size, dtype=jnp.int32)[None]
    ).astype(jnp.float32)
    pair_keep = live[:, None, None] * (1.0 - same[:, None, None] * eye[None])
    pos_blocks = jnp.moveaxis(src_pos.reshape(3, src_blocks, block_size), 1, 0)
    pos_rows = lax.dynamic_slice_in_dim(pos_blocks, row_low, rows, 2)
    feat_blocks = jnp.moveaxis(full_feat.reshape(all_chan, src_blocks, block_size), 1, 0)
    target_pos = jnp.take(pos_rows, target_idx, axis=0, mode="clip")
    source_pos = jnp.take(pos_blocks, source_idx, axis=0, mode="clip")
    source_feat = jnp.take(feat_blocks, source_idx, axis=0, mode="clip")

    def geo_fn(first_pos, second_pos):
        return geometry(first_pos, second_pos, pair_keep, radial_count)

    (harmonics, radial), pullback = jax.vjp(geo_fn, target_pos, source_pos)
    pair_values = (harmonics[:, None] * radial[None]).astype(jnp.bfloat16)
    routed_feat = (
        target_hot[:, :own_blocks, None, None] * source_feat[:, None].astype(jnp.float32)
    ).astype(jnp.bfloat16)
    msg_acc = jnp.einsum(
        "lktij,tbcj->bclki", pair_values, routed_feat, preferred_element_type=jnp.float32
    )
    moments = jnp.einsum("bclki,ck->clbi", msg_acc, full_weight)
    packed = moments.astype(jnp.bfloat16)
    offset = chan_index * chan_dev
    mixed_out = mix_orders(mix_weight, packed, "xc,clbi->xlbi")
    scalar_part = mixed_out[:, 0]
    gate_value = jax.nn.sigmoid(scalar_part)
    result_rows = jnp.concatenate(
        [(scalar_part * gate_value)[:, None], mixed_out[:, 1:] * gate_value[:, None]],
        axis=1,
    ).astype(jnp.bfloat16)
    result = lax.all_to_all(
        result_rows.reshape(all_chan, components, own_blocks, 1, rows),
        "chan",
        0,
        3,
        tiled=True,
    ).reshape(chan_dev, components, atoms_dev)
    grad_rows = lax.all_to_all(
        out_grad.reshape(chan_dev, components, own_blocks, chan_count, rows),
        "chan",
        3,
        0,
        tiled=True,
    ).reshape(all_chan, components, own_blocks, rows)
    upstream = grad_rows.astype(jnp.float32)
    scalar_grad = upstream[:, 0] * (
        gate_value * (1.0 + scalar_part * (1.0 - gate_value))
    ) + gate_value * (1.0 - gate_value) * jnp.sum(upstream[:, 1:] * mixed_out[:, 1:], axis=1)
    rest_grad = upstream[:, 1:] * gate_value[:, None]
    dz_packed = jnp.concatenate([scalar_grad[:, None], rest_grad], axis=1).astype(jnp.bfloat16)
    moment_grad_all = mix_orders(mix_weight, dz_packed, "xc,xlbi->clbi")
    grad_rad = jnp.einsum("bclki,clbi->ck", msg_acc, moment_grad_all)
    grad_blocks = jnp.moveaxis(moment_grad_all, 2, 0)
    tile_grad = jnp.take(grad_blocks, target_idx, axis=0, mode="clip")
    weighted = (
        live[:, None, None, None, None]
        * full_weight[None, :, None, :, None]
        * tile_grad[:, :, :, None, :]
    ).astype(jnp.bfloat16)
    grad_source = jnp.einsum(
        "tclki,lktij->tcj", weighted, pair_values, preferred_element_type=jnp.float32
    )
    value_grad = jnp.einsum(
        "tclki,tcj->lktij", weighted, source_feat, preferred_element_type=jnp.float32
    )
    harm_grad = jnp.sum(value_grad * radial[None], axis=1)
    rad_grad = jnp.sum(value_grad * harmonics[:, None], axis=0)
    target_grad, source_grad_pos = pullback((harm_grad, rad_grad))
    grad_part = jnp.sum(
        source_hot[:, None, :, None] * grad_source[:, :, None, :], axis=0
    ).reshape(all_chan, src_atoms)
    target_part = jnp.sum(target_hot[:, None, :, None] * target_grad[:, :, None, :], axis=0)
    source_part = jnp.sum(
        source_hot[:, None, :, None] * source_grad_pos[:, :, None, :], axis=0
    ).reshape(3, src_blocks, chan_count, rows)
    own_rows = lax.dynamic_index_in_dim(source_part, chan_index, 2, keepdims=False)
    dpos_src = lax.dynamic_update_index_in_dim(
        source_part, own_rows + target_part, chan_index, 2
    ).reshape(3, src_atoms)
    grad_src, (dpos_src, grad_rad) = halving_with(grad_part, (dpos_src, grad_rad), "chan")
    grad_rad = lax.dynamic_slice_in_dim(grad_rad, offset, chan_dev, 0)
    own_both = jnp.concatenate([grad_src[:, :atoms_dev], dpos_src[:, :atoms_dev]], axis=0)
    ghost_rows = chan_dev + 3
    back_list = []
    for level_bit in range(levels):
        low = atoms_dev + level_bit * block_size
        ghost_both = jnp.concatenate(
            [
                grad_src[:, low : low + block_size],
                dpos_src[:, low : low + block_size],
                as_rows(grad_rad, block_size),
            ],
            axis=0,
        )
        back_both = partner(ghost_both, "space", level_bit)
        grad_rad = grad_rad + back_both[ghost_rows:].reshape(-1)[: grad_rad.size].reshape(
            grad_rad.shape
        )
        back_list.append(back_both[:ghost_rows])
    all_rows = send_rows[:levels].reshape(-1)
    ghost_hot = (all_rows[:, None] == jnp.arange(atoms_dev, dtype=jnp.int32)[None]).astype(
        jnp.float32
    )
    own_both = own_both + jnp.dot(
        jnp.concatenate(back_list, axis=1), ghost_hot, precision=lax.Precision.HIGHEST
    )
    own_grad = own_both[:chan_dev]
    own_dpos = own_both[chan_dev:]
    return (result, own_grad.astype(jnp.bfloat16), -own_dpos, grad_rad)


def solution(mesh):
    placed = (
        P(None, "space"),
        P("chan", "space"),
        P("space", None),
        P("space", None),
        P("space"),
        P("chan", None),
        P(),
        P("chan", None, "space"),
    )
    return jax.shard_map(
        body,
        mesh=mesh,
        in_specs=placed,
        out_specs=(P("chan", None, "space"), P("chan", "space"), P(None, "space"), P("chan", None)),
        check_vma=False,
    )
```
